32 devices in a mesh: runs: 2 (over x), depth: 8 (over z, y), screen: 2 (over core).
Axes of the slice: x: 2, y: 2, z: 4, core: 2. Of those that a mesh axis runs over, the one named last changes fastest.
Arguments:
- density: float32 [16, 2, 128, 128, 128], P(('runs', 'depth'), 'screen'), parts along dimension 0, may hold values from -6 to 6
- foot_start: int32 [16, 2], P(('runs', 'depth'), 'screen'), parts along dimension 0, may hold values from 0 to 1920, as said below
- foot_rows: int32 [16, 2], P(('runs', 'depth'), 'screen'), parts along dimension 0, may hold values from 32 to 128, as said below
- extinction: float32 [2], P('runs'), parts along dimension 0, may hold values from 0.4 to 1.6
- colour_slope: float32 [3], replicated, may hold values from 0.5 to 2.5
- colour_offset: float32 [3], replicated, may hold values from -1 to 1
- tile_source: int32 [8192], P('runs'), parts along dimension 0, may hold values from 0 to 4095, as said below
Outputs:
- frame: float32 [8192, 4, 128], P(('runs', 'depth', 'screen')), parts along dimension 0
The draws below stay inside these ranges and needn't reach their ends.
There are 2 independent parts, one for each index of `runs`. The reference program is written for one: setup_inputs(seed, part) draws one part's arguments, and reference() takes and returns one part's arrays. A program takes and returns all parts, laid end to end along the dimension named above; an argument that names none is the same for every part. Nothing has to cross between parts.
Inputs may be any that keep to these rules, and one draw needn't show every extreme that they name: `foot_start`: in each screen half the first rows of the bricks go from one end of the range to the other as depth grows, with a jitter; the rows of a brick meet only those of the bricks next to it along depth in the same screen half. `foot_rows`: some brick of every group shows all 128 of its rows. `tile_source`: a permutation of the image rows; each aligned block of 256 entries takes exactly 32 rows from each of 8 of the image's aligned blocks of 256 rows, and none from the others.
All inputs are finite; a program needn't handle non-finite values.
Results may differ from the reference program's by a relative error of at most 0.0003.
Values sent between devices are 32-bit elements; how exact they have to be, the bound alone decides.
No kernel may reach another device: no remote copies, remote signals or barrier semaphores. Data moves between devices by JAX's collectives and lax.ppermute only.
A program may use at most 128 MiB of HBM per device.

```python
import math
import jax
import jax.numpy as jnp
from jax import lax

BR = 128
STEPS = 128
PIX = 128
BLK = 256
HALF_ROWS = 2048
IMG_ROWS = 4096
CAP = 32
N_DEPTH = 8
N_SCREEN = 2


def draw_foot_start(key, part):
    flip_key = jax.random.fold_in(key, 31)
    jitter_key = jax.random.fold_in(key, 32)
    span = HALF_ROWS - BR
    steps_between = max(N_DEPTH - 1, 1)
    stride = span // steps_between
    reach = max(stride // 3, 1)
    depth_pos = jnp.arange(N_DEPTH, dtype=jnp.int32)[:, None]
    base = depth_pos * span // steps_between
    jitter = jax.random.randint(jitter_key, (N_DEPTH, N_SCREEN), -reach, reach + 1)
    interior = (depth_pos > 0) & (depth_pos < N_DEPTH - 1)
    leading = base + jitter * interior.astype(jnp.int32)
    previous = jnp.concatenate([leading[:1], leading[:-1]], axis=0)
    paired = interior & (depth_pos % 2 == 0)
    placed = jnp.where(paired, previous + BR // 4, leading)
    placed = jnp.clip(placed, 0, span)
    flips = jax.random.randint(flip_key, (1, N_SCREEN), 0, 2)
    rows = jnp.where(flips == 1, span - placed, placed)
    return rows.astype(jnp.int32)


def draw_foot_rows(key, part):
    low_counts = jax.random.randint(jax.random.fold_in(key, 21), (N_DEPTH, N_SCREEN), BR // 4, BR + 1)
    high_counts = jax.random.randint(jax.random.fold_in(key, 22), (N_DEPTH, N_SCREEN), BR // 2, BR + 1)
    depth_pos = jnp.arange(N_DEPTH, dtype=jnp.int32)[:, None]
    screen_pos = jnp.arange(N_SCREEN, dtype=jnp.int32)[None, :]
    interior = (depth_pos > 0) & (depth_pos < N_DEPTH - 1)
    counts = jnp.where(interior, high_counts, low_counts)
    full_depth = jax.random.randint(jax.random.fold_in(key, 23), (), 1, N_DEPTH - 1)
    full_screen = jax.random.randint(jax.random.fold_in(key, 24), (), 0, N_SCREEN)
    counts = jnp.where((depth_pos == full_depth) & (screen_pos == full_screen), BR, counts)
    narrow_depth = jax.random.randint(jax.random.fold_in(key, 25), (), 0, 2) * (N_DEPTH - 1)
    narrow_screen = jax.random.randint(jax.random.fold_in(key, 26), (), 0, N_SCREEN)
    counts = jnp.where((depth_pos == narrow_depth) & (screen_pos == narrow_screen), BR // 4, counts)
    return counts.astype(jnp.int32)


def draw_tile_source(key, part):
    device_count = N_DEPTH * N_SCREEN
    shift_key = jax.random.fold_in(key, 11)
    row_key = jax.random.fold_in(key, 12)
    slot_key = jax.random.fold_in(key, 13)
    shifts = jax.random.permutation(shift_key, device_count)[:N_DEPTH]
    row_orders = jax.vmap(lambda single: jax.random.permutation(single, BLK))(jax.random.split(row_key, device_count))
    slot_orders = jax.vmap(lambda single: jax.random.permutation(single, BLK))(jax.random.split(slot_key, device_count))
    owners = jnp.arange(device_count)[:, None, None]
    groups = jnp.arange(N_DEPTH)[None, :, None]
    within = jnp.arange(CAP)[None, None, :]
    sources = (owners + shifts[groups]) % device_count
    flat_slot = groups * CAP + within
    source_rows = row_orders[sources, flat_slot]
    values = sources % N_SCREEN * HALF_ROWS + sources // N_SCREEN * BLK + source_rows
    positions = owners * BLK + slot_orders[owners, flat_slot]
    return jnp.zeros((IMG_ROWS,), jnp.int32).at[positions.reshape(-1)].set(values.reshape(-1).astype(jnp.int32))


def steps_of(own_key, shape, shards, least, largest):
    def one(dim, shards_of):
        steps = jax.random.uniform(jax.random.fold_in(jax.random.fold_in(own_key, 6), dim), (shards_of,), jnp.float32, least / len(shards), largest / len(shards))
        return jnp.repeat(jnp.exp(steps), shape[dim] // shards_of).reshape((-1,) + (1,) * (len(shape) - dim - 1))

    loudness = one(*shards[0])
    for cut in shards[1:]:
        loudness = loudness * one(*cut)
    return loudness


def centred(rng, extent, spread, most, pieces=(), held_as=jnp.bfloat16):
    gain = steps_of(rng, extent, pieces, -0.22, 0.18) if pieces else 1.0
    drawn = jax.random.normal(rng, extent, jnp.float32) * spread * gain
    return jnp.minimum(jnp.maximum(drawn, -most), most).astype(held_as)


def setup_inputs(seed: int = 0, part: int = 0) -> dict:
    arg_keys = jax.random.split(jax.random.key(seed), 8)
    own_keys = jax.random.split(jax.random.fold_in(arg_keys[7], part), 8)
    density = centred(own_keys[0], (N_DEPTH, N_SCREEN, BR, STEPS, PIX), 1.0, 6.0, ((0, 8), (1, 2)), jnp.float32)
    foot_start = draw_foot_start(jax.random.fold_in(jax.random.fold_in(arg_keys[7], part), 71), part)
    foot_rows = draw_foot_rows(jax.random.fold_in(jax.random.fold_in(arg_keys[7], part), 71), part)
    extinction = jnp.clip(jnp.exp(jax.random.uniform(own_keys[3], (1,), jnp.float32, math.log(0.4), math.log(1.6))), 0.4, 1.6)
    colour_slope = jnp.clip(jax.random.uniform(arg_keys[4], (3,), jnp.float32, 0.5, 2.5), 0.5, 2.5)
    colour_offset = jnp.clip(jax.random.uniform(arg_keys[5], (3,), jnp.float32, -1.0, 1.0), -1.0, 1.0)
    tile_source = draw_tile_source(jax.random.fold_in(jax.random.fold_in(arg_keys[7], part), 71), part)
    return dict(density=density, foot_start=foot_start, foot_rows=foot_rows, extinction=extinction, colour_slope=colour_slope, colour_offset=colour_offset, tile_source=tile_source)


def render_brick(density_block, start_row, shown_rows, absorb, colour_slope, colour_offset):
    optical = absorb * jax.nn.softplus(density_block) / STEPS
    ahead_sum = jnp.cumsum(optical, axis=1) - optical
    depth_sum = jnp.sum(optical, axis=1)
    weight = jnp.exp(-ahead_sum) * (1.0 - jnp.exp(-optical))
    colours = [jnp.sum(weight * jax.nn.sigmoid(colour_slope[channel] * density_block + colour_offset[channel]), axis=1) for channel in range(3)]
    layers = jnp.stack(colours + [depth_sum], axis=1)
    visible = (jnp.arange(BR) < shown_rows)[:, None, None]
    layers = jnp.where(visible, layers, jnp.zeros_like(layers))
    canvas = jnp.zeros((HALF_ROWS, 4, PIX), layers.dtype)
    return lax.dynamic_update_slice(canvas, layers, (start_row.astype(jnp.int32), jnp.int32(0), jnp.int32(0)))


def reference(density, foot_start, foot_rows, extinction, colour_slope, colour_offset, tile_source):
    absorb = extinction[0]
    bricks = density.reshape(N_DEPTH * N_SCREEN, BR, STEPS, PIX)

    def render_one(packed):
        density_block, start_row, shown_rows = packed
        return render_brick(density_block, start_row, shown_rows, absorb, colour_slope, colour_offset)

    partials = lax.map(render_one, (bricks, foot_start.reshape(-1), foot_rows.reshape(-1)))
    partials = partials.reshape(N_DEPTH, N_SCREEN, HALF_ROWS, 4, PIX)
    optical = partials[:, :, :, 3, :]
    ahead_sum = jnp.cumsum(optical, axis=0) - optical
    total_depth = jnp.sum(optical, axis=0)
    colours = jnp.sum(jnp.exp(-ahead_sum)[:, :, :, None, :] * partials[:, :, :, :3, :], axis=0)
    opacity = 1.0 - jnp.exp(-total_depth)
    picture = jnp.concatenate([colours, opacity[:, :, None, :]], axis=2).reshape(IMG_ROWS, 4, PIX)
    return jnp.take(picture, tile_source.astype(jnp.int32), axis=0)
```

```python
import jax
import jax.numpy as jnp
from jax import lax
from jax.sharding import PartitionSpec as P

BLK = 256


def render_layers(density_block, shown_rows, absorb, colour_slope, colour_offset):
    brick_rows, sample_count, pixels = density_block.shape
    optical = absorb * jax.nn.softplus(density_block) / sample_count
    below_mask = (
        lax.broadcasted_iota(jnp.int32, (sample_count, sample_count), 0)
        > lax.broadcasted_iota(jnp.int32, (sample_count, sample_count), 1)
    ).astype(jnp.float32)
    ahead_sum = jnp.einsum("kj,rjp->rkp", below_mask, optical, precision=lax.Precision.HIGHEST)
    depth_sum = jnp.sum(optical, axis=1)
    weight = jnp.exp(-ahead_sum) * (1.0 - jnp.exp(-optical))
    colours = [
        jnp.sum(
            weight * jax.nn.sigmoid(colour_slope[channel] * density_block + colour_offset[channel]),
            axis=1,
        )
        for channel in range(3)
    ]
    layers = jnp.stack(colours + [depth_sum], axis=1)
    visible = (jnp.arange(brick_rows) < shown_rows)[:, None, None]
    return jnp.where(visible, layers, jnp.zeros_like(layers))


def composite_rows(bricks, starts, counts, image_rows):
    depth_count, brick_rows = bricks.shape[0], bricks.shape[1]
    flat = bricks.reshape((depth_count * brick_rows,) + bricks.shape[2:])
    offset = image_rows[:, None] - starts[None, :]
    covered = (offset >= 0) & (offset < counts[None, :])
    depth_ids = jnp.arange(depth_count)[None, :]
    back = jnp.max(jnp.where(covered, depth_ids, -1), axis=1)
    any_back = back >= 0
    back_c = jnp.maximum(back, 0)
    front_c = jnp.maximum(back - 1, 0)
    back_off = jnp.take_along_axis(offset, back_c[:, None], axis=1)[:, 0]
    front_off = jnp.take_along_axis(offset, front_c[:, None], axis=1)[:, 0]
    front_cov = jnp.take_along_axis(covered, front_c[:, None], axis=1)[:, 0] & (back >= 1)
    back_idx = back_c * brick_rows + jnp.clip(back_off, 0, brick_rows - 1)
    front_idx = front_c * brick_rows + jnp.clip(front_off, 0, brick_rows - 1)
    back_rows = jnp.take(flat, back_idx, axis=0)
    front_rows = jnp.take(flat, front_idx, axis=0)
    back_rows = jnp.where(any_back[:, None, None], back_rows, 0.0)
    front_rows = jnp.where(front_cov[:, None, None], front_rows, 0.0)
    front_depth = front_rows[:, 3:4, :]
    colours = front_rows[:, :3, :] + jnp.exp(-front_depth) * back_rows[:, :3, :]
    opacity = 1.0 - jnp.exp(-(front_depth + back_rows[:, 3:4, :]))
    return jnp.concatenate([colours, opacity], axis=1)


def on_device(density, foot_start, foot_rows, extinction, colour_slope, colour_offset, tile_source):
    depth_count = lax.axis_size("depth")
    screen_count = lax.axis_size("screen")
    depth_index = lax.axis_index("depth")
    screen_index = lax.axis_index("screen")
    image_total = tile_source.shape[0]
    half_rows = image_total // screen_count
    owner_rows = image_total // (depth_count * screen_count)
    my_starts = foot_start.reshape(depth_count, screen_count)
    my_counts = foot_rows.reshape(depth_count, screen_count)
    shown = my_counts[depth_index, screen_index]
    layers = render_layers(density[0, 0], shown, extinction[0], colour_slope, colour_offset)
    bricks = lax.all_gather(layers, "depth")
    starts = lax.dynamic_index_in_dim(my_starts, screen_index, axis=1, keepdims=False)
    counts = lax.dynamic_index_in_dim(my_counts, screen_index, axis=1, keepdims=False)
    self_owner = depth_index * screen_count + screen_index
    partner_owner = depth_index * screen_count + (1 - screen_index)
    wanted_self = lax.dynamic_slice_in_dim(tile_source, self_owner * owner_rows, owner_rows)
    wanted_partner = lax.dynamic_slice_in_dim(tile_source, partner_owner * owner_rows, owner_rows)
    wanted = jnp.concatenate([wanted_self, wanted_partner])
    rows = composite_rows(bricks, starts, counts, wanted % half_rows)
    mine = rows[:owner_rows]
    for_partner = rows[owner_rows:]
    received = lax.ppermute(for_partner, "screen", [(0, 1), (1, 0)])
    in_my_half = (wanted_self // half_rows) == screen_index
    return jnp.where(in_my_half[:, None, None], mine, received)


def solution(mesh):
    return jax.shard_map(
        on_device,
        mesh=mesh,
        in_specs=(
            P(("runs", "depth"), "screen", None, None, None),
            P("runs", None),
            P("runs", None),
            P("runs"),
            P(),
            P(),
            P("runs"),
        ),
        out_specs=P(("runs", "depth", "screen"), None, None),
        check_vma=False,
    )
```

```python
import jax
import jax.numpy as jnp
from jax import lax
from jax.sharding import PartitionSpec as P

BLK = 256


def render_layers(density_block, shown_rows, absorb, colour_slope, colour_offset):
    brick_rows, sample_count, pixels = density_block.shape
    optical = absorb * jax.nn.softplus(density_block) / sample_count
    below_mask = (
        lax.broadcasted_iota(jnp.int32, (sample_count, sample_count), 0)
        > lax.broadcasted_iota(jnp.int32, (sample_count, sample_count), 1)
    ).astype(jnp.float32)
    ahead_sum = jnp.einsum("kj,rjp->rkp", below_mask, optical, precision=lax.Precision.HIGHEST)
    depth_sum = jnp.sum(optical, axis=1)
    weight = jnp.exp(-ahead_sum) * (1.0 - jnp.exp(-optical))
    colours = [
        jnp.sum(
            weight * jax.nn.sigmoid(colour_slope[channel] * density_block + colour_offset[channel]),
            axis=1,
        )
        for channel in range(3)
    ]
    layers = jnp.stack(colours + [depth_sum], axis=1)
    visible = (jnp.arange(brick_rows) < shown_rows)[:, None, None]
    return jnp.where(visible, layers, jnp.zeros_like(layers))


def composite_rows(flat, starts, counts, stride, image_rows):
    depth_count = starts.shape[0]
    offset = image_rows[:, None] - starts[None, :]
    covered = (offset >= 0) & (offset < counts[None, :])
    depth_ids = jnp.arange(depth_count, dtype=jnp.int32)[None, :]
    back = jnp.max(jnp.where(covered, depth_ids, -1), axis=1)
    is_back = depth_ids == back[:, None]
    is_front = (depth_ids == back[:, None] - 1) & covered
    back_off = jnp.sum(jnp.where(is_back, offset, 0), axis=1)
    front_off = jnp.sum(jnp.where(is_front, offset, 0), axis=1)
    has_front = jnp.any(is_front, axis=1)
    has_back = back >= 0
    back_idx = jnp.where(has_back, back * stride + back_off, 0)
    front_idx = jnp.where(has_front, (back - 1) * stride + front_off, 0)
    back_rows = jnp.take(flat, back_idx, axis=0, mode="clip")
    front_rows = jnp.take(flat, front_idx, axis=0, mode="clip")
    back_rows = jnp.where(has_back[:, None, None], back_rows, 0.0)
    front_rows = jnp.where(has_front[:, None, None], front_rows, 0.0)
    front_depth = front_rows[:, 3:4, :]
    colours = front_rows[:, :3, :] + jnp.exp(-front_depth) * back_rows[:, :3, :]
    opacity = 1.0 - jnp.exp(-(front_depth + back_rows[:, 3:4, :]))
    return jnp.concatenate([colours, opacity], axis=1)


def on_device(density, foot_start, foot_rows, extinction, colour_slope, colour_offset, tile_source):
    depth_count = lax.axis_size("depth")
    screen_count = lax.axis_size("screen")
    depth_index = lax.axis_index("depth")
    screen_index = lax.axis_index("screen")
    image_total = tile_source.shape[0]
    half_rows = image_total // screen_count
    owner_rows = image_total // (depth_count * screen_count)
    start = foot_start[0, 0]
    shown = foot_rows[0, 0]
    layers = render_layers(density[0, 0], shown, extinction[0], colour_slope, colour_offset)
    brick_rows, channels, pixels = layers.shape
    lane = lax.broadcasted_iota(jnp.int32, (1, channels, pixels), 2)
    meta = jnp.where(lane == 0, start, jnp.where(lane == 1, shown, 0)).astype(jnp.float32)
    stride = brick_rows + 1
    flat = lax.all_gather(jnp.concatenate([layers, meta], axis=0), "depth", tiled=True)
    meta_rows = flat.reshape(depth_count, stride, channels, pixels)[:, brick_rows, 0, :2]
    starts = meta_rows[:, 0].astype(jnp.int32)
    counts = meta_rows[:, 1].astype(jnp.int32)
    self_owner = depth_index * screen_count + screen_index
    partner_owner = depth_index * screen_count + (1 - screen_index)
    wanted_self = lax.dynamic_slice_in_dim(tile_source, self_owner * owner_rows, owner_rows)
    wanted_partner = lax.dynamic_slice_in_dim(tile_source, partner_owner * owner_rows, owner_rows)
    wanted = jnp.concatenate([wanted_self, wanted_partner])
    rows = composite_rows(flat, starts, counts, stride, wanted % half_rows)
    mine = rows[:owner_rows]
    for_partner = rows[owner_rows:]
    received = lax.ppermute(for_partner, "screen", [(0, 1), (1, 0)])
    in_my_half = (wanted_self // half_rows) == screen_index
    return jnp.where(in_my_half[:, None, None], mine, received)


def solution(mesh):
    return jax.shard_map(
        on_device,
        mesh=mesh,
        in_specs=(
            P(("runs", "depth"), "screen", None, None, None),
            P(("runs", "depth"), "screen"),
            P(("runs", "depth"), "screen"),
            P("runs"),
            P(),
            P(),
            P("runs"),
        ),
        out_specs=P(("runs", "depth", "screen"), None, None),
        check_vma=False,
    )
```

```python
import jax
import jax.numpy as jnp
from jax import lax
from jax.sharding import PartitionSpec as P

BLK = 256


def render_layers(density_block, shown_rows, absorb, colour_slope, colour_offset):
    brick_rows, sample_count, pixels = density_block.shape
    optical = absorb * jax.nn.softplus(density_block) / sample_count
    below_mask = (
        lax.broadcasted_iota(jnp.int32, (sample_count, sample_count), 0)
        > lax.broadcasted_iota(jnp.int32, (sample_count, sample_count), 1)
    ).astype(jnp.float32)
    ahead_sum = jnp.einsum("kj,rjp->rkp", below_mask, optical, precision=lax.Precision.HIGHEST)
    depth_sum = jnp.sum(optical, axis=1)
    weight = jnp.exp(-ahead_sum) * (1.0 - jnp.exp(-optical))
    colours = [
        jnp.sum(
            weight * jax.nn.sigmoid(colour_slope[channel] * density_block + colour_offset[channel]),
            axis=1,
        )
        for channel in range(3)
    ]
    layers = jnp.stack(colours + [depth_sum], axis=1)
    visible = (jnp.arange(brick_rows) < shown_rows)[:, None, None]
    return jnp.where(visible, layers, jnp.zeros_like(layers))


def composite_rows(flat, starts, counts, brick_ids, stride, image_rows):
    slot_count = starts.shape[0]
    offset = image_rows[:, None] - starts[None, :]
    covered = (offset >= 0) & (offset < counts[None, :])
    depth_ids = brick_ids[None, :]
    slot_ids = jnp.arange(slot_count, dtype=jnp.int32)[None, :]
    back = jnp.max(jnp.where(covered, depth_ids, -1), axis=1)
    is_back = (depth_ids == back[:, None]) & covered
    is_front = (depth_ids == back[:, None] - 1) & covered
    back_off = jnp.sum(jnp.where(is_back, offset, 0), axis=1)
    front_off = jnp.sum(jnp.where(is_front, offset, 0), axis=1)
    back_slot = jnp.sum(jnp.where(is_back, slot_ids, 0), axis=1)
    front_slot = jnp.sum(jnp.where(is_front, slot_ids, 0), axis=1)
    has_front = jnp.any(is_front, axis=1)
    has_back = back >= 0
    back_idx = jnp.where(has_back, back_slot * stride + back_off, 0)
    front_idx = jnp.where(has_front, front_slot * stride + front_off, 0)
    back_rows = jnp.take(flat, back_idx, axis=0, mode="clip")
    front_rows = jnp.take(flat, front_idx, axis=0, mode="clip")
    back_rows = jnp.where(has_back[:, None, None], back_rows, 0.0)
    front_rows = jnp.where(has_front[:, None, None], front_rows, 0.0)
    front_depth = front_rows[:, 3:4, :]
    colours = front_rows[:, :3, :] + jnp.exp(-front_depth) * back_rows[:, :3, :]
    opacity = 1.0 - jnp.exp(-(front_depth + back_rows[:, 3:4, :]))
    return jnp.concatenate([colours, opacity], axis=1)


def ring_order(count):
    return list(range(0, count, 2)) + list(range(count - 1 - count % 2, 0, -2))


def ring_gather(own, count):
    order = ring_order(count)
    forward = [(order[k], order[(k + 1) % count]) for k in range(count)]
    backward = [(b, a) for a, b in forward]
    slots = [own]
    ahead = own
    behind = own
    for step in range(1, count // 2 + 1):
        ahead = lax.ppermute(ahead, "depth", forward)
        slots.append(ahead)
        if 2 * step < count:
            behind = lax.ppermute(behind, "depth", backward)
            slots.append(behind)
    return jnp.concatenate(slots, axis=0)


def on_device(density, foot_start, foot_rows, extinction, colour_slope, colour_offset, tile_source):
    depth_count = lax.axis_size("depth")
    screen_count = lax.axis_size("screen")
    depth_index = lax.axis_index("depth")
    screen_index = lax.axis_index("screen")
    image_total = tile_source.shape[0]
    half_rows = image_total // screen_count
    owner_rows = image_total // (depth_count * screen_count)
    start = foot_start[0, 0]
    shown = foot_rows[0, 0]
    layers = render_layers(density[0, 0], shown, extinction[0], colour_slope, colour_offset)
    brick_rows, channels, pixels = layers.shape
    lane = lax.broadcasted_iota(jnp.int32, (1, channels, pixels), 2)
    meta = jnp.where(lane == 0, start, jnp.where(lane == 1, shown, jnp.where(lane == 2, depth_index, 0)))
    stride = brick_rows + 1
    own = jnp.concatenate([layers, meta.astype(jnp.float32)], axis=0)
    flat = ring_gather(own, depth_count)
    meta_rows = flat.reshape(depth_count, stride, channels, pixels)[:, brick_rows, 0, :3]
    starts = meta_rows[:, 0].astype(jnp.int32)
    counts = meta_rows[:, 1].astype(jnp.int32)
    brick_ids = meta_rows[:, 2].astype(jnp.int32)
    self_owner = depth_index * screen_count + screen_index
    partner_owner = depth_index * screen_count + (1 - screen_index)
    wanted_self = lax.dynamic_slice_in_dim(tile_source, self_owner * owner_rows, owner_rows)
    wanted_partner = lax.dynamic_slice_in_dim(tile_source, partner_owner * owner_rows, owner_rows)
    wanted = jnp.concatenate([wanted_self, wanted_partner])
    rows = composite_rows(flat, starts, counts, brick_ids, stride, wanted % half_rows)
    mine = rows[:owner_rows]
    for_partner = rows[owner_rows:]
    received = lax.ppermute(for_partner, "screen", [(0, 1), (1, 0)])
    in_my_half = (wanted_self // half_rows) == screen_index
    return jnp.where(in_my_half[:, None, None], mine, received)


def solution(mesh):
    return jax.shard_map(
        on_device,
        mesh=mesh,
        in_specs=(
            P(("runs", "depth"), "screen", None, None, None),
            P(("runs", "depth"), "screen"),
            P(("runs", "depth"), "screen"),
            P("runs"),
            P(),
            P(),
            P("runs"),
        ),
        out_specs=P(("runs", "depth", "screen"), None, None),
        check_vma=False,
    )
```

```python
import jax
import jax.numpy as jnp
from jax import lax
from jax.sharding import PartitionSpec as P
from jax.experimental import pallas as pl
from jax.experimental.pallas import tpu as pltpu

BLK = 256


def render_kernel(params_ref, density_ref, out_ref):
    block_rows, sample_count, pixels = density_ref.shape
    absorb = params_ref[0]
    shown = params_ref[7]
    below_mask = (
        lax.broadcasted_iota(jnp.int32, (sample_count, sample_count), 0)
        > lax.broadcasted_iota(jnp.int32, (sample_count, sample_count), 1)
    ).astype(jnp.float32)
    first_row = pl.program_id(0) * block_rows

    def one_row(row, carry):
        values = density_ref[row]
        optical = absorb * jax.nn.softplus(values) / sample_count
        ahead_sum = jnp.dot(below_mask, optical, precision=lax.Precision.HIGHEST,
                            preferred_element_type=jnp.float32)
        weight = jnp.exp(-ahead_sum) * (1.0 - jnp.exp(-optical))
        parts = [
            jnp.sum(weight * jax.nn.sigmoid(params_ref[1 + channel] * values + params_ref[4 + channel]),
                    axis=0, keepdims=True)
            for channel in range(3)
        ]
        parts.append(jnp.sum(optical, axis=0, keepdims=True))
        layer = jnp.concatenate(parts, axis=0)
        visible = (first_row + row).astype(jnp.float32) < shown
        out_ref[row] = jnp.where(visible, layer, 0.0)
        return carry

    lax.fori_loop(0, block_rows, one_row, 0)


def render_layers(density_block, shown_rows, absorb, colour_slope, colour_offset, block_rows=8):
    brick_rows, sample_count, pixels = density_block.shape
    params = jnp.concatenate([
        absorb.reshape(1), colour_slope, colour_offset,
        shown_rows.astype(jnp.float32).reshape(1),
    ])
    return pl.pallas_call(
        render_kernel,
        grid=(brick_rows // block_rows,),
        in_specs=[
            pl.BlockSpec(memory_space=pltpu.SMEM),
            pl.BlockSpec((block_rows, sample_count, pixels), lambda i: (i, 0, 0)),
        ],
        out_specs=pl.BlockSpec((block_rows, 4, pixels), lambda i: (i, 0, 0)),
        out_shape=jax.ShapeDtypeStruct((brick_rows, 4, pixels), jnp.float32),
    )(params, density_block)


def composite_rows(flat, starts, counts, brick_ids, stride, image_rows):
    slot_count = starts.shape[0]
    offset = image_rows[:, None] - starts[None, :]
    covered = (offset >= 0) & (offset < counts[None, :])
    depth_ids = brick_ids[None, :]
    slot_ids = jnp.arange(slot_count, dtype=jnp.int32)[None, :]
    back = jnp.max(jnp.where(covered, depth_ids, -1), axis=1)
    is_back = (depth_ids == back[:, None]) & covered
    is_front = (depth_ids == back[:, None] - 1) & covered
    back_off = jnp.sum(jnp.where(is_back, offset, 0), axis=1)
    front_off = jnp.sum(jnp.where(is_front, offset, 0), axis=1)
    back_slot = jnp.sum(jnp.where(is_back, slot_ids, 0), axis=1)
    front_slot = jnp.sum(jnp.where(is_front, slot_ids, 0), axis=1)
    has_front = jnp.any(is_front, axis=1)
    has_back = back >= 0
    back_idx = jnp.where(has_back, back_slot * stride + back_off, 0)
    front_idx = jnp.where(has_front, front_slot * stride + front_off, 0)
    back_rows = jnp.take(flat, back_idx, axis=0, mode="clip")
    front_rows = jnp.take(flat, front_idx, axis=0, mode="clip")
    back_rows = jnp.where(has_back[:, None, None], back_rows, 0.0)
    front_rows = jnp.where(has_front[:, None, None], front_rows, 0.0)
    front_depth = front_rows[:, 3:4, :]
    colours = front_rows[:, :3, :] + jnp.exp(-front_depth) * back_rows[:, :3, :]
    opacity = 1.0 - jnp.exp(-(front_depth + back_rows[:, 3:4, :]))
    return jnp.concatenate([colours, opacity], axis=1)


def ring_order(count):
    return list(range(0, count, 2)) + list(range(count - 1 - count % 2, 0, -2))


def ring_gather(own, count):
    order = ring_order(count)
    forward = [(order[k], order[(k + 1) % count]) for k in range(count)]
    backward = [(b, a) for a, b in forward]
    slots = [own]
    ahead = own
    behind = own
    for step in range(1, count // 2 + 1):
        ahead = lax.ppermute(ahead, "depth", forward)
        slots.append(ahead)
        if 2 * step < count:
            behind = lax.ppermute(behind, "depth", backward)
            slots.append(behind)
    return jnp.concatenate(slots, axis=0)


def on_device(density, foot_start, foot_rows, extinction, colour_slope, colour_offset, tile_source):
    depth_count = lax.axis_size("depth")
    screen_count = lax.axis_size("screen")
    depth_index = lax.axis_index("depth")
    screen_index = lax.axis_index("screen")
    image_total = tile_source.shape[0]
    half_rows = image_total // screen_count
    owner_rows = image_total // (depth_count * screen_count)
    start = foot_start[0, 0]
    shown = foot_rows[0, 0]
    layers = render_layers(density[0, 0], shown, extinction[0], colour_slope, colour_offset)
    brick_rows, channels, pixels = layers.shape
    lane = lax.broadcasted_iota(jnp.int32, (1, channels, pixels), 2)
    meta = jnp.where(lane == 0, start, jnp.where(lane == 1, shown, jnp.where(lane == 2, depth_index, 0)))
    stride = brick_rows + 1
    own = jnp.concatenate([layers, meta.astype(jnp.float32)], axis=0)
    flat = ring_gather(own, depth_count)
    meta_rows = flat.reshape(depth_count, stride, channels, pixels)[:, brick_rows, 0, :3]
    starts = meta_rows[:, 0].astype(jnp.int32)
    counts = meta_rows[:, 1].astype(jnp.int32)
    brick_ids = meta_rows[:, 2].astype(jnp.int32)
    self_owner = depth_index * screen_count + screen_index
    partner_owner = depth_index * screen_count + (1 - screen_index)
    wanted_self = lax.dynamic_slice_in_dim(tile_source, self_owner * owner_rows, owner_rows)
    wanted_partner = lax.dynamic_slice_in_dim(tile_source, partner_owner * owner_rows, owner_rows)
    wanted = jnp.concatenate([wanted_self, wanted_partner])
    rows = composite_rows(flat, starts, counts, brick_ids, stride, wanted % half_rows)
    mine = rows[:owner_rows]
    for_partner = rows[owner_rows:]
    received = lax.ppermute(for_partner, "screen", [(0, 1), (1, 0)])
    in_my_half = (wanted_self // half_rows) == screen_index
    return jnp.where(in_my_half[:, None, None], mine, received)


def solution(mesh):
    return jax.shard_map(
        on_device,
        mesh=mesh,
        in_specs=(
            P(("runs", "depth"), "screen", None, None, None),
            P(("runs", "depth"), "screen"),
            P(("runs", "depth"), "screen"),
            P("runs"),
            P(),
            P(),
            P("runs"),
        ),
        out_specs=P(("runs", "depth", "screen"), None, None),
        check_vma=False,
    )
```

```python
import jax
import jax.numpy as jnp
from jax import lax
from jax.sharding import PartitionSpec as P
from jax.experimental import pallas as pl
from jax.experimental.pallas import tpu as pltpu

BLK = 256


def render_kernel(params_ref, density_ref, out_ref):
    block_rows = out_ref.shape[1]
    pixels = out_ref.shape[2]
    sample_count = density_ref.shape[0] // block_rows
    absorb = params_ref[0]
    slopes = [params_ref[1 + channel] for channel in range(3)]
    offsets = [params_ref[4 + channel] for channel in range(3)]
    shown = params_ref[7]

    def one_step(step, carry):
        transmit, depth_sum = carry[0], carry[1]
        values = density_ref[pl.ds(step, block_rows, stride=sample_count), :]
        optical = absorb * jax.nn.softplus(values) / sample_count
        passed = jnp.exp(-optical)
        weight = transmit * (1.0 - passed)
        colours = tuple(
            carry[2 + channel] + weight * jax.nn.sigmoid(slopes[channel] * values + offsets[channel])
            for channel in range(3)
        )
        return (transmit * passed, depth_sum + optical) + colours

    zeros = jnp.zeros((block_rows, pixels), jnp.float32)
    carry = (jnp.ones((block_rows, pixels), jnp.float32), zeros, zeros, zeros, zeros)
    carry = lax.fori_loop(0, sample_count, one_step, carry, unroll=8)
    row_ids = pl.program_id(0) * block_rows + lax.broadcasted_iota(jnp.int32, (block_rows, pixels), 0)
    visible = row_ids.astype(jnp.float32) < shown
    for channel in range(3):
        out_ref[channel] = jnp.where(visible, carry[2 + channel], 0.0)
    out_ref[3] = jnp.where(visible, carry[1], 0.0)


def render_layers(density_block, shown_rows, absorb, colour_slope, colour_offset, block_rows=8):
    brick_rows, sample_count, pixels = density_block.shape
    params = jnp.concatenate([
        absorb.reshape(1), colour_slope, colour_offset,
        shown_rows.astype(jnp.float32).reshape(1),
    ])
    planes = pl.pallas_call(
        render_kernel,
        grid=(brick_rows // block_rows,),
        in_specs=[
            pl.BlockSpec(memory_space=pltpu.SMEM),
            pl.BlockSpec((block_rows * sample_count, pixels), lambda i: (i, 0)),
        ],
        out_specs=pl.BlockSpec((4, block_rows, pixels), lambda i: (0, i, 0)),
        out_shape=jax.ShapeDtypeStruct((4, brick_rows, pixels), jnp.float32),
    )(params, density_block.reshape(brick_rows * sample_count, pixels))
    return jnp.transpose(planes, (1, 0, 2))


def composite_rows(flat, starts, counts, brick_ids, stride, image_rows):
    slot_count = starts.shape[0]
    offset = image_rows[:, None] - starts[None, :]
    covered = (offset >= 0) & (offset < counts[None, :])
    depth_ids = brick_ids[None, :]
    slot_ids = jnp.arange(slot_count, dtype=jnp.int32)[None, :]
    back = jnp.max(jnp.where(covered, depth_ids, -1), axis=1)
    is_back = (depth_ids == back[:, None]) & covered
    is_front = (depth_ids == back[:, None] - 1) & covered
    back_off = jnp.sum(jnp.where(is_back, offset, 0), axis=1)
    front_off = jnp.sum(jnp.where(is_front, offset, 0), axis=1)
    back_slot = jnp.sum(jnp.where(is_back, slot_ids, 0), axis=1)
    front_slot = jnp.sum(jnp.where(is_front, slot_ids, 0), axis=1)
    has_front = jnp.any(is_front, axis=1)
    has_back = back >= 0
    back_idx = jnp.where(has_back, back_slot * stride + back_off, 0)
    front_idx = jnp.where(has_front, front_slot * stride + front_off, 0)
    back_rows = jnp.take(flat, back_idx, axis=0, mode="clip")
    front_rows = jnp.take(flat, front_idx, axis=0, mode="clip")
    back_rows = jnp.where(has_back[:, None, None], back_rows, 0.0)
    front_rows = jnp.where(has_front[:, None, None], front_rows, 0.0)
    front_depth = front_rows[:, 3:4, :]
    colours = front_rows[:, :3, :] + jnp.exp(-front_depth) * back_rows[:, :3, :]
    opacity = 1.0 - jnp.exp(-(front_depth + back_rows[:, 3:4, :]))
    return jnp.concatenate([colours, opacity], axis=1)


def ring_order(count):
    return list(range(0, count, 2)) + list(range(count - 1 - count % 2, 0, -2))


def ring_gather(own, count):
    order = ring_order(count)
    forward = [(order[k], order[(k + 1) % count]) for k in range(count)]
    backward = [(b, a) for a, b in forward]
    slots = [own]
    ahead = own
    behind = own
    for step in range(1, count // 2 + 1):
        ahead = lax.ppermute(ahead, "depth", forward)
        slots.append(ahead)
        if 2 * step < count:
            behind = lax.ppermute(behind, "depth", backward)
            slots.append(behind)
    return jnp.concatenate(slots, axis=0)


def on_device(density, foot_start, foot_rows, extinction, colour_slope, colour_offset, tile_source):
    depth_count = lax.axis_size("depth")
    screen_count = lax.axis_size("screen")
    depth_index = lax.axis_index("depth")
    screen_index = lax.axis_index("screen")
    image_total = tile_source.shape[0]
    half_rows = image_total // screen_count
    owner_rows = image_total // (depth_count * screen_count)
    start = foot_start[0, 0]
    shown = foot_rows[0, 0]
    layers = render_layers(density[0, 0], shown, extinction[0], colour_slope, colour_offset)
    brick_rows, channels, pixels = layers.shape
    lane = lax.broadcasted_iota(jnp.int32, (1, channels, pixels), 2)
    meta = jnp.where(lane == 0, start, jnp.where(lane == 1, shown, jnp.where(lane == 2, depth_index, 0)))
    stride = brick_rows + 1
    own = jnp.concatenate([layers, meta.astype(jnp.float32)], axis=0)
    flat = ring_gather(own, depth_count)
    meta_rows = flat.reshape(depth_count, stride, channels, pixels)[:, brick_rows, 0, :3]
    starts = meta_rows[:, 0].astype(jnp.int32)
    counts = meta_rows[:, 1].astype(jnp.int32)
    brick_ids = meta_rows[:, 2].astype(jnp.int32)
    self_owner = depth_index * screen_count + screen_index
    partner_owner = depth_index * screen_count + (1 - screen_index)
    wanted_self = lax.dynamic_slice_in_dim(tile_source, self_owner * owner_rows, owner_rows)
    wanted_partner = lax.dynamic_slice_in_dim(tile_source, partner_owner * owner_rows, owner_rows)
    wanted = jnp.concatenate([wanted_self, wanted_partner])
    rows = composite_rows(flat, starts, counts, brick_ids, stride, wanted % half_rows)
    mine = rows[:owner_rows]
    for_partner = rows[owner_rows:]
    received = lax.ppermute(for_partner, "screen", [(0, 1), (1, 0)])
    in_my_half = (wanted_self // half_rows) == screen_index
    return jnp.where(in_my_half[:, None, None], mine, received)


def solution(mesh):
    return jax.shard_map(
        on_device,
        mesh=mesh,
        in_specs=(
            P(("runs", "depth"), "screen", None, None, None),
            P(("runs", "depth"), "screen"),
            P(("runs", "depth"), "screen"),
            P("runs"),
            P(),
            P(),
            P("runs"),
        ),
        out_specs=P(("runs", "depth", "screen"), None, None),
        check_vma=False,
    )
```

```python
import jax
import jax.numpy as jnp
from jax import lax
from jax.sharding import PartitionSpec as P
from jax.experimental import pallas as pl
from jax.experimental.pallas import tpu as pltpu

BLK = 256


def render_kernel(params_ref, density_ref, out_ref):
    block_rows = out_ref.shape[0]
    pixels = out_ref.shape[2]
    sample_count = density_ref.shape[0] // block_rows
    absorb = params_ref[0]
    slopes = [params_ref[1 + channel] for channel in range(3)]
    offsets = [params_ref[4 + channel] for channel in range(3)]
    shown = params_ref[7]

    def one_step(step, carry):
        transmit, depth_sum = carry[0], carry[1]
        values = density_ref[pl.ds(step, block_rows, stride=sample_count), :]
        optical = absorb * jax.nn.softplus(values) / sample_count
        passed = jnp.exp(-optical)
        weight = transmit * (1.0 - passed)
        colours = tuple(
            carry[2 + channel] + weight * jax.nn.sigmoid(slopes[channel] * values + offsets[channel])
            for channel in range(3)
        )
        return (transmit * passed, depth_sum + optical) + colours

    zeros = jnp.zeros((block_rows, pixels), jnp.float32)
    carry = (jnp.ones((block_rows, pixels), jnp.float32), zeros, zeros, zeros, zeros)
    carry = lax.fori_loop(0, sample_count, one_step, carry, unroll=8)
    row_ids = pl.program_id(0) * block_rows + lax.broadcasted_iota(jnp.int32, (block_rows, pixels), 0)
    visible = row_ids.astype(jnp.float32) < shown
    for channel in range(3):
        out_ref[:, channel, :] = jnp.where(visible, carry[2 + channel], 0.0)
    out_ref[:, 3, :] = jnp.where(visible, carry[1], 0.0)


def render_layers(density_block, shown_rows, absorb, colour_slope, colour_offset, block_rows=8):
    brick_rows, sample_count, pixels = density_block.shape
    params = jnp.concatenate([
        absorb.reshape(1), colour_slope, colour_offset,
        shown_rows.astype(jnp.float32).reshape(1),
    ])
    return pl.pallas_call(
        render_kernel,
        grid=(brick_rows // block_rows,),
        in_specs=[
            pl.BlockSpec(memory_space=pltpu.SMEM),
            pl.BlockSpec((block_rows * sample_count, pixels), lambda i: (i, 0)),
        ],
        out_specs=pl.BlockSpec((block_rows, 4, pixels), lambda i: (i, 0, 0)),
        out_shape=jax.ShapeDtypeStruct((brick_rows, 4, pixels), jnp.float32),
    )(params, density_block.reshape(brick_rows * sample_count, pixels))


def composite_rows(flat, starts, counts, brick_ids, stride, image_rows):
    slot_count = starts.shape[0]
    offset = image_rows[:, None] - starts[None, :]
    covered = (offset >= 0) & (offset < counts[None, :])
    depth_ids = brick_ids[None, :]
    slot_ids = jnp.arange(slot_count, dtype=jnp.int32)[None, :]
    back = jnp.max(jnp.where(covered, depth_ids, -1), axis=1)
    is_back = (depth_ids == back[:, None]) & covered
    is_front = (depth_ids == back[:, None] - 1) & covered
    back_off = jnp.sum(jnp.where(is_back, offset, 0), axis=1)
    front_off = jnp.sum(jnp.where(is_front, offset, 0), axis=1)
    back_slot = jnp.sum(jnp.where(is_back, slot_ids, 0), axis=1)
    front_slot = jnp.sum(jnp.where(is_front, slot_ids, 0), axis=1)
    has_front = jnp.any(is_front, axis=1)
    has_back = back >= 0
    back_idx = jnp.where(has_back, back_slot * stride + back_off, 0)
    front_idx = jnp.where(has_front, front_slot * stride + front_off, 0)
    back_rows = jnp.take(flat, back_idx, axis=0, mode="clip")
    front_rows = jnp.take(flat, front_idx, axis=0, mode="clip")
    back_rows = jnp.where(has_back[:, None, None], back_rows, 0.0)
    front_rows = jnp.where(has_front[:, None, None], front_rows, 0.0)
    front_depth = front_rows[:, 3:4, :]
    colours = front_rows[:, :3, :] + jnp.exp(-front_depth) * back_rows[:, :3, :]
    opacity = 1.0 - jnp.exp(-(front_depth + back_rows[:, 3:4, :]))
    return jnp.concatenate([colours, opacity], axis=1)


def ring_order(count):
    return list(range(0, count, 2)) + list(range(count - 1 - count % 2, 0, -2))


def ring_gather(own, count):
    order = ring_order(count)
    forward = [(order[k], order[(k + 1) % count]) for k in range(count)]
    backward = [(b, a) for a, b in forward]
    slots = [own]
    ahead = own
    behind = own
    for step in range(1, count // 2 + 1):
        ahead = lax.ppermute(ahead, "depth", forward)
        slots.append(ahead)
        if 2 * step < count:
            behind = lax.ppermute(behind, "depth", backward)
            slots.append(behind)
    return jnp.concatenate(slots, axis=0)


def on_device(density, foot_start, foot_rows, extinction, colour_slope, colour_offset, tile_source):
    depth_count = lax.axis_size("depth")
    screen_count = lax.axis_size("screen")
    depth_index = lax.axis_index("depth")
    screen_index = lax.axis_index("screen")
    image_total = tile_source.shape[0]
    half_rows = image_total // screen_count
    owner_rows = image_total // (depth_count * screen_count)
    start = foot_start[0, 0]
    shown = foot_rows[0, 0]
    layers = render_layers(density[0, 0], shown, extinction[0], colour_slope, colour_offset)
    brick_rows, channels, pixels = layers.shape
    lane = lax.broadcasted_iota(jnp.int32, (1, channels, pixels), 2)
    meta = jnp.where(lane == 0, start, jnp.where(lane == 1, shown, jnp.where(lane == 2, depth_index, 0)))
    stride = brick_rows + 1
    own = jnp.concatenate([layers, meta.astype(jnp.float32)], axis=0)
    flat = ring_gather(own, depth_count)
    meta_rows = flat.reshape(depth_count, stride, channels, pixels)[:, brick_rows, 0, :3]
    starts = meta_rows[:, 0].astype(jnp.int32)
    counts = meta_rows[:, 1].astype(jnp.int32)
    brick_ids = meta_rows[:, 2].astype(jnp.int32)
    self_owner = depth_index * screen_count + screen_index
    partner_owner = depth_index * screen_count + (1 - screen_index)
    wanted_self = lax.dynamic_slice_in_dim(tile_source, self_owner * owner_rows, owner_rows)
    wanted_partner = lax.dynamic_slice_in_dim(tile_source, partner_owner * owner_rows, owner_rows)
    wanted = jnp.concatenate([wanted_self, wanted_partner])
    rows = composite_rows(flat, starts, counts, brick_ids, stride, wanted % half_rows)
    mine = rows[:owner_rows]
    for_partner = rows[owner_rows:]
    received = lax.ppermute(for_partner, "screen", [(0, 1), (1, 0)])
    in_my_half = (wanted_self // half_rows) == screen_index
    return jnp.where(in_my_half[:, None, None], mine, received)


def solution(mesh):
    return jax.shard_map(
        on_device,
        mesh=mesh,
        in_specs=(
            P(("runs", "depth"), "screen", None, None, None),
            P(("runs", "depth"), "screen"),
            P(("runs", "depth"), "screen"),
            P("runs"),
            P(),
            P(),
            P("runs"),
        ),
        out_specs=P(("runs", "depth", "screen"), None, None),
        check_vma=False,
    )
```

```python
import functools

import jax
import jax.numpy as jnp
from jax import lax
from jax.sharding import PartitionSpec as P
from jax.experimental import pallas as pl
from jax.experimental.pallas import tpu as pltpu

BLK = 256


def render_kernel(first_block, params_ref, density_ref, out_ref):
    block_rows = out_ref.shape[0]
    pixels = out_ref.shape[2]
    sample_count = density_ref.shape[0] // block_rows
    absorb = params_ref[0]
    slopes = [params_ref[1 + channel] for channel in range(3)]
    offsets = [params_ref[4 + channel] for channel in range(3)]
    shown = params_ref[7]

    def one_step(step, carry):
        transmit, depth_sum = carry[0], carry[1]
        values = density_ref[pl.ds(step, block_rows, stride=sample_count), :]
        optical = absorb * jax.nn.softplus(values) / sample_count
        passed = jnp.exp(-optical)
        weight = transmit * (1.0 - passed)
        colours = tuple(
            carry[2 + channel] + weight * jax.nn.sigmoid(slopes[channel] * values + offsets[channel])
            for channel in range(3)
        )
        return (transmit * passed, depth_sum + optical) + colours

    zeros = jnp.zeros((block_rows, pixels), jnp.float32)
    carry = (jnp.ones((block_rows, pixels), jnp.float32), zeros, zeros, zeros, zeros)
    carry = lax.fori_loop(0, sample_count, one_step, carry, unroll=8)
    row_ids = (pl.program_id(0) + first_block) * block_rows + lax.broadcasted_iota(jnp.int32, (block_rows, pixels), 0)
    visible = row_ids.astype(jnp.float32) < shown
    for channel in range(3):
        out_ref[:, channel, :] = jnp.where(visible, carry[2 + channel], 0.0)
    out_ref[:, 3, :] = jnp.where(visible, carry[1], 0.0)


def render_layers(density_block, shown_rows, absorb, colour_slope, colour_offset, first_row, row_count,
                  block_rows=8):
    brick_rows, sample_count, pixels = density_block.shape
    first_block = first_row // block_rows
    params = jnp.concatenate([
        absorb.reshape(1), colour_slope, colour_offset,
        shown_rows.astype(jnp.float32).reshape(1),
    ])
    return pl.pallas_call(
        functools.partial(render_kernel, first_block),
        grid=(row_count // block_rows,),
        in_specs=[
            pl.BlockSpec(memory_space=pltpu.SMEM),
            pl.BlockSpec((block_rows * sample_count, pixels), lambda i: (i + first_block, 0)),
        ],
        out_specs=pl.BlockSpec((block_rows, 4, pixels), lambda i: (i, 0, 0)),
        out_shape=jax.ShapeDtypeStruct((row_count, 4, pixels), jnp.float32),
    )(params, density_block.reshape(brick_rows * sample_count, pixels))


def composite_rows(flat, starts, counts, brick_ids, stride, split, image_rows):
    slot_count = starts.shape[0]
    offset = image_rows[:, None] - starts[None, :]
    covered = (offset >= 0) & (offset < counts[None, :])
    depth_ids = brick_ids[None, :]
    slot_ids = jnp.arange(slot_count, dtype=jnp.int32)[None, :]
    back = jnp.max(jnp.where(covered, depth_ids, -1), axis=1)
    is_back = (depth_ids == back[:, None]) & covered
    is_front = (depth_ids == back[:, None] - 1) & covered
    back_off = jnp.sum(jnp.where(is_back, offset, 0), axis=1)
    front_off = jnp.sum(jnp.where(is_front, offset, 0), axis=1)
    back_slot = jnp.sum(jnp.where(is_back, slot_ids, 0), axis=1)
    front_slot = jnp.sum(jnp.where(is_front, slot_ids, 0), axis=1)
    has_front = jnp.any(is_front, axis=1)
    has_back = back >= 0
    back_off = back_off + (back_off >= split).astype(jnp.int32)
    front_off = front_off + (front_off >= split).astype(jnp.int32)
    back_idx = jnp.where(has_back, back_slot * stride + back_off, 0)
    front_idx = jnp.where(has_front, front_slot * stride + front_off, 0)
    back_rows = jnp.take(flat, back_idx, axis=0, mode="clip")
    front_rows = jnp.take(flat, front_idx, axis=0, mode="clip")
    back_rows = jnp.where(has_back[:, None, None], back_rows, 0.0)
    front_rows = jnp.where(has_front[:, None, None], front_rows, 0.0)
    front_depth = front_rows[:, 3:4, :]
    colours = front_rows[:, :3, :] + jnp.exp(-front_depth) * back_rows[:, :3, :]
    opacity = 1.0 - jnp.exp(-(front_depth + back_rows[:, 3:4, :]))
    return jnp.concatenate([colours, opacity], axis=1)


def ring_order(count):
    return list(range(0, count, 2)) + list(range(count - 1 - count % 2, 0, -2))


def ring_gather(own, count):
    order = ring_order(count)
    forward = [(order[k], order[(k + 1) % count]) for k in range(count)]
    backward = [(b, a) for a, b in forward]
    slots = [own]
    ahead = own
    behind = own
    for step in range(1, count // 2 + 1):
        ahead = lax.ppermute(ahead, "depth", forward)
        slots.append(ahead)
        if 2 * step < count:
            behind = lax.ppermute(behind, "depth", backward)
            slots.append(behind)
    return slots


def on_device(density, foot_start, foot_rows, extinction, colour_slope, colour_offset, tile_source):
    depth_count = lax.axis_size("depth")
    screen_count = lax.axis_size("screen")
    depth_index = lax.axis_index("depth")
    screen_index = lax.axis_index("screen")
    image_total = tile_source.shape[0]
    half_rows = image_total // screen_count
    owner_rows = image_total // (depth_count * screen_count)
    start = foot_start[0, 0]
    shown = foot_rows[0, 0]
    brick_rows, pixels = density.shape[2], density.shape[4]
    channels = 4
    split = brick_rows // 2
    lane = lax.broadcasted_iota(jnp.int32, (1, channels, pixels), 2)
    meta = jnp.where(lane == 0, start, jnp.where(lane == 1, shown, jnp.where(lane == 2, depth_index, 0)))
    stride = brick_rows + 1
    front_half = render_layers(density[0, 0], shown, extinction[0], colour_slope, colour_offset, 0, split)
    front_slots = ring_gather(jnp.concatenate([front_half, meta.astype(jnp.float32)], axis=0), depth_count)
    back_half = render_layers(density[0, 0], shown, extinction[0], colour_slope, colour_offset, split,
                              brick_rows - split)
    back_slots = ring_gather(back_half, depth_count)
    flat = jnp.concatenate([part for pair in zip(front_slots, back_slots) for part in pair], axis=0)
    meta_rows = flat.reshape(depth_count, stride, channels, pixels)[:, split, 0, :3]
    starts = meta_rows[:, 0].astype(jnp.int32)
    counts = meta_rows[:, 1].astype(jnp.int32)
    brick_ids = meta_rows[:, 2].astype(jnp.int32)
    self_owner = depth_index * screen_count + screen_index
    partner_owner = depth_index * screen_count + (1 - screen_index)
    wanted_self = lax.dynamic_slice_in_dim(tile_source, self_owner * owner_rows, owner_rows)
    wanted_partner = lax.dynamic_slice_in_dim(tile_source, partner_owner * owner_rows, owner_rows)
    wanted = jnp.concatenate([wanted_self, wanted_partner])
    rows = composite_rows(flat, starts, counts, brick_ids, stride, split, wanted % half_rows)
    mine = rows[:owner_rows]
    for_partner = rows[owner_rows:]
    received = lax.ppermute(for_partner, "screen", [(0, 1), (1, 0)])
    in_my_half = (wanted_self // half_rows) == screen_index
    return jnp.where(in_my_half[:, None, None], mine, received)


def solution(mesh):
    return jax.shard_map(
        on_device,
        mesh=mesh,
        in_specs=(
            P(("runs", "depth"), "screen", None, None, None),
            P(("runs", "depth"), "screen"),
            P(("runs", "depth"), "screen"),
            P("runs"),
            P(),
            P(),
            P("runs"),
        ),
        out_specs=P(("runs", "depth", "screen"), None, None),
        check_vma=False,
    )
```

```python
import jax
import jax.numpy as jnp
from jax import lax
from jax.sharding import PartitionSpec as P
from jax.experimental import pallas as pl
from jax.experimental.pallas import tpu as pltpu

BLK = 256


def render_kernel(params_ref, density_ref, out_ref):
    block_rows = out_ref.shape[0]
    pixels = out_ref.shape[1] // 4
    sample_count = density_ref.shape[0] // block_rows
    absorb = params_ref[0]
    slopes = [params_ref[1 + channel] for channel in range(3)]
    offsets = [params_ref[4 + channel] for channel in range(3)]
    shown = params_ref[7]

    def one_step(step, carry):
        transmit, depth_sum = carry[0], carry[1]
        values = density_ref[pl.ds(step, block_rows, stride=sample_count), :]
        optical = absorb * jax.nn.softplus(values) / sample_count
        passed = jnp.exp(-optical)
        weight = transmit * (1.0 - passed)
        colours = tuple(
            carry[2 + channel] + weight * jax.nn.sigmoid(slopes[channel] * values + offsets[channel])
            for channel in range(3)
        )
        return (transmit * passed, depth_sum + optical) + colours

    zeros = jnp.zeros((block_rows, pixels), jnp.float32)
    carry = (jnp.ones((block_rows, pixels), jnp.float32), zeros, zeros, zeros, zeros)
    carry = lax.fori_loop(0, sample_count, one_step, carry, unroll=8)
    row_ids = pl.program_id(0) * block_rows + lax.broadcasted_iota(jnp.int32, (block_rows, pixels), 0)
    visible = row_ids.astype(jnp.float32) < shown
    for channel in range(3):
        out_ref[:, channel * pixels:(channel + 1) * pixels] = jnp.where(visible, carry[2 + channel], 0.0)
    out_ref[:, 3 * pixels:] = jnp.where(visible, carry[1], 0.0)


def render_layers(density_block, shown_rows, absorb, colour_slope, colour_offset, block_rows=8):
    brick_rows, sample_count, pixels = density_block.shape
    params = jnp.concatenate([
        absorb.reshape(1), colour_slope, colour_offset,
        shown_rows.astype(jnp.float32).reshape(1),
    ])
    return pl.pallas_call(
        render_kernel,
        grid=(brick_rows // block_rows,),
        in_specs=[
            pl.BlockSpec(memory_space=pltpu.SMEM),
            pl.BlockSpec((block_rows * sample_count, pixels), lambda i: (i, 0)),
        ],
        out_specs=pl.BlockSpec((block_rows, 4 * pixels), lambda i: (i, 0)),
        out_shape=jax.ShapeDtypeStruct((brick_rows, 4 * pixels), jnp.float32),
    )(params, density_block.reshape(brick_rows * sample_count, pixels))


def composite_rows(flat, starts, counts, brick_ids, stride, image_rows):
    slot_count = starts.shape[0]
    pixels = flat.shape[1] // 4
    zero_row = flat.shape[0] - 1
    offset = image_rows[:, None] - starts[None, :]
    covered = (offset >= 0) & (offset < counts[None, :])
    depth_ids = brick_ids[None, :]
    slot_ids = jnp.arange(slot_count, dtype=jnp.int32)[None, :]
    back = jnp.max(jnp.where(covered, depth_ids, -1), axis=1)
    is_back = (depth_ids == back[:, None]) & covered
    is_front = (depth_ids == back[:, None] - 1) & covered
    back_idx = jnp.sum(jnp.where(is_back, slot_ids * stride + offset, 0), axis=1)
    front_idx = jnp.sum(jnp.where(is_front, slot_ids * stride + offset, 0), axis=1)
    back_idx = jnp.where(back >= 0, back_idx, zero_row)
    front_idx = jnp.where(jnp.any(is_front, axis=1), front_idx, zero_row)
    back_rows = jnp.take(flat, back_idx, axis=0, mode="clip")
    front_rows = jnp.take(flat, front_idx, axis=0, mode="clip")
    front_depth = front_rows[:, 3 * pixels:]
    through = jnp.exp(-front_depth)
    colours = front_rows[:, :3 * pixels] + jnp.concatenate([through] * 3, axis=1) * back_rows[:, :3 * pixels]
    opacity = 1.0 - jnp.exp(-(front_depth + back_rows[:, 3 * pixels:]))
    return jnp.concatenate([colours, opacity], axis=1)


def ring_order(count):
    return list(range(0, count, 2)) + list(range(count - 1 - count % 2, 0, -2))


def ring_gather(own, count):
    order = ring_order(count)
    forward = [(order[k], order[(k + 1) % count]) for k in range(count)]
    backward = [(b, a) for a, b in forward]
    slots = [own]
    ahead = own
    behind = own
    for step in range(1, count // 2 + 1):
        ahead = lax.ppermute(ahead, "depth", forward)
        slots.append(ahead)
        if 2 * step < count:
            behind = lax.ppermute(behind, "depth", backward)
            slots.append(behind)
    return slots


def on_device(density, foot_start, foot_rows, extinction, colour_slope, colour_offset, tile_source):
    depth_count = lax.axis_size("depth")
    screen_count = lax.axis_size("screen")
    depth_index = lax.axis_index("depth")
    screen_index = lax.axis_index("screen")
    image_total = tile_source.shape[0]
    half_rows = image_total // screen_count
    owner_rows = image_total // (depth_count * screen_count)
    start = foot_start[0, 0]
    shown = foot_rows[0, 0]
    layers = render_layers(density[0, 0], shown, extinction[0], colour_slope, colour_offset)
    brick_rows, width = layers.shape
    lane = lax.broadcasted_iota(jnp.int32, (1, width), 1)
    meta = jnp.where(lane == 0, start, jnp.where(lane == 1, shown, jnp.where(lane == 2, depth_index, 0)))
    stride = brick_rows + 1
    own = jnp.concatenate([layers, meta.astype(jnp.float32)], axis=0)
    slots = ring_gather(own, depth_count)
    flat = jnp.concatenate(slots + [jnp.zeros((1, width), jnp.float32)], axis=0)
    meta_rows = jnp.concatenate([slot[brick_rows:, :3] for slot in slots], axis=0)
    starts = meta_rows[:, 0].astype(jnp.int32)
    counts = meta_rows[:, 1].astype(jnp.int32)
    brick_ids = meta_rows[:, 2].astype(jnp.int32)
    self_owner = depth_index * screen_count + screen_index
    partner_owner = depth_index * screen_count + (1 - screen_index)
    wanted_self = lax.dynamic_slice_in_dim(tile_source, self_owner * owner_rows, owner_rows)
    wanted_partner = lax.dynamic_slice_in_dim(tile_source, partner_owner * owner_rows, owner_rows)
    wanted = jnp.concatenate([wanted_self, wanted_partner])
    rows = composite_rows(flat, starts, counts, brick_ids, stride, wanted % half_rows)
    mine = rows[:owner_rows]
    for_partner = rows[owner_rows:]
    received = lax.ppermute(for_partner, "screen", [(0, 1), (1, 0)])
    in_my_half = (wanted_self // half_rows) == screen_index
    frame = jnp.where(in_my_half[:, None], mine, received)
    return frame.reshape(owner_rows, 4, width // 4)


def solution(mesh):
    return jax.shard_map(
        on_device,
        mesh=mesh,
        in_specs=(
            P(("runs", "depth"), "screen", None, None, None),
            P(("runs", "depth"), "screen"),
            P(("runs", "depth"), "screen"),
            P("runs"),
            P(),
            P(),
            P("runs"),
        ),
        out_specs=P(("runs", "depth", "screen"), None, None),
        check_vma=False,
    )
```

```python
import jax
import jax.numpy as jnp
from jax import lax
from jax.sharding import PartitionSpec as P
from jax.experimental import pallas as pl
from jax.experimental.pallas import tpu as pltpu

BLK = 256


def render_kernel(absorb_ref, slope_ref, offset_ref, shown_ref, density_ref, out_ref):
    block_rows = out_ref.shape[0]
    pixels = out_ref.shape[1] // 4
    sample_count = density_ref.shape[0] // block_rows
    absorb = absorb_ref[0]
    slopes = [slope_ref[channel] for channel in range(3)]
    offsets = [offset_ref[channel] for channel in range(3)]
    shown = shown_ref[0, 0]

    def one_step(step, carry):
        transmit, depth_sum = carry[0], carry[1]
        values = density_ref[pl.ds(step, block_rows, stride=sample_count), :]
        optical = absorb * jax.nn.softplus(values) / sample_count
        passed = jnp.exp(-optical)
        weight = transmit * (1.0 - passed)
        colours = tuple(
            carry[2 + channel] + weight * jax.nn.sigmoid(slopes[channel] * values + offsets[channel])
            for channel in range(3)
        )
        return (transmit * passed, depth_sum + optical) + colours

    zeros = jnp.zeros((block_rows, pixels), jnp.float32)
    carry = (jnp.ones((block_rows, pixels), jnp.float32), zeros, zeros, zeros, zeros)
    carry = lax.fori_loop(0, sample_count, one_step, carry, unroll=8)
    row_ids = pl.program_id(0) * block_rows + lax.broadcasted_iota(jnp.int32, (block_rows, pixels), 0)
    visible = row_ids < shown
    for channel in range(3):
        out_ref[:, channel * pixels:(channel + 1) * pixels] = jnp.where(visible, carry[2 + channel], 0.0)
    out_ref[:, 3 * pixels:] = jnp.where(visible, carry[1], 0.0)


def render_layers(density_block, shown_rows, absorb, colour_slope, colour_offset, block_rows=8):
    brick_rows, sample_count, pixels = density_block.shape
    return pl.pallas_call(
        render_kernel,
        grid=(brick_rows // block_rows,),
        in_specs=[
            pl.BlockSpec(memory_space=pltpu.SMEM),
            pl.BlockSpec(memory_space=pltpu.SMEM),
            pl.BlockSpec(memory_space=pltpu.SMEM),
            pl.BlockSpec(memory_space=pltpu.SMEM),
            pl.BlockSpec((block_rows * sample_count, pixels), lambda i: (i, 0)),
        ],
        out_specs=pl.BlockSpec((block_rows, 4 * pixels), lambda i: (i, 0)),
        out_shape=jax.ShapeDtypeStruct((brick_rows, 4 * pixels), jnp.float32),
    )(absorb, colour_slope, colour_offset, shown_rows, density_block.reshape(brick_rows * sample_count, pixels))


def composite_rows(flat, starts, counts, brick_ids, stride, image_rows):
    slot_count = starts.shape[0]
    pixels = flat.shape[1] // 4
    zero_row = flat.shape[0] - 1
    offset = image_rows[:, None] - starts[None, :]
    covered = (offset >= 0) & (offset < counts[None, :])
    depth_ids = brick_ids[None, :]
    slot_ids = jnp.arange(slot_count, dtype=jnp.int32)[None, :]
    back = jnp.max(jnp.where(covered, depth_ids, -1), axis=1)
    is_back = (depth_ids == back[:, None]) & covered
    is_front = (depth_ids == back[:, None] - 1) & covered
    back_idx = jnp.sum(jnp.where(is_back, slot_ids * stride + offset, 0), axis=1)
    front_idx = jnp.sum(jnp.where(is_front, slot_ids * stride + offset, 0), axis=1)
    back_idx = jnp.where(back >= 0, back_idx, zero_row)
    front_idx = jnp.where(jnp.any(is_front, axis=1), front_idx, zero_row)
    back_rows = jnp.take(flat, back_idx, axis=0, mode="clip")
    front_rows = jnp.take(flat, front_idx, axis=0, mode="clip")
    front_depth = front_rows[:, 3 * pixels:]
    through = jnp.exp(-front_depth)
    colours = front_rows[:, :3 * pixels] + jnp.concatenate([through] * 3, axis=1) * back_rows[:, :3 * pixels]
    opacity = 1.0 - jnp.exp(-(front_depth + back_rows[:, 3 * pixels:]))
    return jnp.concatenate([colours, opacity], axis=1)


def ring_order(count):
    return list(range(0, count, 2)) + list(range(count - 1 - count % 2, 0, -2))


def ring_gather(own, count):
    order = ring_order(count)
    forward = [(order[k], order[(k + 1) % count]) for k in range(count)]
    backward = [(b, a) for a, b in forward]
    slots = [own]
    ahead = own
    behind = own
    for step in range(1, count // 2 + 1):
        ahead = lax.ppermute(ahead, "depth", forward)
        slots.append(ahead)
        if 2 * step < count:
            behind = lax.ppermute(behind, "depth", backward)
            slots.append(behind)
    return slots


def on_device(density, foot_start, foot_rows, extinction, colour_slope, colour_offset, tile_source):
    depth_count = lax.axis_size("depth")
    screen_count = lax.axis_size("screen")
    depth_index = lax.axis_index("depth")
    screen_index = lax.axis_index("screen")
    image_total = tile_source.shape[0]
    half_rows = image_total // screen_count
    owner_rows = image_total // (depth_count * screen_count)
    start = foot_start[0, 0]
    shown = foot_rows[0, 0]
    layers = render_layers(density[0, 0], foot_rows, extinction, colour_slope, colour_offset)
    brick_rows, width = layers.shape
    lane = lax.broadcasted_iota(jnp.int32, (1, width), 1)
    meta = jnp.where(lane == 0, start, jnp.where(lane == 1, shown, jnp.where(lane == 2, depth_index, 0)))
    stride = brick_rows + 1
    own = jnp.concatenate([layers, meta.astype(jnp.float32)], axis=0)
    slots = ring_gather(own, depth_count)
    flat = jnp.concatenate(slots + [jnp.zeros((1, width), jnp.float32)], axis=0)
    meta_rows = flat[:depth_count * stride].reshape(depth_count, stride, width)[:, brick_rows, :3]
    starts = meta_rows[:, 0].astype(jnp.int32)
    counts = meta_rows[:, 1].astype(jnp.int32)
    brick_ids = meta_rows[:, 2].astype(jnp.int32)
    self_owner = depth_index * screen_count + screen_index
    partner_owner = depth_index * screen_count + (1 - screen_index)
    wanted_self = lax.dynamic_slice_in_dim(tile_source, self_owner * owner_rows, owner_rows)
    wanted_partner = lax.dynamic_slice_in_dim(tile_source, partner_owner * owner_rows, owner_rows)
    wanted = jnp.concatenate([wanted_self, wanted_partner])
    rows = composite_rows(flat, starts, counts, brick_ids, stride, wanted % half_rows)
    mine = rows[:owner_rows]
    for_partner = rows[owner_rows:]
    received = lax.ppermute(for_partner, "screen", [(0, 1), (1, 0)])
    in_my_half = (wanted_self // half_rows) == screen_index
    frame = jnp.where(in_my_half[:, None], mine, received)
    return frame.reshape(owner_rows, 4, width // 4)


def solution(mesh):
    return jax.shard_map(
        on_device,
        mesh=mesh,
        in_specs=(
            P(("runs", "depth"), "screen", None, None, None),
            P(("runs", "depth"), "screen"),
            P(("runs", "depth"), "screen"),
            P("runs"),
            P(),
            P(),
            P("runs"),
        ),
        out_specs=P(("runs", "depth", "screen"), None, None),
        check_vma=False,
    )
```

```python
import jax
import jax.numpy as jnp
from jax import lax
from jax.sharding import PartitionSpec as P
from jax.experimental import pallas as pl
from jax.experimental.pallas import tpu as pltpu

BLK = 256


def render_kernel(absorb_ref, slope_ref, offset_ref, shown_ref, density_ref, out_ref):
    block_rows = out_ref.shape[0]
    pixels = out_ref.shape[2]
    sample_count = density_ref.shape[0] // block_rows
    absorb = absorb_ref[0]
    slopes = [slope_ref[channel] for channel in range(3)]
    offsets = [offset_ref[channel] for channel in range(3)]
    shown = shown_ref[0, 0]

    def one_step(step, carry):
        transmit, depth_sum = carry[0], carry[1]
        values = density_ref[pl.ds(step, block_rows, stride=sample_count), :]
        optical = absorb * jax.nn.softplus(values) / sample_count
        passed = jnp.exp(-optical)
        weight = transmit * (1.0 - passed)
        colours = tuple(
            carry[2 + channel] + weight * jax.nn.sigmoid(slopes[channel] * values + offsets[channel])
            for channel in range(3)
        )
        return (transmit * passed, depth_sum + optical) + colours

    zeros = jnp.zeros((block_rows, pixels), jnp.float32)
    carry = (jnp.ones((block_rows, pixels), jnp.float32), zeros, zeros, zeros, zeros)
    carry = lax.fori_loop(0, sample_count, one_step, carry, unroll=8)
    row_ids = pl.program_id(0) * block_rows + lax.broadcasted_iota(jnp.int32, (block_rows, pixels), 0)
    visible = row_ids < shown
    for channel in range(3):
        out_ref[:, channel, :] = jnp.where(visible, carry[2 + channel], 0.0)
    out_ref[:, 3, :] = jnp.where(visible, carry[1], 0.0)


def render_layers(density_block, shown_rows, absorb, colour_slope, colour_offset, block_rows=8):
    brick_rows, sample_count, pixels = density_block.shape
    return pl.pallas_call(
        render_kernel,
        grid=(brick_rows // block_rows,),
        in_specs=[
            pl.BlockSpec(memory_space=pltpu.SMEM),
            pl.BlockSpec(memory_space=pltpu.SMEM),
            pl.BlockSpec(memory_space=pltpu.SMEM),
            pl.BlockSpec(memory_space=pltpu.SMEM),
            pl.BlockSpec((block_rows * sample_count, pixels), lambda i: (i, 0)),
        ],
        out_specs=pl.BlockSpec((block_rows, 4, pixels), lambda i: (i, 0, 0)),
        out_shape=jax.ShapeDtypeStruct((brick_rows, 4, pixels), jnp.float32),
    )(absorb, colour_slope, colour_offset, shown_rows, density_block.reshape(brick_rows * sample_count, pixels))


def composite_rows(flat, starts, counts, brick_ids, stride, image_rows):
    slot_count = starts.shape[0]
    offset = image_rows[:, None] - starts[None, :]
    covered = (offset >= 0) & (offset < counts[None, :])
    depth_ids = brick_ids[None, :]
    slot_ids = jnp.arange(slot_count, dtype=jnp.int32)[None, :]
    back = jnp.max(jnp.where(covered, depth_ids, -1), axis=1)
    is_back = (depth_ids == back[:, None]) & covered
    is_front = (depth_ids == back[:, None] - 1) & covered
    back_off = jnp.sum(jnp.where(is_back, offset, 0), axis=1)
    front_off = jnp.sum(jnp.where(is_front, offset, 0), axis=1)
    back_slot = jnp.sum(jnp.where(is_back, slot_ids, 0), axis=1)
    front_slot = jnp.sum(jnp.where(is_front, slot_ids, 0), axis=1)
    has_front = jnp.any(is_front, axis=1)
    has_back = back >= 0
    zero_row = flat.shape[0] - 1
    back_idx = jnp.where(has_back, back_slot * stride + back_off, zero_row)
    front_idx = jnp.where(has_front, front_slot * stride + front_off, zero_row)
    back_rows = jnp.take(flat, back_idx, axis=0, mode="clip")
    front_rows = jnp.take(flat, front_idx, axis=0, mode="clip")
    front_depth = front_rows[:, 3:4, :]
    colours = front_rows[:, :3, :] + jnp.exp(-front_depth) * back_rows[:, :3, :]
    opacity = 1.0 - jnp.exp(-(front_depth + back_rows[:, 3:4, :]))
    return jnp.concatenate([colours, opacity], axis=1)


def ring_order(count):
    return list(range(0, count, 2)) + list(range(count - 1 - count % 2, 0, -2))


def ring_gather(own, count):
    order = ring_order(count)
    forward = [(order[k], order[(k + 1) % count]) for k in range(count)]
    backward = [(b, a) for a, b in forward]
    slots = [own]
    ahead = own
    behind = own
    for step in range(1, count // 2 + 1):
        ahead = lax.ppermute(ahead, "depth", forward)
        slots.append(ahead)
        if 2 * step < count:
            behind = lax.ppermute(behind, "depth", backward)
            slots.append(behind)
    return jnp.concatenate(slots + [jnp.zeros((1,) + own.shape[1:], own.dtype)], axis=0)


def on_device(density, foot_start, foot_rows, extinction, colour_slope, colour_offset, tile_source):
    depth_count = lax.axis_size("depth")
    screen_count = lax.axis_size("screen")
    depth_index = lax.axis_index("depth")
    screen_index = lax.axis_index("screen")
    image_total = tile_source.shape[0]
    half_rows = image_total // screen_count
    owner_rows = image_total // (depth_count * screen_count)
    start = foot_start[0, 0]
    shown = foot_rows[0, 0]
    layers = render_layers(density[0, 0], foot_rows, extinction, colour_slope, colour_offset)
    brick_rows, channels, pixels = layers.shape
    lane = lax.broadcasted_iota(jnp.int32, (1, channels, pixels), 2)
    meta = jnp.where(lane == 0, start, jnp.where(lane == 1, shown, jnp.where(lane == 2, depth_index, 0)))
    stride = brick_rows + 1
    own = jnp.concatenate([layers, meta.astype(jnp.float32)], axis=0)
    flat = ring_gather(own, depth_count)
    meta_rows = flat[:depth_count * stride].reshape(depth_count, stride, channels, pixels)[:, brick_rows, 0, :3]
    starts = meta_rows[:, 0].astype(jnp.int32)
    counts = meta_rows[:, 1].astype(jnp.int32)
    brick_ids = meta_rows[:, 2].astype(jnp.int32)
    self_owner = depth_index * screen_count + screen_index
    partner_owner = depth_index * screen_count + (1 - screen_index)
    wanted_self = lax.dynamic_slice_in_dim(tile_source, self_owner * owner_rows, owner_rows)
    wanted_partner = lax.dynamic_slice_in_dim(tile_source, partner_owner * owner_rows, owner_rows)
    wanted = jnp.concatenate([wanted_self, wanted_partner])
    rows = composite_rows(flat, starts, counts, brick_ids, stride, wanted % half_rows)
    mine = rows[:owner_rows]
    for_partner = rows[owner_rows:]
    received = lax.ppermute(for_partner, "screen", [(0, 1), (1, 0)])
    in_my_half = (wanted_self // half_rows) == screen_index
    return jnp.where(in_my_half[:, None, None], mine, received)


def solution(mesh):
    return jax.shard_map(
        on_device,
        mesh=mesh,
        in_specs=(
            P(("runs", "depth"), "screen", None, None, None),
            P(("runs", "depth"), "screen"),
            P(("runs", "depth"), "screen"),
            P("runs"),
            P(),
            P(),
            P("runs"),
        ),
        out_specs=P(("runs", "depth", "screen"), None, None),
        check_vma=False,
    )
```

```python
import jax
import jax.numpy as jnp
from jax import lax
from jax.sharding import PartitionSpec as P
from jax.experimental import pallas as pl
from jax.experimental.pallas import tpu as pltpu

BLK = 256


def render_kernel(absorb_ref, slope_ref, offset_ref, shown_ref, density_ref, out_ref):
    block_rows = out_ref.shape[0]
    pixels = out_ref.shape[2]
    sample_count = density_ref.shape[0] // block_rows
    absorb = absorb_ref[0]
    slopes = [slope_ref[channel] for channel in range(3)]
    offsets = [offset_ref[channel] for channel in range(3)]
    shown = shown_ref[0, 0]

    def one_step(step, carry):
        transmit, depth_sum = carry[0], carry[1]
        values = density_ref[pl.ds(step, block_rows, stride=sample_count), :]
        optical = absorb * jnp.log1p(jnp.exp(values)) / sample_count
        passed = jnp.exp(-optical)
        weight = transmit * (1.0 - passed)
        colours = tuple(
            carry[2 + channel] + weight * (0.5 * jnp.tanh(0.5 * (slopes[channel] * values + offsets[channel])) + 0.5)
            for channel in range(3)
        )
        return (transmit * passed, depth_sum + optical) + colours

    zeros = jnp.zeros((block_rows, pixels), jnp.float32)
    carry = (jnp.ones((block_rows, pixels), jnp.float32), zeros, zeros, zeros, zeros)
    carry = lax.fori_loop(0, sample_count, one_step, carry, unroll=8)
    row_ids = pl.program_id(0) * block_rows + lax.broadcasted_iota(jnp.int32, (block_rows, pixels), 0)
    visible = row_ids < shown
    for channel in range(3):
        out_ref[:, channel, :] = jnp.where(visible, carry[2 + channel], 0.0)
    out_ref[:, 3, :] = jnp.where(visible, carry[1], 0.0)


def render_layers(density_block, shown_rows, absorb, colour_slope, colour_offset, block_rows=8):
    brick_rows, sample_count, pixels = density_block.shape
    return pl.pallas_call(
        render_kernel,
        grid=(brick_rows // block_rows,),
        in_specs=[
            pl.BlockSpec(memory_space=pltpu.SMEM),
            pl.BlockSpec(memory_space=pltpu.SMEM),
            pl.BlockSpec(memory_space=pltpu.SMEM),
            pl.BlockSpec(memory_space=pltpu.SMEM),
            pl.BlockSpec((block_rows * sample_count, pixels), lambda i: (i, 0)),
        ],
        out_specs=pl.BlockSpec((block_rows, 4, pixels), lambda i: (i, 0, 0)),
        out_shape=jax.ShapeDtypeStruct((brick_rows, 4, pixels), jnp.float32),
    )(absorb, colour_slope, colour_offset, shown_rows, density_block.reshape(brick_rows * sample_count, pixels))


def composite_rows(flat, starts, counts, brick_ids, stride, image_rows):
    slot_count = starts.shape[0]
    offset = image_rows[:, None] - starts[None, :]
    covered = (offset >= 0) & (offset < counts[None, :])
    depth_ids = brick_ids[None, :]
    slot_ids = jnp.arange(slot_count, dtype=jnp.int32)[None, :]
    back = jnp.max(jnp.where(covered, depth_ids, -1), axis=1)
    is_back = (depth_ids == back[:, None]) & covered
    is_front = (depth_ids == back[:, None] - 1) & covered
    back_off = jnp.sum(jnp.where(is_back, offset, 0), axis=1)
    front_off = jnp.sum(jnp.where(is_front, offset, 0), axis=1)
    back_slot = jnp.sum(jnp.where(is_back, slot_ids, 0), axis=1)
    front_slot = jnp.sum(jnp.where(is_front, slot_ids, 0), axis=1)
    has_front = jnp.any(is_front, axis=1)
    has_back = back >= 0
    zero_row = stride - 1
    back_idx = jnp.where(has_back, back_slot * stride + back_off, zero_row)
    front_idx = jnp.where(has_front, front_slot * stride + front_off, zero_row)
    back_rows = jnp.take(flat, back_idx, axis=0, mode="clip")
    front_rows = jnp.take(flat, front_idx, axis=0, mode="clip")
    front_depth = front_rows[:, 3:4, :]
    colours = front_rows[:, :3, :] + jnp.exp(-front_depth) * back_rows[:, :3, :]
    opacity = 1.0 - jnp.exp(-(front_depth + back_rows[:, 3:4, :]))
    return jnp.concatenate([colours, opacity], axis=1)


def ring_order(count):
    return list(range(0, count, 2)) + list(range(count - 1 - count % 2, 0, -2))


def ring_gather(own, count):
    order = ring_order(count)
    forward = [(order[k], order[(k + 1) % count]) for k in range(count)]
    backward = [(b, a) for a, b in forward]
    slots = [own]
    ahead = own
    behind = own
    for step in range(1, count // 2 + 1):
        ahead = lax.ppermute(ahead, "depth", forward)
        slots.append(ahead)
        if 2 * step < count:
            behind = lax.ppermute(behind, "depth", backward)
            slots.append(behind)
    return jnp.concatenate(slots, axis=0)


def on_device(density, foot_start, foot_rows, extinction, colour_slope, colour_offset, tile_source):
    depth_count = lax.axis_size("depth")
    screen_count = lax.axis_size("screen")
    depth_index = lax.axis_index("depth")
    screen_index = lax.axis_index("screen")
    image_total = tile_source.shape[0]
    half_rows = image_total // screen_count
    owner_rows = image_total // (depth_count * screen_count)
    start = foot_start[0, 0]
    shown = foot_rows[0, 0]
    layers = render_layers(density[0, 0], foot_rows, extinction, colour_slope, colour_offset)
    brick_rows, channels, pixels = layers.shape
    lane = lax.broadcasted_iota(jnp.int32, (1, channels, pixels), 2)
    meta = jnp.where(lane == 0, start, jnp.where(lane == 1, shown, jnp.where(lane == 2, depth_index, 0)))
    stride = brick_rows + 2
    own = jnp.concatenate([layers, meta.astype(jnp.float32), jnp.zeros_like(meta, jnp.float32)], axis=0)
    flat = ring_gather(own, depth_count)
    meta_rows = flat.reshape(depth_count, stride, channels, pixels)[:, brick_rows, 0, :3]
    starts = meta_rows[:, 0].astype(jnp.int32)
    counts = meta_rows[:, 1].astype(jnp.int32)
    brick_ids = meta_rows[:, 2].astype(jnp.int32)
    self_owner = depth_index * screen_count + screen_index
    partner_owner = depth_index * screen_count + (1 - screen_index)
    wanted_self = lax.dynamic_slice_in_dim(tile_source, self_owner * owner_rows, owner_rows)
    wanted_partner = lax.dynamic_slice_in_dim(tile_source, partner_owner * owner_rows, owner_rows)
    wanted = jnp.concatenate([wanted_self, wanted_partner])
    rows = composite_rows(flat, starts, counts, brick_ids, stride, wanted % half_rows)
    mine = rows[:owner_rows]
    for_partner = rows[owner_rows:]
    received = lax.ppermute(for_partner, "screen", [(0, 1), (1, 0)])
    in_my_half = (wanted_self // half_rows) == screen_index
    return jnp.where(in_my_half[:, None, None], mine, received)


def solution(mesh):
    return jax.shard_map(
        on_device,
        mesh=mesh,
        in_specs=(
            P(("runs", "depth"), "screen", None, None, None),
            P(("runs", "depth"), "screen"),
            P(("runs", "depth"), "screen"),
            P("runs"),
            P(),
            P(),
            P("runs"),
        ),
        out_specs=P(("runs", "depth", "screen"), None, None),
        check_vma=False,
    )
```

```python
import jax
import jax.numpy as jnp
from jax import lax
from jax.sharding import PartitionSpec as P
from jax.experimental import pallas as pl
from jax.experimental.pallas import tpu as pltpu

BLK = 256


def render_kernel(absorb_ref, slope_ref, offset_ref, shown_ref, density_ref, out_ref):
    block_rows = out_ref.shape[0]
    pixels = out_ref.shape[2]
    sample_count = density_ref.shape[0] // block_rows
    scale = absorb_ref[0] / sample_count
    half_slopes = [0.5 * slope_ref[channel] for channel in range(3)]
    half_offsets = [0.5 * offset_ref[channel] for channel in range(3)]
    shown = shown_ref[0, 0]

    def one_step(step, carry):
        half_transmit, depth_sum, weight_sum = carry[0], carry[1], carry[2]
        values = density_ref[pl.ds(step, block_rows, stride=sample_count), :]
        optical = scale * jnp.log1p(jnp.exp(values))
        passed = jnp.exp(-optical)
        half_weight = half_transmit * (1.0 - passed)
        colours = tuple(
            carry[3 + channel] + half_weight * jnp.tanh(half_slopes[channel] * values + half_offsets[channel])
            for channel in range(3)
        )
        return (half_transmit * passed, depth_sum + optical, weight_sum + half_weight) + colours

    zeros = jnp.zeros((block_rows, pixels), jnp.float32)
    carry = (jnp.full((block_rows, pixels), 0.5, jnp.float32), zeros, zeros, zeros, zeros, zeros)
    carry = lax.fori_loop(0, sample_count, one_step, carry, unroll=8)
    row_ids = pl.program_id(0) * block_rows + lax.broadcasted_iota(jnp.int32, (block_rows, pixels), 0)
    visible = row_ids < shown
    for channel in range(3):
        out_ref[:, channel, :] = jnp.where(visible, carry[2] + carry[3 + channel], 0.0)
    out_ref[:, 3, :] = jnp.where(visible, carry[1], 0.0)


def render_layers(density_block, shown_rows, absorb, colour_slope, colour_offset, block_rows=8):
    brick_rows, sample_count, pixels = density_block.shape
    return pl.pallas_call(
        render_kernel,
        grid=(brick_rows // block_rows,),
        in_specs=[
            pl.BlockSpec(memory_space=pltpu.SMEM),
            pl.BlockSpec(memory_space=pltpu.SMEM),
            pl.BlockSpec(memory_space=pltpu.SMEM),
            pl.BlockSpec(memory_space=pltpu.SMEM),
            pl.BlockSpec((block_rows * sample_count, pixels), lambda i: (i, 0)),
        ],
        out_specs=pl.BlockSpec((block_rows, 4, pixels), lambda i: (i, 0, 0)),
        out_shape=jax.ShapeDtypeStruct((brick_rows, 4, pixels), jnp.float32),
    )(absorb, colour_slope, colour_offset, shown_rows, density_block.reshape(brick_rows * sample_count, pixels))


def composite_rows(flat, starts, counts, brick_ids, stride, image_rows):
    slot_count = starts.shape[0]
    offset = image_rows[:, None] - starts[None, :]
    covered = (offset >= 0) & (offset < counts[None, :])
    depth_ids = brick_ids[None, :]
    slot_ids = jnp.arange(slot_count, dtype=jnp.int32)[None, :]
    back = jnp.max(jnp.where(covered, depth_ids, -1), axis=1)
    is_back = (depth_ids == back[:, None]) & covered
    is_front = (depth_ids == back[:, None] - 1) & covered
    back_off = jnp.sum(jnp.where(is_back, offset, 0), axis=1)
    front_off = jnp.sum(jnp.where(is_front, offset, 0), axis=1)
    back_slot = jnp.sum(jnp.where(is_back, slot_ids, 0), axis=1)
    front_slot = jnp.sum(jnp.where(is_front, slot_ids, 0), axis=1)
    has_front = jnp.any(is_front, axis=1)
    has_back = back >= 0
    zero_row = stride - 1
    back_idx = jnp.where(has_back, back_slot * stride + back_off, zero_row)
    front_idx = jnp.where(has_front, front_slot * stride + front_off, zero_row)
    back_rows = jnp.take(flat, back_idx, axis=0, mode="clip")
    front_rows = jnp.take(flat, front_idx, axis=0, mode="clip")
    front_depth = front_rows[:, 3:4, :]
    colours = front_rows[:, :3, :] + jnp.exp(-front_depth) * back_rows[:, :3, :]
    opacity = 1.0 - jnp.exp(-(front_depth + back_rows[:, 3:4, :]))
    return jnp.concatenate([colours, opacity], axis=1)


def ring_order(count):
    return list(range(0, count, 2)) + list(range(count - 1 - count % 2, 0, -2))


def ring_gather(own, count):
    order = ring_order(count)
    forward = [(order[k], order[(k + 1) % count]) for k in range(count)]
    backward = [(b, a) for a, b in forward]
    slots = [own]
    ahead = own
    behind = own
    for step in range(1, count // 2 + 1):
        ahead = lax.ppermute(ahead, "depth", forward)
        slots.append(ahead)
        if 2 * step < count:
            behind = lax.ppermute(behind, "depth", backward)
            slots.append(behind)
    return jnp.concatenate(slots, axis=0)


def on_device(density, foot_start, foot_rows, extinction, colour_slope, colour_offset, tile_source):
    depth_count = lax.axis_size("depth")
    screen_count = lax.axis_size("screen")
    depth_index = lax.axis_index("depth")
    screen_index = lax.axis_index("screen")
    image_total = tile_source.shape[0]
    half_rows = image_total // screen_count
    owner_rows = image_total // (depth_count * screen_count)
    start = foot_start[0, 0]
    shown = foot_rows[0, 0]
    layers = render_layers(density[0, 0], foot_rows, extinction, colour_slope, colour_offset)
    brick_rows, channels, pixels = layers.shape
    lane = lax.broadcasted_iota(jnp.int32, (1, channels, pixels), 2)
    meta = jnp.where(lane == 0, start, jnp.where(lane == 1, shown, jnp.where(lane == 2, depth_index, 0)))
    stride = brick_rows + 2
    own = jnp.concatenate([layers, meta.astype(jnp.float32), jnp.zeros_like(meta, jnp.float32)], axis=0)
    flat = ring_gather(own, depth_count)
    meta_rows = flat.reshape(depth_count, stride, channels, pixels)[:, brick_rows, 0, :3]
    starts = meta_rows[:, 0].astype(jnp.int32)
    counts = meta_rows[:, 1].astype(jnp.int32)
    brick_ids = meta_rows[:, 2].astype(jnp.int32)
    self_owner = depth_index * screen_count + screen_index
    partner_owner = depth_index * screen_count + (1 - screen_index)
    wanted_self = lax.dynamic_slice_in_dim(tile_source, self_owner * owner_rows, owner_rows)
    wanted_partner = lax.dynamic_slice_in_dim(tile_source, partner_owner * owner_rows, owner_rows)
    wanted = jnp.concatenate([wanted_self, wanted_partner])
    rows = composite_rows(flat, starts, counts, brick_ids, stride, wanted % half_rows)
    mine = rows[:owner_rows]
    for_partner = rows[owner_rows:]
    received = lax.ppermute(for_partner, "screen", [(0, 1), (1, 0)])
    in_my_half = (wanted_self // half_rows) == screen_index
    return jnp.where(in_my_half[:, None, None], mine, received)


def solution(mesh):
    return jax.shard_map(
        on_device,
        mesh=mesh,
        in_specs=(
            P(("runs", "depth"), "screen", None, None, None),
            P(("runs", "depth"), "screen"),
            P(("runs", "depth"), "screen"),
            P("runs"),
            P(),
            P(),
            P("runs"),
        ),
        out_specs=P(("runs", "depth", "screen"), None, None),
        check_vma=False,
    )
```

```python
import jax
import jax.numpy as jnp
from jax import lax
from jax.sharding import PartitionSpec as P
from jax.experimental import pallas as pl
from jax.experimental.pallas import tpu as pltpu

BLK = 256


def render_kernel(absorb_ref, slope_ref, offset_ref, shown_ref, density_ref, out_ref):
    block_rows = out_ref.shape[0]
    pixels = out_ref.shape[2]
    sample_count = density_ref.shape[0] // block_rows
    scale = absorb_ref[0] / sample_count
    half_slopes = [0.5 * slope_ref[channel] for channel in range(3)]
    half_offsets = [0.5 * offset_ref[channel] for channel in range(3)]
    shown = shown_ref[0, 0]

    def one_step(step, carry):
        half_transmit, depth_sum, weight_sum = carry[0], carry[1], carry[2]
        values = density_ref[pl.ds(step, block_rows, stride=sample_count), :]
        optical = scale * jnp.log1p(jnp.exp(values))
        passed = jnp.exp(-optical)
        half_weight = half_transmit * (1.0 - passed)
        colours = tuple(
            carry[3 + channel] + half_weight * jnp.tanh(half_slopes[channel] * values + half_offsets[channel])
            for channel in range(3)
        )
        return (half_transmit * passed, depth_sum + optical, weight_sum + half_weight) + colours

    zeros = jnp.zeros((block_rows, pixels), jnp.float32)
    carry = (jnp.full((block_rows, pixels), 0.5, jnp.float32), zeros, zeros, zeros, zeros, zeros)
    carry = lax.fori_loop(0, sample_count, one_step, carry, unroll=16)
    row_ids = pl.program_id(0) * block_rows + lax.broadcasted_iota(jnp.int32, (block_rows, pixels), 0)
    visible = row_ids < shown
    for channel in range(3):
        out_ref[:, channel, :] = jnp.where(visible, carry[2] + carry[3 + channel], 0.0)
    out_ref[:, 3, :] = jnp.where(visible, carry[1], 0.0)


def render_layers(density_block, shown_rows, absorb, colour_slope, colour_offset, block_rows=16):
    brick_rows, sample_count, pixels = density_block.shape
    return pl.pallas_call(
        render_kernel,
        grid=(brick_rows // block_rows,),
        in_specs=[
            pl.BlockSpec(memory_space=pltpu.SMEM),
            pl.BlockSpec(memory_space=pltpu.SMEM),
            pl.BlockSpec(memory_space=pltpu.SMEM),
            pl.BlockSpec(memory_space=pltpu.SMEM),
            pl.BlockSpec((block_rows * sample_count, pixels), lambda i: (i, 0)),
        ],
        out_specs=pl.BlockSpec((block_rows, 4, pixels), lambda i: (i, 0, 0)),
        out_shape=jax.ShapeDtypeStruct((brick_rows, 4, pixels), jnp.float32),
    )(absorb, colour_slope, colour_offset, shown_rows, density_block.reshape(brick_rows * sample_count, pixels))


def composite_rows(flat, starts, counts, brick_ids, stride, image_rows):
    slot_count = starts.shape[0]
    offset = image_rows[:, None] - starts[None, :]
    covered = (offset >= 0) & (offset < counts[None, :])
    depth_ids = brick_ids[None, :]
    slot_ids = jnp.arange(slot_count, dtype=jnp.int32)[None, :]
    back = jnp.max(jnp.where(covered, depth_ids, -1), axis=1)
    is_back = (depth_ids == back[:, None]) & covered
    is_front = (depth_ids == back[:, None] - 1) & covered
    back_off = jnp.sum(jnp.where(is_back, offset, 0), axis=1)
    front_off = jnp.sum(jnp.where(is_front, offset, 0), axis=1)
    back_slot = jnp.sum(jnp.where(is_back, slot_ids, 0), axis=1)
    front_slot = jnp.sum(jnp.where(is_front, slot_ids, 0), axis=1)
    has_front = jnp.any(is_front, axis=1)
    has_back = back >= 0
    zero_row = stride - 1
    back_idx = jnp.where(has_back, back_slot * stride + back_off, zero_row)
    front_idx = jnp.where(has_front, front_slot * stride + front_off, zero_row)
    back_rows = jnp.take(flat, back_idx, axis=0, mode="clip")
    front_rows = jnp.take(flat, front_idx, axis=0, mode="clip")
    front_depth = front_rows[:, 3:4, :]
    colours = front_rows[:, :3, :] + jnp.exp(-front_depth) * back_rows[:, :3, :]
    opacity = 1.0 - jnp.exp(-(front_depth + back_rows[:, 3:4, :]))
    return jnp.concatenate([colours, opacity], axis=1)


def ring_order(count):
    return list(range(0, count, 2)) + list(range(count - 1 - count % 2, 0, -2))


def ring_gather(own, count):
    order = ring_order(count)
    forward = [(order[k], order[(k + 1) % count]) for k in range(count)]
    backward = [(b, a) for a, b in forward]
    slots = [own]
    ahead = own
    behind = own
    for step in range(1, count // 2 + 1):
        ahead = lax.ppermute(ahead, "depth", forward)
        slots.append(ahead)
        if 2 * step < count:
            behind = lax.ppermute(behind, "depth", backward)
            slots.append(behind)
    return jnp.concatenate(slots, axis=0)


def on_device(density, foot_start, foot_rows, extinction, colour_slope, colour_offset, tile_source):
    depth_count = lax.axis_size("depth")
    screen_count = lax.axis_size("screen")
    depth_index = lax.axis_index("depth")
    screen_index = lax.axis_index("screen")
    image_total = tile_source.shape[0]
    half_rows = image_total // screen_count
    owner_rows = image_total // (depth_count * screen_count)
    start = foot_start[0, 0]
    shown = foot_rows[0, 0]
    layers = render_layers(density[0, 0], foot_rows, extinction, colour_slope, colour_offset)
    brick_rows, channels, pixels = layers.shape
    lane = lax.broadcasted_iota(jnp.int32, (1, channels, pixels), 2)
    meta = jnp.where(lane == 0, start, jnp.where(lane == 1, shown, jnp.where(lane == 2, depth_index, 0)))
    stride = brick_rows + 2
    own = jnp.concatenate([layers, meta.astype(jnp.float32), jnp.zeros_like(meta, jnp.float32)], axis=0)
    flat = ring_gather(own, depth_count)
    meta_rows = flat.reshape(depth_count, stride, channels, pixels)[:, brick_rows, 0, :3]
    starts = meta_rows[:, 0].astype(jnp.int32)
    counts = meta_rows[:, 1].astype(jnp.int32)
    brick_ids = meta_rows[:, 2].astype(jnp.int32)
    self_owner = depth_index * screen_count + screen_index
    partner_owner = depth_index * screen_count + (1 - screen_index)
    wanted_self = lax.dynamic_slice_in_dim(tile_source, self_owner * owner_rows, owner_rows)
    wanted_partner = lax.dynamic_slice_in_dim(tile_source, partner_owner * owner_rows, owner_rows)
    wanted = jnp.concatenate([wanted_self, wanted_partner])
    rows = composite_rows(flat, starts, counts, brick_ids, stride, wanted % half_rows)
    mine = rows[:owner_rows]
    for_partner = rows[owner_rows:]
    received = lax.ppermute(for_partner, "screen", [(0, 1), (1, 0)])
    in_my_half = (wanted_self // half_rows) == screen_index
    return jnp.where(in_my_half[:, None, None], mine, received)


def solution(mesh):
    return jax.shard_map(
        on_device,
        mesh=mesh,
        in_specs=(
            P(("runs", "depth"), "screen", None, None, None),
            P(("runs", "depth"), "screen"),
            P(("runs", "depth"), "screen"),
            P("runs"),
            P(),
            P(),
            P("runs"),
        ),
        out_specs=P(("runs", "depth", "screen"), None, None),
        check_vma=False,
    )
```

```python
import jax
import jax.numpy as jnp
from jax import lax
from jax.sharding import PartitionSpec as P
from jax.experimental import pallas as pl
from jax.experimental.pallas import tpu as pltpu

BLK = 256


def render_kernel(absorb_ref, slope_ref, offset_ref, shown_ref, density_ref, out_ref):
    block_rows = out_ref.shape[0]
    pixels = out_ref.shape[2]
    sample_count = density_ref.shape[0] // block_rows
    scale = absorb_ref[0] / sample_count
    half_slopes = [0.5 * slope_ref[channel] for channel in range(3)]
    half_offsets = [0.5 * offset_ref[channel] for channel in range(3)]
    shown = shown_ref[0, 0]

    def one_step(step, carry):
        half_transmit, depth_sum, weight_sum = carry[0], carry[1], carry[2]
        values = density_ref[pl.ds(step, block_rows, stride=sample_count), :]
        optical = scale * jnp.log1p(jnp.exp(values))
        passed = jnp.exp(-optical)
        half_weight = half_transmit * (1.0 - passed)
        colours = tuple(
            carry[3 + channel] + half_weight * jnp.tanh(half_slopes[channel] * values + half_offsets[channel])
            for channel in range(3)
        )
        return (half_transmit * passed, depth_sum + optical, weight_sum + half_weight) + colours

    zeros = jnp.zeros((block_rows, pixels), jnp.float32)
    carry = (jnp.full((block_rows, pixels), 0.5, jnp.float32), zeros, zeros, zeros, zeros, zeros)
    carry = lax.fori_loop(0, sample_count, one_step, carry, unroll=16)
    row_ids = pl.program_id(0) * block_rows + lax.broadcasted_iota(jnp.int32, (block_rows, pixels), 0)
    visible = row_ids < shown
    for channel in range(3):
        out_ref[:, channel, :] = jnp.where(visible, carry[2] + carry[3 + channel], 0.0)
    out_ref[:, 3, :] = jnp.where(visible, carry[1], 0.0)


def render_layers(density_block, shown_rows, absorb, colour_slope, colour_offset, block_rows=16):
    brick_rows, sample_count, pixels = density_block.shape
    return pl.pallas_call(
        render_kernel,
        grid=(brick_rows // block_rows,),
        in_specs=[
            pl.BlockSpec(memory_space=pltpu.SMEM),
            pl.BlockSpec(memory_space=pltpu.SMEM),
            pl.BlockSpec(memory_space=pltpu.SMEM),
            pl.BlockSpec(memory_space=pltpu.SMEM),
            pl.BlockSpec((block_rows * sample_count, pixels), lambda i: (i, 0)),
        ],
        out_specs=pl.BlockSpec((block_rows, 4, pixels), lambda i: (i, 0, 0)),
        out_shape=jax.ShapeDtypeStruct((brick_rows, 4, pixels), jnp.float32),
    )(absorb, colour_slope, colour_offset, shown_rows, density_block.reshape(brick_rows * sample_count, pixels))


def composite_rows(flat, starts, counts, brick_ids, stride, image_rows):
    slot_count = starts.shape[0]
    offset = image_rows[:, None] - starts[None, :]
    covered = (offset >= 0) & (offset < counts[None, :])
    depth_ids = brick_ids[None, :]
    slot_ids = jnp.arange(slot_count, dtype=jnp.int32)[None, :]
    back = jnp.max(jnp.where(covered, depth_ids, -1), axis=1)
    is_back = (depth_ids == back[:, None]) & covered
    is_front = (depth_ids == back[:, None] - 1) & covered
    back_off = jnp.sum(jnp.where(is_back, offset, 0), axis=1)
    front_off = jnp.sum(jnp.where(is_front, offset, 0), axis=1)
    back_slot = jnp.sum(jnp.where(is_back, slot_ids, 0), axis=1)
    front_slot = jnp.sum(jnp.where(is_front, slot_ids, 0), axis=1)
    has_front = jnp.any(is_front, axis=1)
    has_back = back >= 0
    zero_row = stride - 1
    back_idx = jnp.where(has_back, back_slot * stride + back_off, zero_row)
    front_idx = jnp.where(has_front, front_slot * stride + front_off, zero_row)
    return back_idx, front_idx


def blend_kernel(back_idx_ref, front_idx_ref, flat_ref, out_ref):
    def one_row(row, carry):
        back = flat_ref[back_idx_ref[row]]
        front = flat_ref[front_idx_ref[row]]
        front_depth = front[3:4, :]
        out_ref[row, 0:3, :] = front[0:3, :] + jnp.exp(-front_depth) * back[0:3, :]
        out_ref[row, 3:4, :] = 1.0 - jnp.exp(-(front_depth + back[3:4, :]))
        return carry

    lax.fori_loop(0, out_ref.shape[0], one_row, 0, unroll=8)


def blend_rows(flat, back_idx, front_idx):
    rows = back_idx.shape[0]
    return pl.pallas_call(
        blend_kernel,
        grid_spec=pltpu.PrefetchScalarGridSpec(
            num_scalar_prefetch=2,
            grid=(1,),
            in_specs=[pl.BlockSpec(flat.shape, lambda i, *_: (0, 0, 0))],
            out_specs=pl.BlockSpec((rows,) + flat.shape[1:], lambda i, *_: (0, 0, 0)),
        ),
        out_shape=jax.ShapeDtypeStruct((rows,) + flat.shape[1:], flat.dtype),
    )(back_idx, front_idx, flat)


def ring_order(count):
    return list(range(0, count, 2)) + list(range(count - 1 - count % 2, 0, -2))


def ring_gather(own, count):
    order = ring_order(count)
    forward = [(order[k], order[(k + 1) % count]) for k in range(count)]
    backward = [(b, a) for a, b in forward]
    slots = [own]
    ahead = own
    behind = own
    for step in range(1, count // 2 + 1):
        ahead = lax.ppermute(ahead, "depth", forward)
        slots.append(ahead)
        if 2 * step < count:
            behind = lax.ppermute(behind, "depth", backward)
            slots.append(behind)
    return jnp.concatenate(slots, axis=0)


def on_device(density, foot_start, foot_rows, extinction, colour_slope, colour_offset, tile_source):
    depth_count = lax.axis_size("depth")
    screen_count = lax.axis_size("screen")
    depth_index = lax.axis_index("depth")
    screen_index = lax.axis_index("screen")
    image_total = tile_source.shape[0]
    half_rows = image_total // screen_count
    owner_rows = image_total // (depth_count * screen_count)
    start = foot_start[0, 0]
    shown = foot_rows[0, 0]
    layers = render_layers(density[0, 0], foot_rows, extinction, colour_slope, colour_offset)
    brick_rows, channels, pixels = layers.shape
    lane = lax.broadcasted_iota(jnp.int32, (1, channels, pixels), 2)
    meta = jnp.where(lane == 0, start, jnp.where(lane == 1, shown, jnp.where(lane == 2, depth_index, 0)))
    stride = brick_rows + 2
    own = jnp.concatenate([layers, meta.astype(jnp.float32), jnp.zeros_like(meta, jnp.float32)], axis=0)
    flat = ring_gather(own, depth_count)
    meta_rows = flat.reshape(depth_count, stride, channels, pixels)[:, brick_rows, 0, :3]
    starts = meta_rows[:, 0].astype(jnp.int32)
    counts = meta_rows[:, 1].astype(jnp.int32)
    brick_ids = meta_rows[:, 2].astype(jnp.int32)
    self_owner = depth_index * screen_count + screen_index
    partner_owner = depth_index * screen_count + (1 - screen_index)
    wanted_self = lax.dynamic_slice_in_dim(tile_source, self_owner * owner_rows, owner_rows)
    wanted_partner = lax.dynamic_slice_in_dim(tile_source, partner_owner * owner_rows, owner_rows)
    wanted = jnp.concatenate([wanted_partner, wanted_self])
    back_idx, front_idx = composite_rows(flat, starts, counts, brick_ids, stride, wanted % half_rows)
    for_partner = blend_rows(flat, back_idx[:owner_rows], front_idx[:owner_rows])
    mine = blend_rows(flat, back_idx[owner_rows:], front_idx[owner_rows:])
    received = lax.ppermute(for_partner, "screen", [(0, 1), (1, 0)])
    in_my_half = (wanted_self // half_rows) == screen_index
    return jnp.where(in_my_half[:, None, None], mine, received)


def solution(mesh):
    return jax.shard_map(
        on_device,
        mesh=mesh,
        in_specs=(
            P(("runs", "depth"), "screen", None, None, None),
            P(("runs", "depth"), "screen"),
            P(("runs", "depth"), "screen"),
            P("runs"),
            P(),
            P(),
            P("runs"),
        ),
        out_specs=P(("runs", "depth", "screen"), None, None),
        check_vma=False,
    )
```

```python
import jax
import jax.numpy as jnp
from jax import lax
from jax.sharding import PartitionSpec as P
from jax.experimental import pallas as pl
from jax.experimental.pallas import tpu as pltpu

BLK = 256


def render_kernel(absorb_ref, slope_ref, offset_ref, shown_ref, density_ref, out_ref):
    block_rows = out_ref.shape[0]
    pixels = out_ref.shape[2]
    sample_count = density_ref.shape[0] // block_rows
    scale = absorb_ref[0] / sample_count
    half_slopes = [0.5 * slope_ref[channel] for channel in range(3)]
    half_offsets = [0.5 * offset_ref[channel] for channel in range(3)]
    shown = shown_ref[0, 0]

    def one_step(step, carry):
        half_transmit, depth_sum, weight_sum = carry[0], carry[1], carry[2]
        values = density_ref[pl.ds(step, block_rows, stride=sample_count), :]
        optical = scale * jnp.log1p(jnp.exp(values))
        passed = jnp.exp(-optical)
        half_weight = half_transmit * (1.0 - passed)
        colours = tuple(
            carry[3 + channel] + half_weight * jnp.tanh(half_slopes[channel] * values + half_offsets[channel])
            for channel in range(3)
        )
        return (half_transmit * passed, depth_sum + optical, weight_sum + half_weight) + colours

    zeros = jnp.zeros((block_rows, pixels), jnp.float32)
    carry = (jnp.full((block_rows, pixels), 0.5, jnp.float32), zeros, zeros, zeros, zeros, zeros)
    carry = lax.fori_loop(0, sample_count, one_step, carry, unroll=16)
    row_ids = pl.program_id(0) * block_rows + lax.broadcasted_iota(jnp.int32, (block_rows, pixels), 0)
    visible = row_ids < shown
    for channel in range(3):
        out_ref[:, channel, :] = jnp.where(visible, carry[2] + carry[3 + channel], 0.0)
    out_ref[:, 3, :] = jnp.where(visible, carry[1], 0.0)


def render_layers(density_block, shown_rows, absorb, colour_slope, colour_offset, block_rows=16):
    brick_rows, sample_count, pixels = density_block.shape
    return pl.pallas_call(
        render_kernel,
        grid=(brick_rows // block_rows,),
        in_specs=[
            pl.BlockSpec(memory_space=pltpu.SMEM),
            pl.BlockSpec(memory_space=pltpu.SMEM),
            pl.BlockSpec(memory_space=pltpu.SMEM),
            pl.BlockSpec(memory_space=pltpu.SMEM),
            pl.BlockSpec((block_rows * sample_count, pixels), lambda i: (i, 0)),
        ],
        out_specs=pl.BlockSpec((block_rows, 4, pixels), lambda i: (i, 0, 0)),
        out_shape=jax.ShapeDtypeStruct((brick_rows, 4, pixels), jnp.float32),
    )(absorb, colour_slope, colour_offset, shown_rows, density_block.reshape(brick_rows * sample_count, pixels))


def composite_rows(flat, starts, counts, brick_ids, stride, image_rows):
    slot_count = starts.shape[0]
    offset = image_rows[:, None] - starts[None, :]
    covered = (offset >= 0) & (offset < counts[None, :])
    depth_ids = brick_ids[None, :]
    slot_ids = jnp.arange(slot_count, dtype=jnp.int32)[None, :]
    back = jnp.max(jnp.where(covered, depth_ids, -1), axis=1)
    is_back = (depth_ids == back[:, None]) & covered
    is_front = (depth_ids == back[:, None] - 1) & covered
    back_off = jnp.sum(jnp.where(is_back, offset, 0), axis=1)
    front_off = jnp.sum(jnp.where(is_front, offset, 0), axis=1)
    back_slot = jnp.sum(jnp.where(is_back, slot_ids, 0), axis=1)
    front_slot = jnp.sum(jnp.where(is_front, slot_ids, 0), axis=1)
    has_front = jnp.any(is_front, axis=1)
    has_back = back >= 0
    zero_row = stride - 1
    back_idx = jnp.where(has_back, back_slot * stride + back_off, zero_row)
    front_idx = jnp.where(has_front, front_slot * stride + front_off, zero_row)
    back_rows = jnp.take(flat, back_idx, axis=0, mode="clip")
    front_rows = jnp.take(flat, front_idx, axis=0, mode="clip")
    front_depth = front_rows[:, 3:4, :]
    colours = front_rows[:, :3, :] + jnp.exp(-front_depth) * back_rows[:, :3, :]
    opacity = 1.0 - jnp.exp(-(front_depth + back_rows[:, 3:4, :]))
    return jnp.concatenate([colours, opacity], axis=1)


def ring_order(count):
    return list(range(0, count, 2)) + list(range(count - 1 - count % 2, 0, -2))


def ring_gather(own, count):
    order = ring_order(count)
    forward = [(order[k], order[(k + 1) % count]) for k in range(count)]
    backward = [(b, a) for a, b in forward]
    slots = [own]
    ahead = own
    behind = own
    for step in range(1, count // 2 + 1):
        ahead = lax.ppermute(ahead, "depth", forward)
        slots.append(ahead)
        if 2 * step < count:
            behind = lax.ppermute(behind, "depth", backward)
            slots.append(behind)
    return jnp.concatenate(slots, axis=0)


def on_device(density, foot_start, foot_rows, extinction, colour_slope, colour_offset, tile_source):
    depth_count = lax.axis_size("depth")
    screen_count = lax.axis_size("screen")
    depth_index = lax.axis_index("depth")
    screen_index = lax.axis_index("screen")
    image_total = tile_source.shape[0]
    half_rows = image_total // screen_count
    owner_rows = image_total // (depth_count * screen_count)
    start = foot_start[0, 0]
    shown = foot_rows[0, 0]
    layers = render_layers(density[0, 0], foot_rows, extinction, colour_slope, colour_offset)
    brick_rows, channels, pixels = layers.shape
    lane = lax.broadcasted_iota(jnp.int32, (1, channels, pixels), 2)
    meta = jnp.where(lane == 0, start, jnp.where(lane == 1, shown, jnp.where(lane == 2, depth_index, 0)))
    stride = brick_rows + 2
    own = jnp.concatenate([layers, meta.astype(jnp.float32), jnp.zeros_like(meta, jnp.float32)], axis=0)
    flat = ring_gather(own, depth_count)
    meta_rows = flat.reshape(depth_count, stride, channels, pixels)[:, brick_rows, 0, :3]
    starts = meta_rows[:, 0].astype(jnp.int32)
    counts = meta_rows[:, 1].astype(jnp.int32)
    brick_ids = meta_rows[:, 2].astype(jnp.int32)
    self_owner = depth_index * screen_count + screen_index
    partner_owner = depth_index * screen_count + (1 - screen_index)
    wanted_self = lax.dynamic_slice_in_dim(tile_source, self_owner * owner_rows, owner_rows)
    wanted_partner = lax.dynamic_slice_in_dim(tile_source, partner_owner * owner_rows, owner_rows)
    for_partner = composite_rows(flat, starts, counts, brick_ids, stride, wanted_partner % half_rows)
    received = lax.ppermute(for_partner, "screen", [(0, 1), (1, 0)])
    mine = composite_rows(flat, starts, counts, brick_ids, stride, wanted_self % half_rows)
    in_my_half = (wanted_self // half_rows) == screen_index
    return jnp.where(in_my_half[:, None, None], mine, received)


def solution(mesh):
    return jax.shard_map(
        on_device,
        mesh=mesh,
        in_specs=(
            P(("runs", "depth"), "screen", None, None, None),
            P(("runs", "depth"), "screen"),
            P(("runs", "depth"), "screen"),
            P("runs"),
            P(),
            P(),
            P("runs"),
        ),
        out_specs=P(("runs", "depth", "screen"), None, None),
        check_vma=False,
    )
```

```python
import jax
import jax.numpy as jnp
from jax import lax
from jax.sharding import PartitionSpec as P
from jax.experimental import pallas as pl
from jax.experimental.pallas import tpu as pltpu

BLK = 256


def render_kernel(absorb_ref, slope_ref, offset_ref, shown_ref, density_ref, out_ref):
    block_rows = out_ref.shape[0]
    pixels = out_ref.shape[2]
    sample_count = density_ref.shape[0] // block_rows
    scale = absorb_ref[0] / sample_count
    half_slopes = [0.5 * slope_ref[channel] for channel in range(3)]
    half_offsets = [0.5 * offset_ref[channel] for channel in range(3)]
    shown = shown_ref[0, 0]

    def one_step(step, carry):
        half_transmit, depth_sum, weight_sum = carry[0], carry[1], carry[2]
        values = density_ref[pl.ds(step, block_rows, stride=sample_count), :]
        optical = scale * jnp.log1p(jnp.exp(values))
        passed = jnp.exp(-optical)
        half_weight = half_transmit * (1.0 - passed)
        colours = tuple(
            carry[3 + channel] + half_weight * jnp.tanh(half_slopes[channel] * values + half_offsets[channel])
            for channel in range(3)
        )
        return (half_transmit * passed, depth_sum + optical, weight_sum + half_weight) + colours

    zeros = jnp.zeros((block_rows, pixels), jnp.float32)
    carry = (jnp.full((block_rows, pixels), 0.5, jnp.float32), zeros, zeros, zeros, zeros, zeros)
    carry = lax.fori_loop(0, sample_count, one_step, carry, unroll=16)
    row_ids = pl.program_id(0) * block_rows + lax.broadcasted_iota(jnp.int32, (block_rows, pixels), 0)
    visible = row_ids < shown
    for channel in range(3):
        out_ref[:, channel, :] = jnp.where(visible, carry[2] + carry[3 + channel], 0.0)
    out_ref[:, 3, :] = jnp.where(visible, carry[1], 0.0)


def render_layers(density_block, shown_rows, absorb, colour_slope, colour_offset, block_rows=16):
    brick_rows, sample_count, pixels = density_block.shape
    return pl.pallas_call(
        render_kernel,
        grid=(brick_rows // block_rows,),
        in_specs=[
            pl.BlockSpec(memory_space=pltpu.SMEM),
            pl.BlockSpec(memory_space=pltpu.SMEM),
            pl.BlockSpec(memory_space=pltpu.SMEM),
            pl.BlockSpec(memory_space=pltpu.SMEM),
            pl.BlockSpec((block_rows * sample_count, pixels), lambda i: (i, 0)),
        ],
        out_specs=pl.BlockSpec((block_rows, 4, pixels), lambda i: (i, 0, 0)),
        out_shape=jax.ShapeDtypeStruct((brick_rows, 4, pixels), jnp.float32),
    )(absorb, colour_slope, colour_offset, shown_rows, density_block.reshape(brick_rows * sample_count, pixels))


def composite_rows(flat, starts, counts, brick_ids, stride, image_rows):
    slot_count = starts.shape[0]
    offset = image_rows[:, None] - starts[None, :]
    covered = (offset >= 0) & (offset < counts[None, :])
    depth_ids = brick_ids[None, :]
    slot_ids = jnp.arange(slot_count, dtype=jnp.int32)[None, :]
    back = jnp.max(jnp.where(covered, depth_ids, -1), axis=1)
    is_back = (depth_ids == back[:, None]) & covered
    is_front = (depth_ids == back[:, None] - 1) & covered
    back_off = jnp.sum(jnp.where(is_back, offset, 0), axis=1)
    front_off = jnp.sum(jnp.where(is_front, offset, 0), axis=1)
    back_slot = jnp.sum(jnp.where(is_back, slot_ids, 0), axis=1)
    front_slot = jnp.sum(jnp.where(is_front, slot_ids, 0), axis=1)
    has_front = jnp.any(is_front, axis=1)
    has_back = back >= 0
    zero_row = stride - 1
    back_idx = jnp.where(has_back, back_slot * stride + back_off, zero_row)
    front_idx = jnp.where(has_front, front_slot * stride + front_off, zero_row)
    back_rows = jnp.take(flat, back_idx, axis=0, mode="clip")
    front_rows = jnp.take(flat, front_idx, axis=0, mode="clip")
    front_depth = front_rows[:, 3:4, :]
    colours = front_rows[:, :3, :] + jnp.exp(-front_depth) * back_rows[:, :3, :]
    opacity = 1.0 - jnp.exp(-(front_depth + back_rows[:, 3:4, :]))
    return jnp.concatenate([colours, opacity], axis=1)


def ring_order(count):
    return list(range(0, count, 2)) + list(range(count - 1 - count % 2, 0, -2))


def ring_gather(own, count):
    order = ring_order(count)
    forward = [(order[k], order[(k + 1) % count]) for k in range(count)]
    backward = [(b, a) for a, b in forward]
    slots = [own]
    ahead = own
    behind = own
    for step in range(1, (count + 1) // 2):
        ahead = lax.ppermute(ahead, "depth", forward)
        behind = lax.ppermute(behind, "depth", backward)
        slots += [ahead, behind]
    if count % 2 == 0 and count > 1:
        middle = own.shape[0] // 2
        slots.append(jnp.concatenate([
            lax.ppermute(ahead[:middle], "depth", forward),
            lax.ppermute(behind[middle:], "depth", backward),
        ], axis=0))
    return jnp.concatenate(slots, axis=0)


def on_device(density, foot_start, foot_rows, extinction, colour_slope, colour_offset, tile_source):
    depth_count = lax.axis_size("depth")
    screen_count = lax.axis_size("screen")
    depth_index = lax.axis_index("depth")
    screen_index = lax.axis_index("screen")
    image_total = tile_source.shape[0]
    half_rows = image_total // screen_count
    owner_rows = image_total // (depth_count * screen_count)
    start = foot_start[0, 0]
    shown = foot_rows[0, 0]
    layers = render_layers(density[0, 0], foot_rows, extinction, colour_slope, colour_offset)
    brick_rows, channels, pixels = layers.shape
    lane = lax.broadcasted_iota(jnp.int32, (1, channels, pixels), 2)
    meta = jnp.where(lane == 0, start, jnp.where(lane == 1, shown, jnp.where(lane == 2, depth_index, 0)))
    stride = brick_rows + 2
    own = jnp.concatenate([layers, meta.astype(jnp.float32), jnp.zeros_like(meta, jnp.float32)], axis=0)
    flat = ring_gather(own, depth_count)
    meta_rows = flat.reshape(depth_count, stride, channels, pixels)[:, brick_rows, 0, :3]
    starts = meta_rows[:, 0].astype(jnp.int32)
    counts = meta_rows[:, 1].astype(jnp.int32)
    brick_ids = meta_rows[:, 2].astype(jnp.int32)
    self_owner = depth_index * screen_count + screen_index
    partner_owner = depth_index * screen_count + (1 - screen_index)
    wanted_self = lax.dynamic_slice_in_dim(tile_source, self_owner * owner_rows, owner_rows)
    wanted_partner = lax.dynamic_slice_in_dim(tile_source, partner_owner * owner_rows, owner_rows)
    wanted = jnp.concatenate([wanted_self, wanted_partner])
    rows = composite_rows(flat, starts, counts, brick_ids, stride, wanted % half_rows)
    mine = rows[:owner_rows]
    for_partner = rows[owner_rows:]
    received = lax.ppermute(for_partner, "screen", [(0, 1), (1, 0)])
    in_my_half = (wanted_self // half_rows) == screen_index
    return jnp.where(in_my_half[:, None, None], mine, received)


def solution(mesh):
    return jax.shard_map(
        on_device,
        mesh=mesh,
        in_specs=(
            P(("runs", "depth"), "screen", None, None, None),
            P(("runs", "depth"), "screen"),
            P(("runs", "depth"), "screen"),
            P("runs"),
            P(),
            P(),
            P("runs"),
        ),
        out_specs=P(("runs", "depth", "screen"), None, None),
        check_vma=False,
    )
```

```python
import functools

import jax
import jax.numpy as jnp
from jax import lax
from jax.sharding import PartitionSpec as P
from jax.experimental import pallas as pl
from jax.experimental.pallas import tpu as pltpu

BLK = 256


def render_kernel(first_block, absorb_ref, slope_ref, offset_ref, shown_ref, density_ref, out_ref):
    block_rows = out_ref.shape[0]
    pixels = out_ref.shape[2]
    sample_count = density_ref.shape[0] // block_rows
    scale = absorb_ref[0] / sample_count
    half_slopes = [0.5 * slope_ref[channel] for channel in range(3)]
    half_offsets = [0.5 * offset_ref[channel] for channel in range(3)]
    shown = shown_ref[0, 0]

    def one_step(step, carry):
        half_transmit, depth_sum, weight_sum = carry[0], carry[1], carry[2]
        values = density_ref[pl.ds(step, block_rows, stride=sample_count), :]
        optical = scale * jnp.log1p(jnp.exp(values))
        passed = jnp.exp(-optical)
        half_weight = half_transmit * (1.0 - passed)
        colours = tuple(
            carry[3 + channel] + half_weight * jnp.tanh(half_slopes[channel] * values + half_offsets[channel])
            for channel in range(3)
        )
        return (half_transmit * passed, depth_sum + optical, weight_sum + half_weight) + colours

    zeros = jnp.zeros((block_rows, pixels), jnp.float32)
    carry = (jnp.full((block_rows, pixels), 0.5, jnp.float32), zeros, zeros, zeros, zeros, zeros)
    carry = lax.fori_loop(0, sample_count, one_step, carry, unroll=16)
    row_ids = (pl.program_id(0) + first_block) * block_rows + lax.broadcasted_iota(jnp.int32, (block_rows, pixels), 0)
    visible = row_ids < shown
    for channel in range(3):
        out_ref[:, channel, :] = jnp.where(visible, carry[2] + carry[3 + channel], 0.0)
    out_ref[:, 3, :] = jnp.where(visible, carry[1], 0.0)


def render_layers(density_block, shown_rows, absorb, colour_slope, colour_offset, first_row, row_count,
                  block_rows=16):
    brick_rows, sample_count, pixels = density_block.shape
    first_block = first_row // block_rows
    return pl.pallas_call(
        functools.partial(render_kernel, first_block),
        grid=(row_count // block_rows,),
        in_specs=[
            pl.BlockSpec(memory_space=pltpu.SMEM),
            pl.BlockSpec(memory_space=pltpu.SMEM),
            pl.BlockSpec(memory_space=pltpu.SMEM),
            pl.BlockSpec(memory_space=pltpu.SMEM),
            pl.BlockSpec((block_rows * sample_count, pixels), lambda i: (i + first_block, 0)),
        ],
        out_specs=pl.BlockSpec((block_rows, 4, pixels), lambda i: (i, 0, 0)),
        out_shape=jax.ShapeDtypeStruct((row_count, 4, pixels), jnp.float32),
    )(absorb, colour_slope, colour_offset, shown_rows, density_block.reshape(brick_rows * sample_count, pixels))


def composite_rows(flat, starts, counts, brick_ids, stride, split, image_rows):
    slot_count = starts.shape[0]
    offset = image_rows[:, None] - starts[None, :]
    covered = (offset >= 0) & (offset < counts[None, :])
    depth_ids = brick_ids[None, :]
    slot_ids = jnp.arange(slot_count, dtype=jnp.int32)[None, :]
    back = jnp.max(jnp.where(covered, depth_ids, -1), axis=1)
    is_back = (depth_ids == back[:, None]) & covered
    is_front = (depth_ids == back[:, None] - 1) & covered
    back_off = jnp.sum(jnp.where(is_back, offset, 0), axis=1)
    front_off = jnp.sum(jnp.where(is_front, offset, 0), axis=1)
    back_slot = jnp.sum(jnp.where(is_back, slot_ids, 0), axis=1)
    front_slot = jnp.sum(jnp.where(is_front, slot_ids, 0), axis=1)
    has_front = jnp.any(is_front, axis=1)
    has_back = back >= 0
    zero_row = split + 1
    back_off = back_off + 2 * (back_off >= split).astype(jnp.int32)
    front_off = front_off + 2 * (front_off >= split).astype(jnp.int32)
    back_idx = jnp.where(has_back, back_slot * stride + back_off, zero_row)
    front_idx = jnp.where(has_front, front_slot * stride + front_off, zero_row)
    back_rows = jnp.take(flat, back_idx, axis=0, mode="clip")
    front_rows = jnp.take(flat, front_idx, axis=0, mode="clip")
    front_depth = front_rows[:, 3:4, :]
    colours = front_rows[:, :3, :] + jnp.exp(-front_depth) * back_rows[:, :3, :]
    opacity = 1.0 - jnp.exp(-(front_depth + back_rows[:, 3:4, :]))
    return jnp.concatenate([colours, opacity], axis=1)


def ring_order(count):
    return list(range(0, count, 2)) + list(range(count - 1 - count % 2, 0, -2))


def ring_gather(own, count):
    order = ring_order(count)
    forward = [(order[k], order[(k + 1) % count]) for k in range(count)]
    backward = [(b, a) for a, b in forward]
    slots = [own]
    ahead = own
    behind = own
    for step in range(1, count // 2 + 1):
        ahead = lax.ppermute(ahead, "depth", forward)
        slots.append(ahead)
        if 2 * step < count:
            behind = lax.ppermute(behind, "depth", backward)
            slots.append(behind)
    return slots


def on_device(density, foot_start, foot_rows, extinction, colour_slope, colour_offset, tile_source):
    depth_count = lax.axis_size("depth")
    screen_count = lax.axis_size("screen")
    depth_index = lax.axis_index("depth")
    screen_index = lax.axis_index("screen")
    image_total = tile_source.shape[0]
    half_rows = image_total // screen_count
    owner_rows = image_total // (depth_count * screen_count)
    start = foot_start[0, 0]
    shown = foot_rows[0, 0]
    brick_rows, pixels = density.shape[2], density.shape[4]
    channels = 4
    split = brick_rows // 2
    lane = lax.broadcasted_iota(jnp.int32, (1, channels, pixels), 2)
    meta = jnp.where(lane == 0, start, jnp.where(lane == 1, shown, jnp.where(lane == 2, depth_index, 0)))
    stride = brick_rows + 2
    front_half = render_layers(density[0, 0], foot_rows, extinction, colour_slope, colour_offset, 0, split)
    front_own = jnp.concatenate([front_half, meta.astype(jnp.float32), jnp.zeros_like(meta, jnp.float32)], axis=0)
    front_slots = ring_gather(front_own, depth_count)
    back_half = render_layers(density[0, 0], foot_rows, extinction, colour_slope, colour_offset, split,
                              brick_rows - split)
    back_slots = ring_gather(back_half, depth_count)
    flat = jnp.concatenate([part for pair in zip(front_slots, back_slots) for part in pair], axis=0)
    meta_rows = flat.reshape(depth_count, stride, channels, pixels)[:, split, 0, :3]
    starts = meta_rows[:, 0].astype(jnp.int32)
    counts = meta_rows[:, 1].astype(jnp.int32)
    brick_ids = meta_rows[:, 2].astype(jnp.int32)
    self_owner = depth_index * screen_count + screen_index
    partner_owner = depth_index * screen_count + (1 - screen_index)
    wanted_self = lax.dynamic_slice_in_dim(tile_source, self_owner * owner_rows, owner_rows)
    wanted_partner = lax.dynamic_slice_in_dim(tile_source, partner_owner * owner_rows, owner_rows)
    wanted = jnp.concatenate([wanted_self, wanted_partner])
    rows = composite_rows(flat, starts, counts, brick_ids, stride, split, wanted % half_rows)
    mine = rows[:owner_rows]
    for_partner = rows[owner_rows:]
    received = lax.ppermute(for_partner, "screen", [(0, 1), (1, 0)])
    in_my_half = (wanted_self // half_rows) == screen_index
    return jnp.where(in_my_half[:, None, None], mine, received)


def solution(mesh):
    return jax.shard_map(
        on_device,
        mesh=mesh,
        in_specs=(
            P(("runs", "depth"), "screen", None, None, None),
            P(("runs", "depth"), "screen"),
            P(("runs", "depth"), "screen"),
            P("runs"),
            P(),
            P(),
            P("runs"),
        ),
        out_specs=P(("runs", "depth", "screen"), None, None),
        check_vma=False,
    )
```

```python
import jax
import jax.numpy as jnp
from jax import lax
from jax.sharding import PartitionSpec as P
from jax.experimental import pallas as pl
from jax.experimental.pallas import tpu as pltpu

BLK = 256


def render_kernel(absorb_ref, slope_ref, offset_ref, shown_ref, density_ref, out_ref):
    block_rows = out_ref.shape[0]
    pixels = out_ref.shape[2]
    sample_count = density_ref.shape[0] // block_rows
    scale = absorb_ref[0] / sample_count
    half_slopes = [0.5 * slope_ref[channel] for channel in range(3)]
    half_offsets = [0.5 * offset_ref[channel] for channel in range(3)]
    shown = shown_ref[0, 0]

    def one_step(step, carry):
        half_transmit, depth_sum, weight_sum = carry[0], carry[1], carry[2]
        values = density_ref[pl.ds(step, block_rows, stride=sample_count), :]
        optical = scale * jnp.log1p(jnp.exp(values))
        passed = jnp.exp(-optical)
        half_weight = half_transmit * (1.0 - passed)
        colours = tuple(
            carry[3 + channel] + half_weight * jnp.tanh(half_slopes[channel] * values + half_offsets[channel])
            for channel in range(3)
        )
        return (half_transmit * passed, depth_sum + optical, weight_sum + half_weight) + colours

    zeros = jnp.zeros((block_rows, pixels), jnp.float32)
    carry = (jnp.full((block_rows, pixels), 0.5, jnp.float32), zeros, zeros, zeros, zeros, zeros)
    carry = lax.fori_loop(0, sample_count, one_step, carry, unroll=16)
    row_ids = pl.program_id(0) * block_rows + lax.broadcasted_iota(jnp.int32, (block_rows, pixels), 0)
    visible = row_ids < shown
    for channel in range(3):
        out_ref[:, channel, :] = jnp.where(visible, carry[2] + carry[3 + channel], 0.0)
    out_ref[:, 3, :] = jnp.where(visible, carry[1], 0.0)


def render_layers(density_block, shown_rows, absorb, colour_slope, colour_offset, block_rows=16):
    brick_rows, sample_count, pixels = density_block.shape
    return pl.pallas_call(
        render_kernel,
        grid=(brick_rows // block_rows,),
        in_specs=[
            pl.BlockSpec(memory_space=pltpu.SMEM),
            pl.BlockSpec(memory_space=pltpu.SMEM),
            pl.BlockSpec(memory_space=pltpu.SMEM),
            pl.BlockSpec(memory_space=pltpu.SMEM),
            pl.BlockSpec((block_rows * sample_count, pixels), lambda i: (i, 0)),
        ],
        out_specs=pl.BlockSpec((block_rows, 4, pixels), lambda i: (i, 0, 0)),
        out_shape=jax.ShapeDtypeStruct((brick_rows, 4, pixels), jnp.float32),
    )(absorb, colour_slope, colour_offset, shown_rows, density_block.reshape(brick_rows * sample_count, pixels))


def composite_rows(flat, starts, counts, brick_ids, stride, image_rows):
    slot_count = starts.shape[0]
    offset = image_rows[:, None] - starts[None, :]
    covered = (offset >= 0) & (offset < counts[None, :])
    depth_ids = brick_ids[None, :]
    slot_ids = jnp.arange(slot_count, dtype=jnp.int32)[None, :]
    back = jnp.max(jnp.where(covered, depth_ids, -1), axis=1)
    is_back = (depth_ids == back[:, None]) & covered
    is_front = (depth_ids == back[:, None] - 1) & covered
    back_off = jnp.sum(jnp.where(is_back, offset, 0), axis=1)
    front_off = jnp.sum(jnp.where(is_front, offset, 0), axis=1)
    back_slot = jnp.sum(jnp.where(is_back, slot_ids, 0), axis=1)
    front_slot = jnp.sum(jnp.where(is_front, slot_ids, 0), axis=1)
    has_front = jnp.any(is_front, axis=1)
    has_back = back >= 0
    zero_row = stride - 1
    back_idx = jnp.where(has_back, back_slot * stride + back_off, zero_row)
    front_idx = jnp.where(has_front, front_slot * stride + front_off, zero_row)
    back_rows = flat.at[back_idx].get(mode="promise_in_bounds")
    front_rows = flat.at[front_idx].get(mode="promise_in_bounds")
    front_depth = front_rows[:, 3:4, :]
    colours = front_rows[:, :3, :] + jnp.exp(-front_depth) * back_rows[:, :3, :]
    opacity = 1.0 - jnp.exp(-(front_depth + back_rows[:, 3:4, :]))
    return jnp.concatenate([colours, opacity], axis=1)


def ring_order(count):
    return list(range(0, count, 2)) + list(range(count - 1 - count % 2, 0, -2))


def ring_gather(own, count):
    order = ring_order(count)
    forward = [(order[k], order[(k + 1) % count]) for k in range(count)]
    backward = [(b, a) for a, b in forward]
    slots = [own]
    ahead = own
    behind = own
    for step in range(1, count // 2 + 1):
        ahead = lax.ppermute(ahead, "depth", forward)
        slots.append(ahead)
        if 2 * step < count:
            behind = lax.ppermute(behind, "depth", backward)
            slots.append(behind)
    return jnp.concatenate(slots, axis=0)


def on_device(density, foot_start, foot_rows, extinction, colour_slope, colour_offset, tile_source):
    depth_count = lax.axis_size("depth")
    screen_count = lax.axis_size("screen")
    depth_index = lax.axis_index("depth")
    screen_index = lax.axis_index("screen")
    image_total = tile_source.shape[0]
    half_rows = image_total // screen_count
    owner_rows = image_total // (depth_count * screen_count)
    start = foot_start[0, 0]
    shown = foot_rows[0, 0]
    layers = render_layers(density[0, 0], foot_rows, extinction, colour_slope, colour_offset)
    brick_rows, channels, pixels = layers.shape
    lane = lax.broadcasted_iota(jnp.int32, (1, channels, pixels), 2)
    meta = jnp.where(lane == 0, start, jnp.where(lane == 1, shown, jnp.where(lane == 2, depth_index, 0)))
    stride = brick_rows + 2
    own = jnp.concatenate([layers, meta.astype(jnp.float32), jnp.zeros_like(meta, jnp.float32)], axis=0)
    flat = ring_gather(own, depth_count)
    meta_rows = flat.reshape(depth_count, stride, channels, pixels)[:, brick_rows, 0, :3]
    starts = meta_rows[:, 0].astype(jnp.int32)
    counts = meta_rows[:, 1].astype(jnp.int32)
    brick_ids = meta_rows[:, 2].astype(jnp.int32)
    self_owner = depth_index * screen_count + screen_index
    partner_owner = depth_index * screen_count + (1 - screen_index)
    wanted_self = lax.dynamic_slice_in_dim(tile_source, self_owner * owner_rows, owner_rows)
    wanted_partner = lax.dynamic_slice_in_dim(tile_source, partner_owner * owner_rows, owner_rows)
    wanted = jnp.concatenate([wanted_self, wanted_partner])
    rows = composite_rows(flat, starts, counts, brick_ids, stride, wanted % half_rows)
    mine = rows[:owner_rows]
    for_partner = rows[owner_rows:]
    received = lax.ppermute(for_partner, "screen", [(0, 1), (1, 0)])
    in_my_half = (wanted_self // half_rows) == screen_index
    return jnp.where(in_my_half[:, None, None], mine, received)


def solution(mesh):
    return jax.shard_map(
        on_device,
        mesh=mesh,
        in_specs=(
            P(("runs", "depth"), "screen", None, None, None),
            P(("runs", "depth"), "screen"),
            P(("runs", "depth"), "screen"),
            P("runs"),
            P(),
            P(),
            P("runs"),
        ),
        out_specs=P(("runs", "depth", "screen"), None, None),
        check_vma=False,
    )
```

```python
import jax
import jax.numpy as jnp
from jax import lax
from jax.sharding import PartitionSpec as P
from jax.experimental import pallas as pl
from jax.experimental.pallas import tpu as pltpu

BLK = 256


def render_kernel(absorb_ref, slope_ref, offset_ref, shown_ref, density_ref, slot_ref, out_ref):
    del slot_ref
    block_rows = out_ref.shape[0]
    pixels = out_ref.shape[2]
    sample_count = density_ref.shape[0] // block_rows
    scale = absorb_ref[0] / sample_count
    half_slopes = [0.5 * slope_ref[channel] for channel in range(3)]
    half_offsets = [0.5 * offset_ref[channel] for channel in range(3)]
    shown = shown_ref[0, 0]

    def one_step(step, carry):
        half_transmit, depth_sum, weight_sum = carry[0], carry[1], carry[2]
        values = density_ref[pl.ds(step, block_rows, stride=sample_count), :]
        optical = scale * jnp.log1p(jnp.exp(values))
        passed = jnp.exp(-optical)
        half_weight = half_transmit * (1.0 - passed)
        colours = tuple(
            carry[3 + channel] + half_weight * jnp.tanh(half_slopes[channel] * values + half_offsets[channel])
            for channel in range(3)
        )
        return (half_transmit * passed, depth_sum + optical, weight_sum + half_weight) + colours

    zeros = jnp.zeros((block_rows, pixels), jnp.float32)
    carry = (jnp.full((block_rows, pixels), 0.5, jnp.float32), zeros, zeros, zeros, zeros, zeros)
    carry = lax.fori_loop(0, sample_count, one_step, carry, unroll=16)
    row_ids = pl.program_id(0) * block_rows + lax.broadcasted_iota(jnp.int32, (block_rows, pixels), 0)
    visible = row_ids < shown
    for channel in range(3):
        out_ref[:, channel, :] = jnp.where(visible, carry[2] + carry[3 + channel], 0.0)
    out_ref[:, 3, :] = jnp.where(visible, carry[1], 0.0)


def render_layers(density_block, shown_rows, absorb, colour_slope, colour_offset, slot, block_rows=16):
    brick_rows, sample_count, pixels = density_block.shape
    return pl.pallas_call(
        render_kernel,
        grid=(brick_rows // block_rows,),
        in_specs=[
            pl.BlockSpec(memory_space=pltpu.SMEM),
            pl.BlockSpec(memory_space=pltpu.SMEM),
            pl.BlockSpec(memory_space=pltpu.SMEM),
            pl.BlockSpec(memory_space=pltpu.SMEM),
            pl.BlockSpec((block_rows * sample_count, pixels), lambda i: (i, 0)),
            pl.BlockSpec(memory_space=pl.ANY),
        ],
        out_specs=pl.BlockSpec((block_rows, 4, pixels), lambda i: (i, 0, 0)),
        out_shape=jax.ShapeDtypeStruct(slot.shape, jnp.float32),
        input_output_aliases={5: 0},
    )(absorb, colour_slope, colour_offset, shown_rows, density_block.reshape(brick_rows * sample_count, pixels),
      slot)


def composite_rows(flat, starts, counts, brick_ids, stride, image_rows):
    slot_count = starts.shape[0]
    offset = image_rows[:, None] - starts[None, :]
    covered = (offset >= 0) & (offset < counts[None, :])
    depth_ids = brick_ids[None, :]
    slot_ids = jnp.arange(slot_count, dtype=jnp.int32)[None, :]
    back = jnp.max(jnp.where(covered, depth_ids, -1), axis=1)
    is_back = (depth_ids == back[:, None]) & covered
    is_front = (depth_ids == back[:, None] - 1) & covered
    back_off = jnp.sum(jnp.where(is_back, offset, 0), axis=1)
    front_off = jnp.sum(jnp.where(is_front, offset, 0), axis=1)
    back_slot = jnp.sum(jnp.where(is_back, slot_ids, 0), axis=1)
    front_slot = jnp.sum(jnp.where(is_front, slot_ids, 0), axis=1)
    has_front = jnp.any(is_front, axis=1)
    has_back = back >= 0
    zero_row = stride - 1
    back_idx = jnp.where(has_back, back_slot * stride + back_off, zero_row)
    front_idx = jnp.where(has_front, front_slot * stride + front_off, zero_row)
    back_rows = jnp.take(flat, back_idx, axis=0, mode="clip")
    front_rows = jnp.take(flat, front_idx, axis=0, mode="clip")
    front_depth = front_rows[:, 3:4, :]
    colours = front_rows[:, :3, :] + jnp.exp(-front_depth) * back_rows[:, :3, :]
    opacity = 1.0 - jnp.exp(-(front_depth + back_rows[:, 3:4, :]))
    return jnp.concatenate([colours, opacity], axis=1)


def ring_order(count):
    return list(range(0, count, 2)) + list(range(count - 1 - count % 2, 0, -2))


def ring_gather(own, count):
    order = ring_order(count)
    forward = [(order[k], order[(k + 1) % count]) for k in range(count)]
    backward = [(b, a) for a, b in forward]
    slots = [own]
    ahead = own
    behind = own
    for step in range(1, count // 2 + 1):
        ahead = lax.ppermute(ahead, "depth", forward)
        slots.append(ahead)
        if 2 * step < count:
            behind = lax.ppermute(behind, "depth", backward)
            slots.append(behind)
    return jnp.concatenate(slots, axis=0)


def on_device(density, foot_start, foot_rows, extinction, colour_slope, colour_offset, tile_source):
    depth_count = lax.axis_size("depth")
    screen_count = lax.axis_size("screen")
    depth_index = lax.axis_index("depth")
    screen_index = lax.axis_index("screen")
    image_total = tile_source.shape[0]
    half_rows = image_total // screen_count
    owner_rows = image_total // (depth_count * screen_count)
    start = foot_start[0, 0]
    shown = foot_rows[0, 0]
    brick_rows, pixels = density.shape[2], density.shape[4]
    channels = 4
    lane = lax.broadcasted_iota(jnp.int32, (1, channels, pixels), 2)
    meta = jnp.where(lane == 0, start, jnp.where(lane == 1, shown, jnp.where(lane == 2, depth_index, 0)))
    stride = brick_rows + 2
    slot = jnp.concatenate([jnp.zeros((brick_rows, channels, pixels), jnp.float32), meta.astype(jnp.float32),
                            jnp.zeros((1, channels, pixels), jnp.float32)], axis=0)
    own = render_layers(density[0, 0], foot_rows, extinction, colour_slope, colour_offset, slot)
    flat = ring_gather(own, depth_count)
    meta_rows = flat.reshape(depth_count, stride, channels, pixels)[:, brick_rows, 0, :3]
    starts = meta_rows[:, 0].astype(jnp.int32)
    counts = meta_rows[:, 1].astype(jnp.int32)
    brick_ids = meta_rows[:, 2].astype(jnp.int32)
    self_owner = depth_index * screen_count + screen_index
    partner_owner = depth_index * screen_count + (1 - screen_index)
    wanted_self = lax.dynamic_slice_in_dim(tile_source, self_owner * owner_rows, owner_rows)
    wanted_partner = lax.dynamic_slice_in_dim(tile_source, partner_owner * owner_rows, owner_rows)
    wanted = jnp.concatenate([wanted_self, wanted_partner])
    rows = composite_rows(flat, starts, counts, brick_ids, stride, wanted % half_rows)
    mine = rows[:owner_rows]
    for_partner = rows[owner_rows:]
    received = lax.ppermute(for_partner, "screen", [(0, 1), (1, 0)])
    in_my_half = (wanted_self // half_rows) == screen_index
    return jnp.where(in_my_half[:, None, None], mine, received)


def solution(mesh):
    return jax.shard_map(
        on_device,
        mesh=mesh,
        in_specs=(
            P(("runs", "depth"), "screen", None, None, None),
            P(("runs", "depth"), "screen"),
            P(("runs", "depth"), "screen"),
            P("runs"),
            P(),
            P(),
            P("runs"),
        ),
        out_specs=P(("runs", "depth", "screen"), None, None),
        check_vma=False,
    )
```

```python
import jax
import jax.numpy as jnp
from jax import lax
from jax.sharding import PartitionSpec as P
from jax.experimental import pallas as pl
from jax.experimental.pallas import tpu as pltpu

BLK = 256


def render_kernel(absorb_ref, slope_ref, offset_ref, shown_ref, density_ref, slot_ref, out_ref):
    del slot_ref
    block_rows = out_ref.shape[0]
    pixels = out_ref.shape[2]
    sample_count = density_ref.shape[0] // block_rows
    scale = absorb_ref[0] / sample_count
    half_slopes = [0.5 * slope_ref[channel] for channel in range(3)]
    half_offsets = [0.5 * offset_ref[channel] for channel in range(3)]
    shown = shown_ref[0, 0]

    def one_step(step, carry):
        half_transmit, depth_sum, weight_sum = carry[0], carry[1], carry[2]
        values = density_ref[pl.ds(step, block_rows, stride=sample_count), :]
        optical = scale * jnp.log1p(jnp.exp(values))
        passed = jnp.exp(-optical)
        half_weight = half_transmit * (1.0 - passed)
        colours = tuple(
            carry[3 + channel] + half_weight * jnp.tanh(half_slopes[channel] * values + half_offsets[channel])
            for channel in range(3)
        )
        return (half_transmit * passed, depth_sum + optical, weight_sum + half_weight) + colours

    zeros = jnp.zeros((block_rows, pixels), jnp.float32)
    carry = (jnp.full((block_rows, pixels), 0.5, jnp.float32), zeros, zeros, zeros, zeros, zeros)
    carry = lax.fori_loop(0, sample_count, one_step, carry, unroll=32)
    row_ids = pl.program_id(0) * block_rows + lax.broadcasted_iota(jnp.int32, (block_rows, pixels), 0)
    visible = row_ids < shown
    for channel in range(3):
        out_ref[:, channel, :] = jnp.where(visible, carry[2] + carry[3 + channel], 0.0)
    out_ref[:, 3, :] = jnp.where(visible, carry[1], 0.0)


def render_layers(density_block, shown_rows, absorb, colour_slope, colour_offset, slot, block_rows=16):
    brick_rows, sample_count, pixels = density_block.shape
    return pl.pallas_call(
        render_kernel,
        grid=(brick_rows // block_rows,),
        in_specs=[
            pl.BlockSpec(memory_space=pltpu.SMEM),
            pl.BlockSpec(memory_space=pltpu.SMEM),
            pl.BlockSpec(memory_space=pltpu.SMEM),
            pl.BlockSpec(memory_space=pltpu.SMEM),
            pl.BlockSpec((block_rows * sample_count, pixels), lambda i: (i, 0)),
            pl.BlockSpec(memory_space=pl.ANY),
        ],
        out_specs=pl.BlockSpec((block_rows, 4, pixels), lambda i: (i, 0, 0)),
        out_shape=jax.ShapeDtypeStruct(slot.shape, jnp.float32),
        input_output_aliases={5: 0},
    )(absorb, colour_slope, colour_offset, shown_rows, density_block.reshape(brick_rows * sample_count, pixels),
      slot)


def composite_rows(flat, starts, counts, brick_ids, stride, image_rows):
    slot_count = starts.shape[0]
    offset = image_rows[:, None] - starts[None, :]
    covered = (offset >= 0) & (offset < counts[None, :])
    depth_ids = brick_ids[None, :]
    slot_ids = jnp.arange(slot_count, dtype=jnp.int32)[None, :]
    back = jnp.max(jnp.where(covered, depth_ids, -1), axis=1)
    is_back = (depth_ids == back[:, None]) & covered
    is_front = (depth_ids == back[:, None] - 1) & covered
    back_off = jnp.sum(jnp.where(is_back, offset, 0), axis=1)
    front_off = jnp.sum(jnp.where(is_front, offset, 0), axis=1)
    back_slot = jnp.sum(jnp.where(is_back, slot_ids, 0), axis=1)
    front_slot = jnp.sum(jnp.where(is_front, slot_ids, 0), axis=1)
    has_front = jnp.any(is_front, axis=1)
    has_back = back >= 0
    zero_row = stride - 1
    back_idx = jnp.where(has_back, back_slot * stride + back_off, zero_row)
    front_idx = jnp.where(has_front, front_slot * stride + front_off, zero_row)
    back_rows = jnp.take(flat, back_idx, axis=0, mode="clip")
    front_rows = jnp.take(flat, front_idx, axis=0, mode="clip")
    front_depth = front_rows[:, 3:4, :]
    colours = front_rows[:, :3, :] + jnp.exp(-front_depth) * back_rows[:, :3, :]
    opacity = 1.0 - jnp.exp(-(front_depth + back_rows[:, 3:4, :]))
    return jnp.concatenate([colours, opacity], axis=1)


def ring_order(count):
    return list(range(0, count, 2)) + list(range(count - 1 - count % 2, 0, -2))


def ring_gather(own, count):
    order = ring_order(count)
    forward = [(order[k], order[(k + 1) % count]) for k in range(count)]
    backward = [(b, a) for a, b in forward]
    slots = [own]
    ahead = own
    behind = own
    for step in range(1, count // 2 + 1):
        ahead = lax.ppermute(ahead, "depth", forward)
        slots.append(ahead)
        if 2 * step < count:
            behind = lax.ppermute(behind, "depth", backward)
            slots.append(behind)
    return jnp.concatenate(slots, axis=0)


def on_device(density, foot_start, foot_rows, extinction, colour_slope, colour_offset, tile_source):
    depth_count = lax.axis_size("depth")
    screen_count = lax.axis_size("screen")
    depth_index = lax.axis_index("depth")
    screen_index = lax.axis_index("screen")
    image_total = tile_source.shape[0]
    half_rows = image_total // screen_count
    owner_rows = image_total // (depth_count * screen_count)
    start = foot_start[0, 0]
    shown = foot_rows[0, 0]
    brick_rows, pixels = density.shape[2], density.shape[4]
    channels = 4
    lane = lax.broadcasted_iota(jnp.int32, (1, channels, pixels), 2)
    meta = jnp.where(lane == 0, start, jnp.where(lane == 1, shown, jnp.where(lane == 2, depth_index, 0)))
    stride = brick_rows + 2
    slot = jnp.concatenate([jnp.zeros((brick_rows, channels, pixels), jnp.float32), meta.astype(jnp.float32),
                            jnp.zeros((1, channels, pixels), jnp.float32)], axis=0)
    own = render_layers(density[0, 0], foot_rows, extinction, colour_slope, colour_offset, slot)
    flat = ring_gather(own, depth_count)
    meta_rows = flat.reshape(depth_count, stride, channels, pixels)[:, brick_rows, 0, :3]
    starts = meta_rows[:, 0].astype(jnp.int32)
    counts = meta_rows[:, 1].astype(jnp.int32)
    brick_ids = meta_rows[:, 2].astype(jnp.int32)
    self_owner = depth_index * screen_count + screen_index
    partner_owner = depth_index * screen_count + (1 - screen_index)
    wanted_self = lax.dynamic_slice_in_dim(tile_source, self_owner * owner_rows, owner_rows)
    wanted_partner = lax.dynamic_slice_in_dim(tile_source, partner_owner * owner_rows, owner_rows)
    wanted = jnp.concatenate([wanted_self, wanted_partner])
    rows = composite_rows(flat, starts, counts, brick_ids, stride, wanted % half_rows)
    mine = rows[:owner_rows]
    for_partner = rows[owner_rows:]
    received = lax.ppermute(for_partner, "screen", [(0, 1), (1, 0)])
    in_my_half = (wanted_self // half_rows) == screen_index
    return jnp.where(in_my_half[:, None, None], mine, received)


def solution(mesh):
    return jax.shard_map(
        on_device,
        mesh=mesh,
        in_specs=(
            P(("runs", "depth"), "screen", None, None, None),
            P(("runs", "depth"), "screen"),
            P(("runs", "depth"), "screen"),
            P("runs"),
            P(),
            P(),
            P("runs"),
        ),
        out_specs=P(("runs", "depth", "screen"), None, None),
        check_vma=False,
    )
```

```python
import jax
import jax.numpy as jnp
from jax import lax
from jax.sharding import PartitionSpec as P
from jax.experimental import pallas as pl
from jax.experimental.pallas import tpu as pltpu

BLK = 256


def render_kernel(absorb_ref, slope_ref, offset_ref, shown_ref, density_ref, slot_ref, out_ref):
    del slot_ref
    block_rows = out_ref.shape[0]
    pixels = out_ref.shape[2]
    sample_count = density_ref.shape[0] // block_rows
    scale = absorb_ref[0] / sample_count
    half_slopes = [0.5 * slope_ref[channel] for channel in range(3)]
    half_offsets = [0.5 * offset_ref[channel] for channel in range(3)]
    shown = shown_ref[0, 0]

    def one_step(step, carry):
        half_transmit, depth_sum, weight_sum = carry[0], carry[1], carry[2]
        values = density_ref[pl.ds(step, block_rows, stride=sample_count), :]
        optical = scale * jnp.log1p(jnp.exp(values))
        passed = jnp.exp(-optical)
        half_weight = half_transmit * (1.0 - passed)
        colours = tuple(
            carry[3 + channel] + half_weight * jnp.tanh(half_slopes[channel] * values + half_offsets[channel])
            for channel in range(3)
        )
        return (half_transmit * passed, depth_sum + optical, weight_sum + half_weight) + colours

    zeros = jnp.zeros((block_rows, pixels), jnp.float32)
    carry = (jnp.full((block_rows, pixels), 0.5, jnp.float32), zeros, zeros, zeros, zeros, zeros)
    carry = lax.fori_loop(0, sample_count, one_step, carry, unroll=32)
    row_ids = pl.program_id(0) * block_rows + lax.broadcasted_iota(jnp.int32, (block_rows, pixels), 0)
    visible = row_ids < shown
    for channel in range(3):
        out_ref[:, channel, :] = jnp.where(visible, carry[2] + carry[3 + channel], 0.0)
    out_ref[:, 3, :] = jnp.where(visible, carry[1], 0.0)


def render_layers(density_block, shown_rows, absorb, colour_slope, colour_offset, slot, block_rows=16):
    brick_rows, sample_count, pixels = density_block.shape
    return pl.pallas_call(
        render_kernel,
        grid=(brick_rows // block_rows,),
        in_specs=[
            pl.BlockSpec(memory_space=pltpu.SMEM),
            pl.BlockSpec(memory_space=pltpu.SMEM),
            pl.BlockSpec(memory_space=pltpu.SMEM),
            pl.BlockSpec(memory_space=pltpu.SMEM),
            pl.BlockSpec((block_rows * sample_count, pixels), lambda i: (i, 0)),
            pl.BlockSpec(memory_space=pl.ANY),
        ],
        out_specs=pl.BlockSpec((block_rows, 4, pixels), lambda i: (i, 0, 0)),
        out_shape=jax.ShapeDtypeStruct(slot.shape, jnp.float32),
        input_output_aliases={5: 0},
    )(absorb, colour_slope, colour_offset, shown_rows, density_block.reshape(brick_rows * sample_count, pixels),
      slot)


def composite_rows(flat, starts, counts, brick_ids, stride, image_rows):
    slot_count = starts.shape[0]
    offset = image_rows[:, None] - starts[None, :]
    covered = (offset >= 0) & (offset < counts[None, :])
    depth_ids = brick_ids[None, :]
    slot_ids = jnp.arange(slot_count, dtype=jnp.int32)[None, :]
    back = jnp.max(jnp.where(covered, depth_ids, -1), axis=1)
    is_back = (depth_ids == back[:, None]) & covered
    is_front = (depth_ids == back[:, None] - 1) & covered
    back_off = jnp.sum(jnp.where(is_back, offset, 0), axis=1)
    front_off = jnp.sum(jnp.where(is_front, offset, 0), axis=1)
    back_slot = jnp.sum(jnp.where(is_back, slot_ids, 0), axis=1)
    front_slot = jnp.sum(jnp.where(is_front, slot_ids, 0), axis=1)
    has_front = jnp.any(is_front, axis=1)
    has_back = back >= 0
    zero_row = stride - 1
    back_idx = jnp.where(has_back, back_slot * stride + back_off, zero_row)
    front_idx = jnp.where(has_front, front_slot * stride + front_off, zero_row)
    back_rows = jnp.take(flat, back_idx, axis=0, mode="clip")
    front_rows = jnp.take(flat, front_idx, axis=0, mode="clip")
    front_depth = front_rows[:, 3:4, :]
    colours = front_rows[:, :3, :] + jnp.exp(-front_depth) * back_rows[:, :3, :]
    opacity = 1.0 - jnp.exp(-(front_depth + back_rows[:, 3:4, :]))
    return jnp.concatenate([colours, opacity], axis=1)


def ring_order(count):
    return list(range(0, count, 2)) + list(range(count - 1 - count % 2, 0, -2))


def ring_gather(own, count):
    order = ring_order(count)
    forward = [(order[k], order[(k + 1) % count]) for k in range(count)]
    backward = [(b, a) for a, b in forward]
    slots = [own]
    ahead = own
    behind = own
    for step in range(1, count // 2 + 1):
        ahead = lax.ppermute(ahead, "depth", forward)
        slots.append(ahead)
        if 2 * step < count:
            behind = lax.ppermute(behind, "depth", backward)
            slots.append(behind)
    return jnp.concatenate(slots, axis=0)


def on_device(density, foot_start, foot_rows, extinction, colour_slope, colour_offset, tile_source):
    depth_count = lax.axis_size("depth")
    screen_count = lax.axis_size("screen")
    depth_index = lax.axis_index("depth")
    screen_index = lax.axis_index("screen")
    image_total = tile_source.shape[0]
    half_rows = image_total // screen_count
    owner_rows = image_total // (depth_count * screen_count)
    start = foot_start[0, 0]
    shown = foot_rows[0, 0]
    brick_rows, pixels = density.shape[2], density.shape[4]
    channels = 4
    stride = brick_rows + 2
    meta = jnp.stack([start, shown, depth_index.astype(start.dtype)]).astype(jnp.float32)
    slot = lax.dynamic_update_slice(jnp.zeros((stride, channels, pixels), jnp.float32),
                                    meta.reshape(1, 1, 3), (brick_rows, 0, 0))
    own = render_layers(density[0, 0], foot_rows, extinction, colour_slope, colour_offset, slot)
    flat = ring_gather(own, depth_count)
    meta_rows = flat.reshape(depth_count, stride, channels, pixels)[:, brick_rows, 0, :3]
    starts = meta_rows[:, 0].astype(jnp.int32)
    counts = meta_rows[:, 1].astype(jnp.int32)
    brick_ids = meta_rows[:, 2].astype(jnp.int32)
    self_owner = depth_index * screen_count + screen_index
    partner_owner = depth_index * screen_count + (1 - screen_index)
    wanted_self = lax.dynamic_slice_in_dim(tile_source, self_owner * owner_rows, owner_rows)
    wanted_partner = lax.dynamic_slice_in_dim(tile_source, partner_owner * owner_rows, owner_rows)
    wanted = jnp.concatenate([wanted_self, wanted_partner])
    rows = composite_rows(flat, starts, counts, brick_ids, stride, wanted % half_rows)
    mine = rows[:owner_rows]
    for_partner = rows[owner_rows:]
    received = lax.ppermute(for_partner, "screen", [(0, 1), (1, 0)])
    in_my_half = (wanted_self // half_rows) == screen_index
    return jnp.where(in_my_half[:, None, None], mine, received)


def solution(mesh):
    return jax.shard_map(
        on_device,
        mesh=mesh,
        in_specs=(
            P(("runs", "depth"), "screen", None, None, None),
            P(("runs", "depth"), "screen"),
            P(("runs", "depth"), "screen"),
            P("runs"),
            P(),
            P(),
            P("runs"),
        ),
        out_specs=P(("runs", "depth", "screen"), None, None),
        check_vma=False,
    )
```

```python
import jax
import jax.numpy as jnp
from jax import lax
from jax.sharding import PartitionSpec as P
from jax.experimental import pallas as pl
from jax.experimental.pallas import tpu as pltpu

BLK = 256


def render_kernel(absorb_ref, slope_ref, offset_ref, shown_ref, density_ref, slot_ref, out_ref):
    del slot_ref
    block_rows = out_ref.shape[0]
    pixels = out_ref.shape[2]
    sample_count = density_ref.shape[0] // block_rows
    scale = absorb_ref[0] / sample_count
    half_slopes = [0.5 * slope_ref[channel] for channel in range(3)]
    half_offsets = [0.5 * offset_ref[channel] for channel in range(3)]
    shown = shown_ref[0, 0]

    def one_step(step, carry):
        half_transmit, depth_sum, weight_sum = carry[0], carry[1], carry[2]
        values = density_ref[pl.ds(step, block_rows, stride=sample_count), :]
        optical = scale * jnp.log1p(jnp.exp(values))
        passed = jnp.exp(-optical)
        half_weight = half_transmit * (1.0 - passed)
        colours = tuple(
            carry[3 + channel] + half_weight * jnp.tanh(half_slopes[channel] * values + half_offsets[channel])
            for channel in range(3)
        )
        return (half_transmit * passed, depth_sum + optical, weight_sum + half_weight) + colours

    zeros = jnp.zeros((block_rows, pixels), jnp.float32)
    carry = (jnp.full((block_rows, pixels), 0.5, jnp.float32), zeros, zeros, zeros, zeros, zeros)
    carry = lax.fori_loop(0, sample_count, one_step, carry, unroll=32)
    row_ids = pl.program_id(0) * block_rows + lax.broadcasted_iota(jnp.int32, (block_rows, pixels), 0)
    visible = row_ids < shown
    for channel in range(3):
        out_ref[:, channel, :] = jnp.where(visible, carry[2] + carry[3 + channel], 0.0)
    out_ref[:, 3, :] = jnp.where(visible, carry[1], 0.0)


def render_layers(density_block, shown_rows, absorb, colour_slope, colour_offset, slot, block_rows=16):
    brick_rows, sample_count, pixels = density_block.shape
    return pl.pallas_call(
        render_kernel,
        grid=(brick_rows // block_rows,),
        in_specs=[
            pl.BlockSpec(memory_space=pltpu.SMEM),
            pl.BlockSpec(memory_space=pltpu.SMEM),
            pl.BlockSpec(memory_space=pltpu.SMEM),
            pl.BlockSpec(memory_space=pltpu.SMEM),
            pl.BlockSpec((block_rows * sample_count, pixels), lambda i: (i, 0)),
            pl.BlockSpec(memory_space=pl.ANY),
        ],
        out_specs=pl.BlockSpec((block_rows, 4, pixels), lambda i: (i, 0, 0)),
        out_shape=jax.ShapeDtypeStruct(slot.shape, jnp.float32),
        input_output_aliases={5: 0},
    )(absorb, colour_slope, colour_offset, shown_rows, density_block.reshape(brick_rows * sample_count, pixels),
      slot)


def composite_rows(flat, starts, counts, brick_ids, stride, image_rows):
    slot_count = starts.shape[0]
    offset = image_rows[:, None] - starts[None, :]
    covered = (offset >= 0) & (offset < counts[None, :])
    depth_ids = brick_ids[None, :]
    slot_ids = jnp.arange(slot_count, dtype=jnp.int32)[None, :]
    back = jnp.max(jnp.where(covered, depth_ids, -1), axis=1)
    is_back = (depth_ids == back[:, None]) & covered
    is_front = (depth_ids == back[:, None] - 1) & covered
    back_off = jnp.sum(jnp.where(is_back, offset, 0), axis=1)
    front_off = jnp.sum(jnp.where(is_front, offset, 0), axis=1)
    back_slot = jnp.sum(jnp.where(is_back, slot_ids, 0), axis=1)
    front_slot = jnp.sum(jnp.where(is_front, slot_ids, 0), axis=1)
    has_front = jnp.any(is_front, axis=1)
    has_back = back >= 0
    zero_row = stride - 1
    back_idx = jnp.where(has_back, back_slot * stride + back_off, zero_row)
    front_idx = jnp.where(has_front, front_slot * stride + front_off, zero_row)
    picked = jnp.take(flat, jnp.concatenate([back_idx, front_idx]), axis=0, mode="clip")
    back_rows, front_rows = picked[:back_idx.shape[0]], picked[back_idx.shape[0]:]
    front_depth = front_rows[:, 3:4, :]
    colours = front_rows[:, :3, :] + jnp.exp(-front_depth) * back_rows[:, :3, :]
    opacity = 1.0 - jnp.exp(-(front_depth + back_rows[:, 3:4, :]))
    return jnp.concatenate([colours, opacity], axis=1)


def ring_order(count):
    return list(range(0, count, 2)) + list(range(count - 1 - count % 2, 0, -2))


def ring_gather(own, count):
    order = ring_order(count)
    forward = [(order[k], order[(k + 1) % count]) for k in range(count)]
    backward = [(b, a) for a, b in forward]
    slots = [own]
    ahead = own
    behind = own
    for step in range(1, count // 2 + 1):
        ahead = lax.ppermute(ahead, "depth", forward)
        slots.append(ahead)
        if 2 * step < count:
            behind = lax.ppermute(behind, "depth", backward)
            slots.append(behind)
    return jnp.concatenate(slots, axis=0)


def on_device(density, foot_start, foot_rows, extinction, colour_slope, colour_offset, tile_source):
    depth_count = lax.axis_size("depth")
    screen_count = lax.axis_size("screen")
    depth_index = lax.axis_index("depth")
    screen_index = lax.axis_index("screen")
    image_total = tile_source.shape[0]
    half_rows = image_total // screen_count
    owner_rows = image_total // (depth_count * screen_count)
    start = foot_start[0, 0]
    shown = foot_rows[0, 0]
    brick_rows, pixels = density.shape[2], density.shape[4]
    channels = 4
    stride = brick_rows + 2
    meta = jnp.stack([start, shown, depth_index.astype(start.dtype)]).astype(jnp.float32)
    slot = lax.dynamic_update_slice(jnp.zeros((stride, channels, pixels), jnp.float32),
                                    meta.reshape(1, 1, 3), (brick_rows, 0, 0))
    own = render_layers(density[0, 0], foot_rows, extinction, colour_slope, colour_offset, slot)
    flat = ring_gather(own, depth_count)
    meta_rows = flat.reshape(depth_count, stride, channels, pixels)[:, brick_rows, 0, :3]
    starts = meta_rows[:, 0].astype(jnp.int32)
    counts = meta_rows[:, 1].astype(jnp.int32)
    brick_ids = meta_rows[:, 2].astype(jnp.int32)
    self_owner = depth_index * screen_count + screen_index
    partner_owner = depth_index * screen_count + (1 - screen_index)
    wanted_self = lax.dynamic_slice_in_dim(tile_source, self_owner * owner_rows, owner_rows)
    wanted_partner = lax.dynamic_slice_in_dim(tile_source, partner_owner * owner_rows, owner_rows)
    wanted = jnp.concatenate([wanted_self, wanted_partner])
    rows = composite_rows(flat, starts, counts, brick_ids, stride, wanted % half_rows)
    mine = rows[:owner_rows]
    for_partner = rows[owner_rows:]
    received = lax.ppermute(for_partner, "screen", [(0, 1), (1, 0)])
    in_my_half = (wanted_self // half_rows) == screen_index
    return jnp.where(in_my_half[:, None, None], mine, received)


def solution(mesh):
    return jax.shard_map(
        on_device,
        mesh=mesh,
        in_specs=(
            P(("runs", "depth"), "screen", None, None, None),
            P(("runs", "depth"), "screen"),
            P(("runs", "depth"), "screen"),
            P("runs"),
            P(),
            P(),
            P("runs"),
        ),
        out_specs=P(("runs", "depth", "screen"), None, None),
        check_vma=False,
    )
```

```python
import jax
import jax.numpy as jnp
from jax import lax
from jax.sharding import PartitionSpec as P
from jax.experimental import pallas as pl
from jax.experimental.pallas import tpu as pltpu

BLK = 256


def render_kernel(absorb_ref, slope_ref, offset_ref, shown_ref, density_ref, slot_ref, out_ref):
    del slot_ref
    block_rows = out_ref.shape[0]
    pixels = out_ref.shape[2]
    sample_count = density_ref.shape[0] // block_rows
    scale = absorb_ref[0] / sample_count
    half_slopes = [0.5 * slope_ref[channel] for channel in range(3)]
    half_offsets = [0.5 * offset_ref[channel] for channel in range(3)]
    shown = shown_ref[0, 0]

    def one_step(step, carry):
        half_transmit, depth_sum, weight_sum = carry[0], carry[1], carry[2]
        values = density_ref[pl.ds(step, block_rows, stride=sample_count), :]
        optical = scale * jnp.log1p(jnp.exp(values))
        passed = jnp.exp(-optical)
        half_weight = half_transmit * (1.0 - passed)
        colours = tuple(
            carry[3 + channel] + half_weight * jnp.tanh(half_slopes[channel] * values + half_offsets[channel])
            for channel in range(3)
        )
        return (half_transmit * passed, depth_sum + optical, weight_sum + half_weight) + colours

    zeros = jnp.zeros((block_rows, pixels), jnp.float32)
    carry = (jnp.full((block_rows, pixels), 0.5, jnp.float32), zeros, zeros, zeros, zeros, zeros)
    carry = lax.fori_loop(0, sample_count, one_step, carry, unroll=32)
    row_ids = pl.program_id(0) * block_rows + lax.broadcasted_iota(jnp.int32, (block_rows, pixels), 0)
    visible = row_ids < shown
    for channel in range(3):
        out_ref[:, channel, :] = jnp.where(visible, carry[2] + carry[3 + channel], 0.0)
    out_ref[:, 3, :] = jnp.where(visible, carry[1], 0.0)


def render_layers(density_block, shown_rows, absorb, colour_slope, colour_offset, slot, block_rows=16):
    brick_rows, sample_count, pixels = density_block.shape
    return pl.pallas_call(
        render_kernel,
        grid=(brick_rows // block_rows,),
        in_specs=[
            pl.BlockSpec(memory_space=pltpu.SMEM),
            pl.BlockSpec(memory_space=pltpu.SMEM),
            pl.BlockSpec(memory_space=pltpu.SMEM),
            pl.BlockSpec(memory_space=pltpu.SMEM),
            pl.BlockSpec((block_rows * sample_count, pixels), lambda i: (i, 0)),
            pl.BlockSpec(memory_space=pl.ANY),
        ],
        out_specs=pl.BlockSpec((block_rows, 4, pixels), lambda i: (i, 0, 0)),
        out_shape=jax.ShapeDtypeStruct(slot.shape, jnp.float32),
        input_output_aliases={5: 0},
    )(absorb, colour_slope, colour_offset, shown_rows, density_block.reshape(brick_rows * sample_count, pixels),
      slot)


def composite_rows(flat, starts, counts, brick_ids, stride, image_rows):
    slot_count = starts.shape[0]
    offset = image_rows[:, None] - starts[None, :]
    covered = (offset >= 0) & (offset < counts[None, :])
    depth_ids = brick_ids[None, :]
    slot_ids = jnp.arange(slot_count, dtype=jnp.int32)[None, :]
    back = jnp.max(jnp.where(covered, depth_ids, -1), axis=1)
    is_back = (depth_ids == back[:, None]) & covered
    is_front = (depth_ids == back[:, None] - 1) & covered
    back_off = jnp.sum(jnp.where(is_back, offset, 0), axis=1)
    front_off = jnp.sum(jnp.where(is_front, offset, 0), axis=1)
    back_slot = jnp.sum(jnp.where(is_back, slot_ids, 0), axis=1)
    front_slot = jnp.sum(jnp.where(is_front, slot_ids, 0), axis=1)
    has_front = jnp.any(is_front, axis=1)
    has_back = back >= 0
    zero_row = stride - 1
    back_idx = jnp.where(has_back, back_slot * stride + back_off, zero_row)
    front_idx = jnp.where(has_front, front_slot * stride + front_off, zero_row)
    back_rows = jnp.take(flat, back_idx, axis=0, mode="clip")
    front_rows = jnp.take(flat, front_idx, axis=0, mode="clip")
    front_depth = front_rows[:, 3:4, :]
    colours = front_rows[:, :3, :] + jnp.exp(-front_depth) * back_rows[:, :3, :]
    opacity = 1.0 - jnp.exp(-(front_depth + back_rows[:, 3:4, :]))
    return jnp.concatenate([colours, opacity], axis=1)


def ring_order(count):
    return list(range(0, count, 2)) + list(range(count - 1 - count % 2, 0, -2))


def ring_gather(own, count):
    order = ring_order(count)
    forward = [(order[k], order[(k + 1) % count]) for k in range(count)]
    backward = [(b, a) for a, b in forward]
    slots = [own]
    ahead = own
    behind = own
    for step in range(1, count // 2 + 1):
        ahead = lax.ppermute(ahead, "depth", forward)
        slots.append(ahead)
        if 2 * step < count:
            behind = lax.ppermute(behind, "depth", backward)
            slots.append(behind)
    return jnp.concatenate(slots, axis=0)


def on_device(density, foot_start, foot_rows, extinction, colour_slope, colour_offset, tile_source):
    depth_count = lax.axis_size("depth")
    screen_count = lax.axis_size("screen")
    depth_index = lax.axis_index("depth")
    screen_index = lax.axis_index("screen")
    image_total = tile_source.shape[0]
    half_rows = image_total // screen_count
    owner_rows = image_total // (depth_count * screen_count)
    start = foot_start[0, 0]
    shown = foot_rows[0, 0]
    brick_rows, pixels = density.shape[2], density.shape[4]
    channels = 4
    stride = brick_rows + 2
    meta = jnp.stack([start, shown, depth_index.astype(start.dtype)]).astype(jnp.float32)
    slot = lax.dynamic_update_slice(jnp.zeros((stride, channels, pixels), jnp.float32),
                                    meta.reshape(1, 1, 3), (brick_rows, 0, 0))
    own = render_layers(density[0, 0], foot_rows, extinction, colour_slope, colour_offset, slot)
    flat = ring_gather(own, depth_count)
    meta_rows = flat.reshape(depth_count, stride, channels, pixels)[:, brick_rows, 0, :3]
    starts = meta_rows[:, 0].astype(jnp.int32)
    counts = meta_rows[:, 1].astype(jnp.int32)
    brick_ids = meta_rows[:, 2].astype(jnp.int32)
    self_owner = depth_index * screen_count + screen_index
    partner_owner = depth_index * screen_count + (1 - screen_index)
    wanted_self = lax.dynamic_slice_in_dim(tile_source, self_owner * owner_rows, owner_rows)
    wanted_partner = lax.dynamic_slice_in_dim(tile_source, partner_owner * owner_rows, owner_rows)
    for_partner = composite_rows(flat, starts, counts, brick_ids, stride, wanted_partner % half_rows)
    received = lax.ppermute(for_partner, "screen", [(0, 1), (1, 0)])
    flat, for_partner = lax.optimization_barrier((flat, for_partner))
    mine = composite_rows(flat, starts, counts, brick_ids, stride, wanted_self % half_rows)
    in_my_half = (wanted_self // half_rows) == screen_index
    return jnp.where(in_my_half[:, None, None], mine, received)


def solution(mesh):
    return jax.shard_map(
        on_device,
        mesh=mesh,
        in_specs=(
            P(("runs", "depth"), "screen", None, None, None),
            P(("runs", "depth"), "screen"),
            P(("runs", "depth"), "screen"),
            P("runs"),
            P(),
            P(),
            P("runs"),
        ),
        out_specs=P(("runs", "depth", "screen"), None, None),
        check_vma=False,
    )
```

```python
import jax
import jax.numpy as jnp
from jax import lax
from jax.sharding import PartitionSpec as P
from jax.experimental import pallas as pl
from jax.experimental.pallas import tpu as pltpu

BLK = 256


def render_kernel(absorb_ref, slope_ref, offset_ref, shown_ref, density_ref, slot_ref, out_ref):
    del slot_ref
    block_rows = out_ref.shape[0]
    pixels = out_ref.shape[2]
    sample_count = density_ref.shape[0] // block_rows
    scale = absorb_ref[0] / sample_count
    half_slopes = [0.5 * slope_ref[channel] for channel in range(3)]
    half_offsets = [0.5 * offset_ref[channel] for channel in range(3)]
    shown = shown_ref[0, 0]

    def one_step(step, carry):
        half_transmit, depth_sum, weight_sum = carry[0], carry[1], carry[2]
        values = density_ref[pl.ds(step, block_rows, stride=sample_count), :]
        optical = scale * jnp.log1p(jnp.exp(values))
        passed = jnp.exp(-optical)
        half_weight = half_transmit * (1.0 - passed)
        colours = tuple(
            carry[3 + channel] + half_weight * jnp.tanh(half_slopes[channel] * values + half_offsets[channel])
            for channel in range(3)
        )
        return (half_transmit * passed, depth_sum + optical, weight_sum + half_weight) + colours

    zeros = jnp.zeros((block_rows, pixels), jnp.float32)
    carry = (jnp.full((block_rows, pixels), 0.5, jnp.float32), zeros, zeros, zeros, zeros, zeros)
    carry = lax.fori_loop(0, sample_count, one_step, carry, unroll=64)
    row_ids = pl.program_id(0) * block_rows + lax.broadcasted_iota(jnp.int32, (block_rows, pixels), 0)
    visible = row_ids < shown
    for channel in range(3):
        out_ref[:, channel, :] = jnp.where(visible, carry[2] + carry[3 + channel], 0.0)
    out_ref[:, 3, :] = jnp.where(visible, carry[1], 0.0)


def render_layers(density_block, shown_rows, absorb, colour_slope, colour_offset, slot, block_rows=16):
    brick_rows, sample_count, pixels = density_block.shape
    return pl.pallas_call(
        render_kernel,
        grid=(brick_rows // block_rows,),
        in_specs=[
            pl.BlockSpec(memory_space=pltpu.SMEM),
            pl.BlockSpec(memory_space=pltpu.SMEM),
            pl.BlockSpec(memory_space=pltpu.SMEM),
            pl.BlockSpec(memory_space=pltpu.SMEM),
            pl.BlockSpec((block_rows * sample_count, pixels), lambda i: (i, 0)),
            pl.BlockSpec(memory_space=pl.ANY),
        ],
        out_specs=pl.BlockSpec((block_rows, 4, pixels), lambda i: (i, 0, 0)),
        out_shape=jax.ShapeDtypeStruct(slot.shape, jnp.float32),
        input_output_aliases={5: 0},
    )(absorb, colour_slope, colour_offset, shown_rows, density_block.reshape(brick_rows * sample_count, pixels),
      slot)


def composite_rows(flat, starts, counts, brick_ids, stride, image_rows):
    slot_count = starts.shape[0]
    offset = image_rows[:, None] - starts[None, :]
    covered = (offset >= 0) & (offset < counts[None, :])
    depth_ids = brick_ids[None, :]
    slot_ids = jnp.arange(slot_count, dtype=jnp.int32)[None, :]
    back = jnp.max(jnp.where(covered, depth_ids, -1), axis=1)
    is_back = (depth_ids == back[:, None]) & covered
    is_front = (depth_ids == back[:, None] - 1) & covered
    back_off = jnp.sum(jnp.where(is_back, offset, 0), axis=1)
    front_off = jnp.sum(jnp.where(is_front, offset, 0), axis=1)
    back_slot = jnp.sum(jnp.where(is_back, slot_ids, 0), axis=1)
    front_slot = jnp.sum(jnp.where(is_front, slot_ids, 0), axis=1)
    has_front = jnp.any(is_front, axis=1)
    has_back = back >= 0
    zero_row = stride - 1
    back_idx = jnp.where(has_back, back_slot * stride + back_off, zero_row)
    front_idx = jnp.where(has_front, front_slot * stride + front_off, zero_row)
    back_rows = jnp.take(flat, back_idx, axis=0, mode="clip")
    front_rows = jnp.take(flat, front_idx, axis=0, mode="clip")
    front_depth = front_rows[:, 3:4, :]
    colours = front_rows[:, :3, :] + jnp.exp(-front_depth) * back_rows[:, :3, :]
    opacity = 1.0 - jnp.exp(-(front_depth + back_rows[:, 3:4, :]))
    return jnp.concatenate([colours, opacity], axis=1)


def ring_order(count):
    return list(range(0, count, 2)) + list(range(count - 1 - count % 2, 0, -2))


def ring_gather(own, count):
    order = ring_order(count)
    forward = [(order[k], order[(k + 1) % count]) for k in range(count)]
    backward = [(b, a) for a, b in forward]
    slots = [own]
    ahead = own
    behind = own
    for step in range(1, count // 2 + 1):
        ahead = lax.ppermute(ahead, "depth", forward)
        slots.append(ahead)
        if 2 * step < count:
            behind = lax.ppermute(behind, "depth", backward)
            slots.append(behind)
    return jnp.concatenate(slots, axis=0)


def on_device(density, foot_start, foot_rows, extinction, colour_slope, colour_offset, tile_source):
    depth_count = lax.axis_size("depth")
    screen_count = lax.axis_size("screen")
    depth_index = lax.axis_index("depth")
    screen_index = lax.axis_index("screen")
    image_total = tile_source.shape[0]
    half_rows = image_total // screen_count
    owner_rows = image_total // (depth_count * screen_count)
    start = foot_start[0, 0]
    shown = foot_rows[0, 0]
    brick_rows, pixels = density.shape[2], density.shape[4]
    channels = 4
    stride = brick_rows + 2
    meta = jnp.stack([start, shown, depth_index.astype(start.dtype)]).astype(jnp.float32)
    slot = lax.dynamic_update_slice(jnp.zeros((stride, channels, pixels), jnp.float32),
                                    meta.reshape(1, 1, 3), (brick_rows, 0, 0))
    own = render_layers(density[0, 0], foot_rows, extinction, colour_slope, colour_offset, slot)
    flat = ring_gather(own, depth_count)
    meta_rows = flat.reshape(depth_count, stride, channels, pixels)[:, brick_rows, 0, :3]
    starts = meta_rows[:, 0].astype(jnp.int32)
    counts = meta_rows[:, 1].astype(jnp.int32)
    brick_ids = meta_rows[:, 2].astype(jnp.int32)
    self_owner = depth_index * screen_count + screen_index
    partner_owner = depth_index * screen_count + (1 - screen_index)
    wanted_self = lax.dynamic_slice_in_dim(tile_source, self_owner * owner_rows, owner_rows)
    wanted_partner = lax.dynamic_slice_in_dim(tile_source, partner_owner * owner_rows, owner_rows)
    for_partner = composite_rows(flat, starts, counts, brick_ids, stride, wanted_partner % half_rows)
    received = lax.ppermute(for_partner, "screen", [(0, 1), (1, 0)])
    flat, for_partner = lax.optimization_barrier((flat, for_partner))
    mine = composite_rows(flat, starts, counts, brick_ids, stride, wanted_self % half_rows)
    in_my_half = (wanted_self // half_rows) == screen_index
    return jnp.where(in_my_half[:, None, None], mine, received)


def solution(mesh):
    return jax.shard_map(
        on_device,
        mesh=mesh,
        in_specs=(
            P(("runs", "depth"), "screen", None, None, None),
            P(("runs", "depth"), "screen"),
            P(("runs", "depth"), "screen"),
            P("runs"),
            P(),
            P(),
            P("runs"),
        ),
        out_specs=P(("runs", "depth", "screen"), None, None),
        check_vma=False,
    )
```

```python
import jax
import jax.numpy as jnp
from jax import lax
from jax.sharding import PartitionSpec as P
from jax.experimental import pallas as pl
from jax.experimental.pallas import tpu as pltpu

BLK = 256


def render_kernel(absorb_ref, slope_ref, offset_ref, shown_ref, density_ref, slot_ref, out_ref):
    del slot_ref
    block_rows = out_ref.shape[0]
    pixels = out_ref.shape[2]
    sample_count = density_ref.shape[0] // block_rows
    scale = absorb_ref[0] / sample_count
    half_slopes = [0.5 * slope_ref[channel] for channel in range(3)]
    half_offsets = [0.5 * offset_ref[channel] for channel in range(3)]
    shown = shown_ref[0, 0]

    def one_step(step, carry):
        half_transmit, depth_sum, weight_sum = carry[0], carry[1], carry[2]
        values = density_ref[pl.ds(step, block_rows, stride=sample_count), :]
        optical = scale * jnp.log1p(jnp.exp(values))
        passed = jnp.exp(-optical)
        half_weight = half_transmit * (1.0 - passed)
        colours = tuple(
            carry[3 + channel] + half_weight * jnp.tanh(half_slopes[channel] * values + half_offsets[channel])
            for channel in range(3)
        )
        return (half_transmit * passed, depth_sum + optical, weight_sum + half_weight) + colours

    zeros = jnp.zeros((block_rows, pixels), jnp.float32)
    carry = (jnp.full((block_rows, pixels), 0.5, jnp.float32), zeros, zeros, zeros, zeros, zeros)
    carry = lax.fori_loop(0, sample_count, one_step, carry, unroll=64)
    row_ids = pl.program_id(0) * block_rows + lax.broadcasted_iota(jnp.int32, (block_rows, pixels), 0)
    visible = row_ids < shown
    for channel in range(3):
        out_ref[:, channel, :] = jnp.where(visible, carry[2] + carry[3 + channel], 0.0)
    out_ref[:, 3, :] = jnp.where(visible, carry[1], 0.0)


def render_layers(density_block, shown_rows, absorb, colour_slope, colour_offset, slot, block_rows=16):
    brick_rows, sample_count, pixels = density_block.shape
    return pl.pallas_call(
        render_kernel,
        grid=(brick_rows // block_rows,),
        in_specs=[
            pl.BlockSpec(memory_space=pltpu.SMEM),
            pl.BlockSpec(memory_space=pltpu.SMEM),
            pl.BlockSpec(memory_space=pltpu.SMEM),
            pl.BlockSpec(memory_space=pltpu.SMEM),
            pl.BlockSpec((block_rows * sample_count, pixels), lambda i: (i, 0)),
            pl.BlockSpec(memory_space=pl.ANY),
        ],
        out_specs=pl.BlockSpec((block_rows, 4, pixels), lambda i: (i, 0, 0)),
        out_shape=jax.ShapeDtypeStruct(slot.shape, jnp.float32),
        input_output_aliases={5: 0},
    )(absorb, colour_slope, colour_offset, shown_rows, density_block.reshape(brick_rows * sample_count, pixels),
      slot)


def composite_rows(flat, starts, counts, brick_ids, stride, image_rows):
    slot_count = starts.shape[0]
    offset = image_rows[:, None] - starts[None, :]
    covered = (offset >= 0) & (offset < counts[None, :])
    depth_ids = brick_ids[None, :]
    slot_ids = jnp.arange(slot_count, dtype=jnp.int32)[None, :]
    back = jnp.max(jnp.where(covered, depth_ids, -1), axis=1)
    is_back = (depth_ids == back[:, None]) & covered
    is_front = (depth_ids == back[:, None] - 1) & covered
    back_off = jnp.sum(jnp.where(is_back, offset, 0), axis=1)
    front_off = jnp.sum(jnp.where(is_front, offset, 0), axis=1)
    back_slot = jnp.sum(jnp.where(is_back, slot_ids, 0), axis=1)
    front_slot = jnp.sum(jnp.where(is_front, slot_ids, 0), axis=1)
    has_front = jnp.any(is_front, axis=1)
    has_back = back >= 0
    zero_row = stride - 1
    back_idx = jnp.where(has_back, back_slot * stride + back_off, zero_row)
    front_idx = jnp.where(has_front, front_slot * stride + front_off, zero_row)
    back_rows = jnp.take(flat, back_idx, axis=0, mode="clip")
    front_rows = jnp.take(flat, front_idx, axis=0, mode="clip")
    front_depth = front_rows[:, 3:4, :]
    is_colour = lax.broadcasted_iota(jnp.int32, front_rows.shape, 1) < 3
    colours = front_rows + jnp.exp(-front_depth) * back_rows
    opacity = 1.0 - jnp.exp(-(front_depth + back_rows[:, 3:4, :]))
    return jnp.where(is_colour, colours, opacity)


def ring_order(count):
    return list(range(0, count, 2)) + list(range(count - 1 - count % 2, 0, -2))


def ring_gather(own, count):
    order = ring_order(count)
    forward = [(order[k], order[(k + 1) % count]) for k in range(count)]
    backward = [(b, a) for a, b in forward]
    slots = [own]
    ahead = own
    behind = own
    for step in range(1, count // 2 + 1):
        ahead = lax.ppermute(ahead, "depth", forward)
        slots.append(ahead)
        if 2 * step < count:
            behind = lax.ppermute(behind, "depth", backward)
            slots.append(behind)
    return jnp.concatenate(slots, axis=0)


def on_device(density, foot_start, foot_rows, extinction, colour_slope, colour_offset, tile_source):
    depth_count = lax.axis_size("depth")
    screen_count = lax.axis_size("screen")
    depth_index = lax.axis_index("depth")
    screen_index = lax.axis_index("screen")
    image_total = tile_source.shape[0]
    half_rows = image_total // screen_count
    owner_rows = image_total // (depth_count * screen_count)
    start = foot_start[0, 0]
    shown = foot_rows[0, 0]
    brick_rows, pixels = density.shape[2], density.shape[4]
    channels = 4
    stride = brick_rows + 2
    meta = jnp.stack([start, shown, depth_index.astype(start.dtype)]).astype(jnp.float32)
    slot = lax.dynamic_update_slice(jnp.zeros((stride, channels, pixels), jnp.float32),
                                    meta.reshape(1, 1, 3), (brick_rows, 0, 0))
    own = render_layers(density[0, 0], foot_rows, extinction, colour_slope, colour_offset, slot)
    flat = ring_gather(own, depth_count)
    meta_rows = flat.reshape(depth_count, stride, channels, pixels)[:, brick_rows, 0, :3]
    starts = meta_rows[:, 0].astype(jnp.int32)
    counts = meta_rows[:, 1].astype(jnp.int32)
    brick_ids = meta_rows[:, 2].astype(jnp.int32)
    self_owner = depth_index * screen_count + screen_index
    partner_owner = depth_index * screen_count + (1 - screen_index)
    wanted_self = lax.dynamic_slice_in_dim(tile_source, self_owner * owner_rows, owner_rows)
    wanted_partner = lax.dynamic_slice_in_dim(tile_source, partner_owner * owner_rows, owner_rows)
    for_partner = composite_rows(flat, starts, counts, brick_ids, stride, wanted_partner % half_rows)
    received = lax.ppermute(for_partner, "screen", [(0, 1), (1, 0)])
    flat, for_partner = lax.optimization_barrier((flat, for_partner))
    mine = composite_rows(flat, starts, counts, brick_ids, stride, wanted_self % half_rows)
    in_my_half = (wanted_self // half_rows) == screen_index
    return jnp.where(in_my_half[:, None, None], mine, received)


def solution(mesh):
    return jax.shard_map(
        on_device,
        mesh=mesh,
        in_specs=(
            P(("runs", "depth"), "screen", None, None, None),
            P(("runs", "depth"), "screen"),
            P(("runs", "depth"), "screen"),
            P("runs"),
            P(),
            P(),
            P("runs"),
        ),
        out_specs=P(("runs", "depth", "screen"), None, None),
        check_vma=False,
    )
```

```python
import jax
import jax.numpy as jnp
from jax import lax
from jax.sharding import PartitionSpec as P
from jax.experimental import pallas as pl
from jax.experimental.pallas import tpu as pltpu

BLK = 256


def render_kernel(absorb_ref, slope_ref, offset_ref, shown_ref, density_ref, slot_ref, out_ref):
    del slot_ref
    block_rows = out_ref.shape[0]
    pixels = out_ref.shape[2]
    sample_count = density_ref.shape[0] // block_rows
    scale = absorb_ref[0] / sample_count
    half_slopes = [0.5 * slope_ref[channel] for channel in range(3)]
    half_offsets = [0.5 * offset_ref[channel] for channel in range(3)]
    shown = shown_ref[0, 0]

    def one_step(step, carry):
        half_transmit, depth_sum, weight_sum = carry[0], carry[1], carry[2]
        values = density_ref[pl.ds(step, block_rows, stride=sample_count), :]
        optical = scale * jnp.log1p(jnp.exp(values))
        passed = jnp.exp(-optical)
        half_weight = half_transmit * (1.0 - passed)
        colours = tuple(
            carry[3 + channel] + half_weight * jnp.tanh(half_slopes[channel] * values + half_offsets[channel])
            for channel in range(3)
        )
        return (half_transmit * passed, depth_sum + optical, weight_sum + half_weight) + colours

    zeros = jnp.zeros((block_rows, pixels), jnp.float32)
    carry = (jnp.full((block_rows, pixels), 0.5, jnp.float32), zeros, zeros, zeros, zeros, zeros)
    carry = lax.fori_loop(0, sample_count, one_step, carry, unroll=128)
    row_ids = pl.program_id(0) * block_rows + lax.broadcasted_iota(jnp.int32, (block_rows, pixels), 0)
    visible = row_ids < shown
    for channel in range(3):
        out_ref[:, channel, :] = jnp.where(visible, carry[2] + carry[3 + channel], 0.0)
    out_ref[:, 3, :] = jnp.where(visible, carry[1], 0.0)


def render_layers(density_block, shown_rows, absorb, colour_slope, colour_offset, slot, block_rows=16):
    brick_rows, sample_count, pixels = density_block.shape
    return pl.pallas_call(
        render_kernel,
        grid=(brick_rows // block_rows,),
        in_specs=[
            pl.BlockSpec(memory_space=pltpu.SMEM),
            pl.BlockSpec(memory_space=pltpu.SMEM),
            pl.BlockSpec(memory_space=pltpu.SMEM),
            pl.BlockSpec(memory_space=pltpu.SMEM),
            pl.BlockSpec((block_rows * sample_count, pixels), lambda i: (i, 0)),
            pl.BlockSpec(memory_space=pl.ANY),
        ],
        out_specs=pl.BlockSpec((block_rows, 4, pixels), lambda i: (i, 0, 0)),
        out_shape=jax.ShapeDtypeStruct(slot.shape, jnp.float32),
        input_output_aliases={5: 0},
    )(absorb, colour_slope, colour_offset, shown_rows, density_block.reshape(brick_rows * sample_count, pixels),
      slot)


def composite_rows(flat, starts, counts, brick_ids, stride, image_rows):
    slot_count = starts.shape[0]
    offset = image_rows[:, None] - starts[None, :]
    covered = (offset >= 0) & (offset < counts[None, :])
    depth_ids = brick_ids[None, :]
    slot_ids = jnp.arange(slot_count, dtype=jnp.int32)[None, :]
    back = jnp.max(jnp.where(covered, depth_ids, -1), axis=1)
    is_back = (depth_ids == back[:, None]) & covered
    is_front = (depth_ids == back[:, None] - 1) & covered
    back_off = jnp.sum(jnp.where(is_back, offset, 0), axis=1)
    front_off = jnp.sum(jnp.where(is_front, offset, 0), axis=1)
    back_slot = jnp.sum(jnp.where(is_back, slot_ids, 0), axis=1)
    front_slot = jnp.sum(jnp.where(is_front, slot_ids, 0), axis=1)
    has_front = jnp.any(is_front, axis=1)
    has_back = back >= 0
    zero_row = stride - 1
    back_idx = jnp.where(has_back, back_slot * stride + back_off, zero_row)
    front_idx = jnp.where(has_front, front_slot * stride + front_off, zero_row)
    back_rows = jnp.take(flat, back_idx, axis=0, mode="clip")
    front_rows = jnp.take(flat, front_idx, axis=0, mode="clip")
    front_depth = front_rows[:, 3:4, :]
    colours = front_rows[:, :3, :] + jnp.exp(-front_depth) * back_rows[:, :3, :]
    opacity = 1.0 - jnp.exp(-(front_depth + back_rows[:, 3:4, :]))
    return jnp.concatenate([colours, opacity], axis=1)


def ring_order(count):
    return list(range(0, count, 2)) + list(range(count - 1 - count % 2, 0, -2))


def ring_gather(own, count):
    order = ring_order(count)
    forward = [(order[k], order[(k + 1) % count]) for k in range(count)]
    backward = [(b, a) for a, b in forward]
    slots = [own]
    ahead = own
    behind = own
    for step in range(1, count // 2 + 1):
        ahead = lax.ppermute(ahead, "depth", forward)
        slots.append(ahead)
        if 2 * step < count:
            behind = lax.ppermute(behind, "depth", backward)
            slots.append(behind)
    return jnp.concatenate(slots, axis=0)


def on_device(density, foot_start, foot_rows, extinction, colour_slope, colour_offset, tile_source):
    depth_count = lax.axis_size("depth")
    screen_count = lax.axis_size("screen")
    depth_index = lax.axis_index("depth")
    screen_index = lax.axis_index("screen")
    image_total = tile_source.shape[0]
    half_rows = image_total // screen_count
    owner_rows = image_total // (depth_count * screen_count)
    start = foot_start[0, 0]
    shown = foot_rows[0, 0]
    brick_rows, pixels = density.shape[2], density.shape[4]
    channels = 4
    stride = brick_rows + 2
    meta = jnp.stack([start, shown, depth_index.astype(start.dtype)]).astype(jnp.float32)
    slot = lax.dynamic_update_slice(jnp.zeros((stride, channels, pixels), jnp.float32),
                                    meta.reshape(1, 1, 3), (brick_rows, 0, 0))
    own = render_layers(density[0, 0], foot_rows, extinction, colour_slope, colour_offset, slot)
    flat = ring_gather(own, depth_count)
    meta_rows = flat.reshape(depth_count, stride, channels, pixels)[:, brick_rows, 0, :3]
    starts = meta_rows[:, 0].astype(jnp.int32)
    counts = meta_rows[:, 1].astype(jnp.int32)
    brick_ids = meta_rows[:, 2].astype(jnp.int32)
    self_owner = depth_index * screen_count + screen_index
    partner_owner = depth_index * screen_count + (1 - screen_index)
    wanted_self = lax.dynamic_slice_in_dim(tile_source, self_owner * owner_rows, owner_rows)
    wanted_partner = lax.dynamic_slice_in_dim(tile_source, partner_owner * owner_rows, owner_rows)
    for_partner = composite_rows(flat, starts, counts, brick_ids, stride, wanted_partner % half_rows)
    received = lax.ppermute(for_partner, "screen", [(0, 1), (1, 0)])
    flat, for_partner = lax.optimization_barrier((flat, for_partner))
    mine = composite_rows(flat, starts, counts, brick_ids, stride, wanted_self % half_rows)
    in_my_half = (wanted_self // half_rows) == screen_index
    return jnp.where(in_my_half[:, None, None], mine, received)


def solution(mesh):
    return jax.shard_map(
        on_device,
        mesh=mesh,
        in_specs=(
            P(("runs", "depth"), "screen", None, None, None),
            P(("runs", "depth"), "screen"),
            P(("runs", "depth"), "screen"),
            P("runs"),
            P(),
            P(),
            P("runs"),
        ),
        out_specs=P(("runs", "depth", "screen"), None, None),
        check_vma=False,
    )
```
